128 devices in a mesh: gx: 8 (over z_hi, x), gy: 16 (over z_lo, y, core).
Axes of the slice: x: 4, y: 4, z: 4 (z_hi: 2, z_lo: 2; z = z_hi * 2 + z_lo), core: 2. Of those that a mesh axis runs over, the one named last changes fastest.
Arguments:
- populations: float32 [19, 128, 512, 256], P(None, 'gx', 'gy'), may hold values from 0.02 to 0.08
- ions: float32 [2, 128, 512, 256], P(None, 'gx', 'gy'), may hold values from 0.4 to 1.62, as said below
- mask: int32 [128, 512, 256], P('gx', 'gy'), may hold values from 0 to 1, as said below
Outputs:
- populations_out: float32 [19, 128, 512, 256], P(None, 'gx', 'gy')
- ions_out: float32 [2, 128, 512, 256], P(None, 'gx', 'gy')
- potential: float32 [128, 512, 256], P('gx', 'gy')
The draws below stay inside these ranges and needn't reach their ends.
Inputs may be any that keep to these rules, and one draw needn't show every extreme that they name: `mask`: 1 marks a solid cell: every cell with second index 0 or 511 or third index 0 or 255, and scattered cells elsewhere; 0 marks fluid. `ions`: positive concentrations.
All inputs are finite; a program needn't handle non-finite values.
Results may differ from the reference program's by a relative error of at most 0.0004.
Values sent between devices are 32-bit elements; how exact they have to be, the bound alone decides.
No kernel may reach another device: no remote copies, remote signals or barrier semaphores. Data moves between devices by JAX's collectives and lax.ppermute only.
A program may use at most 128 MiB of HBM per device.

```python
import math
import jax
import jax.numpy as jnp
from jax import lax

NZ = 256
NX = 128
NY = 512


def draw_mask(key, part):
    scatter = jax.random.randint(jax.random.fold_in(key, 11), (NX, NY, NZ), 0, 32)
    solid = (scatter == 0).astype(jnp.int32)
    wid_pos = jnp.arange(NY, dtype=jnp.int32)[None, :, None]
    depth_pos = jnp.arange(NZ, dtype=jnp.int32)[None, None, :]
    walls = (wid_pos == 0) | (wid_pos == NY - 1) | (depth_pos == 0) | (depth_pos == NZ - 1)
    walls = jnp.broadcast_to(walls.astype(jnp.int32), (NX, NY, NZ))
    return jnp.maximum(solid, walls)


def draw_ions(key, part):
    shape = (2, NX, NY, NZ)
    exponent = jax.random.uniform(jax.random.fold_in(key, 23), shape, jnp.float32, math.log(0.4), math.log(1.6))
    values = jnp.exp(exponent)
    return values


def block_scale(key, shape, split, low, largest):
    level = 1.0
    for dim, shards_of in split:
        heights = jax.random.uniform(jax.random.fold_in(jax.random.fold_in(key, 6), dim), (shards_of,), jnp.float32, low / len(split), largest / len(split))
        level = level * jnp.repeat(jnp.exp(heights), shape[dim] // shards_of).reshape((-1,) + (1,) * (len(shape) - 1 - dim))
    return level


def setup_inputs(seed: int = 0) -> dict:
    key_list = jax.random.split(jax.random.key(seed), 4)
    populations = jnp.clip(0.02 + 0.06 * jax.random.uniform(key_list[0], (19, NX, NY, NZ), jnp.float32) ** block_scale(key_list[0], (19, NX, NY, NZ), ((1, 8), (2, 16)), -0.2, 0.2), 0.02, 0.08)
    ions = draw_ions(jax.random.fold_in(key_list[3], 71), 0)
    mask = draw_mask(jax.random.fold_in(key_list[3], 71), 0)
    return dict(populations=populations, ions=ions, mask=mask)


PRECISE = lax.Precision.HIGHEST
LATTICE_VELOCITY = [(0, 0, 0), (1, 0, 0), (-1, 0, 0), (0, 1, 0), (0, -1, 0), (0, 0, 1), (0, 0, -1),
            (1, 1, 0), (-1, -1, 0), (1, -1, 0), (-1, 1, 0), (1, 0, 1), (-1, 0, -1),
            (1, 0, -1), (-1, 0, 1), (0, 1, 1), (0, -1, -1), (0, 1, -1), (0, -1, 1)]
WEIGHTS = [1.0 / 3.0] + [1.0 / 18.0] * 6 + [1.0 / 36.0] * 12
OPPOSITE = [0, 2, 1, 4, 3, 6, 5, 8, 7, 10, 9, 12, 11, 14, 13, 16, 15, 18, 17]
RELAXATION = 0.8
SCREENING = 0.001
WALL_CHARGE = -0.1
FIELD_EXT = 0.3
DIFFUSIVITY = 0.1


def sine_table(length):
    series = jnp.arange(length, dtype=jnp.int32) + 1
    product = (series[:, None] * series[None, :]) % (2 * (length + 1))
    return jnp.sin(product.astype(jnp.float32) * (math.pi / (length + 1)))


def fourier_pair(length):
    series = jnp.arange(length, dtype=jnp.int32)
    product = (series[:, None] * series[None, :]) % length
    angles = product.astype(jnp.float32) * (2.0 * math.pi / length)
    return jnp.stack([jnp.cos(angles), -jnp.sin(angles)])


def wall_eigen(first, number, total):
    modes = (jnp.arange(number, dtype=jnp.int32) + first + 1).astype(jnp.float32)
    return 2.0 - 2.0 * jnp.cos(modes * (math.pi / (total + 1)))


def cycle_angles(first, number, total):
    modes = jnp.arange(number, dtype=jnp.int32) + first
    return modes.astype(jnp.float32) * (2.0 * math.pi / total)


def solve_potential(free_electrostatic_share):
    full_len, full_wid, depth = free_electrostatic_share.shape
    depth_sine = sine_table(depth)
    widthwise_basis_sines = sine_table(full_wid)
    pair = fourier_pair(full_len)
    sectioned = jnp.einsum("xyz,nz->xyn", free_electrostatic_share, depth_sine, precision=PRECISE)
    spectra = jnp.einsum("rkx,xyn->rkyn", pair, sectioned, precision=PRECISE)
    spectra = jnp.einsum("my,rkyn->rkmn", widthwise_basis_sines, spectra, precision=PRECISE)
    angles = cycle_angles(0, full_len, full_len)
    denom = (SCREENING + (2.0 - 2.0 * jnp.cos(angles))[:, None, None]
             + wall_eigen(0, full_wid, full_wid)[None, :, None]
             + wall_eigen(0, depth, depth)[None, None, :])
    spectra = spectra / denom[None]
    level = jnp.einsum("ym,rkmn->rkyn", widthwise_basis_sines, spectra, precision=PRECISE) * (2.0 / (full_wid + 1))
    lines = jnp.einsum("rkx,rkyn->xyn", pair, level, precision=PRECISE) * (1.0 / full_len)
    return jnp.einsum("nz,xyn->xyz", depth_sine, lines, precision=PRECISE) * (2.0 / (depth + 1))


def collide(populations, distribution_tuple, volumetric_push):
    density = jnp.sum(populations, axis=0)
    moment = []
    for component in range(3):
        total = jnp.zeros_like(density)
        for entry in range(19):
            if LATTICE_VELOCITY[entry][component] != 0:
                total = total + LATTICE_VELOCITY[entry][component] * populations[entry]
        moment.append(total)
    velocity = [(moment[component] + 0.5 * volumetric_push[component]) / density for component in range(3)]
    speed_sq = velocity[0] * velocity[0] + velocity[1] * velocity[1] + velocity[2] * velocity[2]
    power = velocity[0] * volumetric_push[0] + velocity[1] * volumetric_push[1] + velocity[2] * volumetric_push[2]
    posts = []
    for entry in range(19):
        along = LATTICE_VELOCITY[entry]
        proj_vel = jnp.zeros_like(density)
        proj_force = jnp.zeros_like(density)
        for component in range(3):
            if along[component] != 0:
                proj_vel = proj_vel + along[component] * velocity[component]
                proj_force = proj_force + along[component] * volumetric_push[component]
        weight = WEIGHTS[entry]
        equil = weight * density * (1.0 + 3.0 * proj_vel + 4.5 * proj_vel * proj_vel - 1.5 * speed_sq)
        source = weight * (3.0 * (proj_force - power) + 9.0 * proj_vel * proj_force)
        moved = populations[entry] - (populations[entry] - equil) / RELAXATION + (1.0 - 0.5 / RELAXATION) * source
        posts.append(distribution_tuple * moved + (1.0 - distribution_tuple) * populations[OPPOSITE[entry]])
    return jnp.stack(posts), velocity


def drift_diffuse(centre, neighbour_cells, distribution_tuple, velocity, gradient_of_voltage, potential, free_electrostatic_share):
    conc = centre[:2]
    laplace = -6.0 * conc
    drift = conc * (SCREENING * potential - free_electrostatic_share)[None]
    advect = jnp.zeros_like(conc)
    for component in range(3):
        upper, lower = neighbour_cells[component]
        up_val = upper[2:3] * upper[:2] + (1.0 - upper[2:3]) * conc
        low_val = lower[2:3] * lower[:2] + (1.0 - lower[2:3]) * conc
        laplace = laplace + up_val + low_val
        slope = 0.5 * (up_val - low_val)
        drift = drift - slope * gradient_of_voltage[component][None]
        advect = advect + slope * velocity[component][None]
    valence = jnp.asarray([1.0, -1.0], jnp.float32)[:, None, None, None]
    change = DIFFUSIVITY * (laplace + valence * drift) - advect
    return conc + distribution_tuple[None] * change


def reference(populations, ions, mask):
    distribution_tuple = (mask == 0).astype(jnp.float32)
    free_electrostatic_share = distribution_tuple * (ions[0] - ions[1]) + (1.0 - distribution_tuple) * WALL_CHARGE
    potential = solve_potential(free_electrostatic_share)
    field_len = FIELD_EXT - 0.5 * (jnp.roll(potential, -1, 0) - jnp.roll(potential, 1, 0))
    padded = jnp.pad(potential, ((0, 0), (1, 1), (1, 1)))
    field_wid = -0.5 * (padded[:, 2:, 1:-1] - padded[:, :-2, 1:-1])
    field_depth = -0.5 * (padded[:, 1:-1, 2:] - padded[:, 1:-1, :-2])
    gradient_of_voltage = [field_len, field_wid, field_depth]
    ion_concentration_sum = distribution_tuple * free_electrostatic_share
    volumetric_push = [ion_concentration_sum * voltage_grid for voltage_grid in gradient_of_voltage]
    post, velocity = collide(populations, distribution_tuple, volumetric_push)
    read = []
    for entry in range(19):
        along = LATTICE_VELOCITY[entry]
        read.append(jnp.roll(post[entry], along, axis=(0, 1, 2)))
    populations_out = jnp.stack(read)
    ionic = jnp.concatenate([ions, distribution_tuple[None]], axis=0)
    neighbour_cells = []
    for component in range(3):
        neighbour_cells.append((jnp.roll(ionic, -1, component + 1), jnp.roll(ionic, 1, component + 1)))
    ions_out = drift_diffuse(ionic, neighbour_cells, distribution_tuple, velocity, gradient_of_voltage, potential, free_electrostatic_share)
    return populations_out, ions_out, potential
```

```python
import math

import jax
import jax.numpy as jnp
from jax import lax
from jax.sharding import PartitionSpec as P

PRECISE = lax.Precision.HIGHEST
LATTICE_VELOCITY = [
    (0, 0, 0),
    (1, 0, 0),
    (-1, 0, 0),
    (0, 1, 0),
    (0, -1, 0),
    (0, 0, 1),
    (0, 0, -1),
    (1, 1, 0),
    (-1, -1, 0),
    (1, -1, 0),
    (-1, 1, 0),
    (1, 0, 1),
    (-1, 0, -1),
    (1, 0, -1),
    (-1, 0, 1),
    (0, 1, 1),
    (0, -1, -1),
    (0, 1, -1),
    (0, -1, 1),
]
WEIGHTS = [1.0 / 3.0] + [1.0 / 18.0] * 6 + [1.0 / 36.0] * 12
OPPOSITE = [0, 2, 1, 4, 3, 6, 5, 8, 7, 10, 9, 12, 11, 14, 13, 16, 15, 18, 17]
RELAXATION = 0.8
SCREENING = 0.001
WALL_CHARGE = -0.1
FIELD_EXT = 0.3
DIFFUSIVITY = 0.1

PLUS_X = [i for i in range(19) if LATTICE_VELOCITY[i][0] == 1]
MINUS_X = [i for i in range(19) if LATTICE_VELOCITY[i][0] == -1]
PLUS_Y = [i for i in range(19) if LATTICE_VELOCITY[i][1] == 1]
MINUS_Y = [i for i in range(19) if LATTICE_VELOCITY[i][1] == -1]


def ring(axis, step):
    count = lax.axis_size(axis)
    return [(i, (i + step) % count) for i in range(count)]


def halos(block, axis, dim):
    n = block.shape[dim]
    low = lax.ppermute(lax.slice_in_dim(block, n - 1, n, axis=dim), axis, ring(axis, 1))
    high = lax.ppermute(lax.slice_in_dim(block, 0, 1, axis=dim), axis, ring(axis, -1))
    return low, high


def diagonal_pairs(step_x, step_y):
    nx = lax.axis_size("gx")
    ny = lax.axis_size("gy")
    pairs = []
    for a in range(nx):
        for b in range(ny):
            pairs.append((a * ny + b, ((a + step_x) % nx) * ny + (b + step_y) % ny))
    return pairs


def sine_table(length):
    series = jnp.arange(length, dtype=jnp.int32) + 1
    product = series[:, None] * series[None, :] % (2 * (length + 1))
    return jnp.sin(product.astype(jnp.float32) * (math.pi / (length + 1)))


def fourier_pair(length):
    series = jnp.arange(length, dtype=jnp.int32)
    product = series[:, None] * series[None, :] % length
    angles = product.astype(jnp.float32) * (2.0 * math.pi / length)
    return jnp.stack([jnp.cos(angles), -jnp.sin(angles)])


def wall_eigen(first, number, total):
    modes = (jnp.arange(number, dtype=jnp.int32) + first + 1).astype(jnp.float32)
    return 2.0 - 2.0 * jnp.cos(modes * (math.pi / (total + 1)))


def cycle_angles(first, number, total):
    modes = jnp.arange(number, dtype=jnp.int32) + first
    return modes.astype(jnp.float32) * (2.0 * math.pi / total)


def solve_potential(charge):
    len_local, wid_local, depth = charge.shape
    len_parts = lax.axis_size("gx")
    wid_parts = lax.axis_size("gy")
    devices = len_parts * wid_parts
    modes_local = depth // devices
    full_len = len_local * len_parts
    full_wid = wid_local * wid_parts
    me = lax.axis_index("gx") * wid_parts + lax.axis_index("gy")
    depth_sine = sine_table(depth)
    sectioned = jnp.einsum("xyz,nz->nxy", charge, depth_sine, precision=PRECISE)
    sectioned = sectioned.reshape(devices, modes_local, len_local, wid_local)
    plane = lax.all_to_all(sectioned, ("gx", "gy"), 0, 0, tiled=True)
    plane = plane.reshape(len_parts, wid_parts, modes_local, len_local, wid_local)
    pair = fourier_pair(full_len).reshape(2, full_len, len_parts, len_local)
    spectra = jnp.einsum("rkax,abnxy->rknby", pair, plane, precision=PRECISE)
    spectra = spectra.reshape(2, full_len, modes_local, full_wid)
    wid_sine = sine_table(full_wid)
    spectra = jnp.einsum("my,rkny->rknm", wid_sine, spectra, precision=PRECISE)
    angles = cycle_angles(0, full_len, full_len)
    denom = (
        SCREENING
        + (2.0 - 2.0 * jnp.cos(angles))[:, None, None]
        + wall_eigen(me * modes_local, modes_local, depth)[None, :, None]
        + wall_eigen(0, full_wid, full_wid)[None, None, :]
    )
    spectra = spectra / denom[None]
    level = jnp.einsum("ym,rknm->rkny", wid_sine, spectra, precision=PRECISE) * (
        2.0 / (full_wid + 1)
    )
    level = level.reshape(2, full_len, modes_local, wid_parts, wid_local)
    lines = jnp.einsum("rkax,rknby->abnxy", pair, level, precision=PRECISE) * (1.0 / full_len)
    lines = lines.reshape(devices, modes_local, len_local, wid_local)
    back = lax.all_to_all(lines, ("gx", "gy"), 0, 0, tiled=True)
    back = back.reshape(depth, len_local, wid_local)
    return jnp.einsum("nz,nxy->xyz", depth_sine, back, precision=PRECISE) * (2.0 / (depth + 1))


def collide(populations, distribution_tuple, volumetric_push):
    density = jnp.sum(populations, axis=0)
    moment = []
    for component in range(3):
        total = jnp.zeros_like(density)
        for entry in range(19):
            if LATTICE_VELOCITY[entry][component] != 0:
                total = total + LATTICE_VELOCITY[entry][component] * populations[entry]
        moment.append(total)
    velocity = [
        (moment[component] + 0.5 * volumetric_push[component]) / density for component in range(3)
    ]
    speed_sq = velocity[0] * velocity[0] + velocity[1] * velocity[1] + velocity[2] * velocity[2]
    power = (
        velocity[0] * volumetric_push[0]
        + velocity[1] * volumetric_push[1]
        + velocity[2] * volumetric_push[2]
    )
    posts = []
    for entry in range(19):
        along = LATTICE_VELOCITY[entry]
        proj_vel = jnp.zeros_like(density)
        proj_force = jnp.zeros_like(density)
        for component in range(3):
            if along[component] != 0:
                proj_vel = proj_vel + along[component] * velocity[component]
                proj_force = proj_force + along[component] * volumetric_push[component]
        weight = WEIGHTS[entry]
        equil = (
            weight * density * (1.0 + 3.0 * proj_vel + 4.5 * proj_vel * proj_vel - 1.5 * speed_sq)
        )
        source = weight * (3.0 * (proj_force - power) + 9.0 * proj_vel * proj_force)
        moved = (
            populations[entry]
            - (populations[entry] - equil) / RELAXATION
            + (1.0 - 0.5 / RELAXATION) * source
        )
        posts.append(
            distribution_tuple * moved + (1.0 - distribution_tuple) * populations[OPPOSITE[entry]]
        )
    return (jnp.stack(posts), velocity)


def drift_diffuse(
    conc,
    neighbour_cells,
    distribution_tuple,
    velocity,
    gradient_of_voltage,
    potential,
    free_electrostatic_share,
):
    laplace = -6.0 * conc
    drift = conc * (SCREENING * potential - free_electrostatic_share)[None]
    advect = jnp.zeros_like(conc)
    for component in range(3):
        upper, lower = neighbour_cells[component]
        up_val = upper[2:3] * upper[:2] + (1.0 - upper[2:3]) * conc
        low_val = lower[2:3] * lower[:2] + (1.0 - lower[2:3]) * conc
        laplace = laplace + up_val + low_val
        slope = 0.5 * (up_val - low_val)
        drift = drift - slope * gradient_of_voltage[component][None]
        advect = advect + slope * velocity[component][None]
    valence = jnp.asarray([1.0, -1.0], jnp.float32)[:, None, None, None]
    change = DIFFUSIVITY * (laplace + valence * drift) - advect
    return conc + distribution_tuple[None] * change


def shift_x(block, low, high, step, dim):
    if step == 1:
        return jnp.concatenate([low, lax.slice_in_dim(block, 0, block.shape[dim] - 1, axis=dim)], dim)
    if step == -1:
        return jnp.concatenate([lax.slice_in_dim(block, 1, None, axis=dim), high], dim)
    return block


def body(populations, ions, mask):
    len_local, wid_local, depth = mask.shape
    wid_parts = lax.axis_size("gy")
    wid_index = lax.axis_index("gy")
    distribution_tuple = (mask == 0).astype(jnp.float32)
    ionic = jnp.concatenate([ions, distribution_tuple[None]], axis=0)
    ionic_x = halos(ionic, "gx", 1)
    ionic_y = halos(ionic, "gy", 2)
    free_electrostatic_share = (
        distribution_tuple * (ions[0] - ions[1]) + (1.0 - distribution_tuple) * WALL_CHARGE
    )
    potential = solve_potential(free_electrostatic_share)
    pot_low_x, pot_high_x = halos(potential, "gx", 0)
    pot_low_y, pot_high_y = halos(potential, "gy", 1)
    pot_up_x = jnp.concatenate([potential[1:], pot_high_x], 0)
    pot_down_x = jnp.concatenate([pot_low_x, potential[:-1]], 0)
    field_len = FIELD_EXT - 0.5 * (pot_up_x - pot_down_x)
    top_keep = 1.0 - (wid_index == wid_parts - 1).astype(jnp.float32)
    bottom_keep = 1.0 - (wid_index == 0).astype(jnp.float32)
    above = jnp.concatenate([potential[:, 1:], pot_high_y * top_keep], 1)
    below = jnp.concatenate([pot_low_y * bottom_keep, potential[:, :-1]], 1)
    field_wid = -0.5 * (above - below)
    depth_pad = jnp.pad(potential, ((0, 0), (0, 0), (1, 1)))
    field_depth = -0.5 * (depth_pad[:, :, 2:] - depth_pad[:, :, :-2])
    gradient_of_voltage = [field_len, field_wid, field_depth]
    ion_concentration_sum = distribution_tuple * free_electrostatic_share
    volumetric_push = [ion_concentration_sum * voltage_grid for voltage_grid in gradient_of_voltage]
    post, velocity = collide(populations, distribution_tuple, volumetric_push)

    low_x = lax.ppermute(jnp.stack([post[i, len_local - 1 :] for i in PLUS_X]), "gx", ring("gx", 1))
    high_x = lax.ppermute(jnp.stack([post[i, :1] for i in MINUS_X]), "gx", ring("gx", -1))
    low_y = lax.ppermute(jnp.stack([post[i, :, wid_local - 1 :] for i in PLUS_Y]), "gy", ring("gy", 1))
    high_y = lax.ppermute(jnp.stack([post[i, :, :1] for i in MINUS_Y]), "gy", ring("gy", -1))
    last_x = len_local - 1
    last_y = wid_local - 1
    corner = {
        7: lax.ppermute(post[7, last_x:, last_y:], ("gx", "gy"), diagonal_pairs(1, 1)),
        8: lax.ppermute(post[8, :1, :1], ("gx", "gy"), diagonal_pairs(-1, -1)),
        9: lax.ppermute(post[9, last_x:, :1], ("gx", "gy"), diagonal_pairs(1, -1)),
        10: lax.ppermute(post[10, :1, last_y:], ("gx", "gy"), diagonal_pairs(-1, 1)),
    }
    read = []
    for entry in range(19):
        cx, cy, cz = LATTICE_VELOCITY[entry]
        piece = post[entry]
        xlo = low_x[PLUS_X.index(entry)] if cx == 1 else None
        xhi = high_x[MINUS_X.index(entry)] if cx == -1 else None
        piece = shift_x(piece, xlo, xhi, cx, 0)
        if cy != 0:
            ylo = low_y[PLUS_Y.index(entry)] if cy == 1 else None
            yhi = high_y[MINUS_Y.index(entry)] if cy == -1 else None
            if cx != 0:
                if cy == 1:
                    ylo = shift_x(ylo, corner[entry], corner[entry], cx, 0)
                else:
                    yhi = shift_x(yhi, corner[entry], corner[entry], cx, 0)
            piece = shift_x(piece, ylo, yhi, cy, 1)
        if cz != 0:
            piece = jnp.roll(piece, cz, axis=2)
        read.append(piece)
    populations_out = jnp.stack(read)

    low_ix, high_ix = ionic_x
    low_iy, high_iy = ionic_y
    neighbour_cells = [
        (shift_x(ionic, None, high_ix, -1, 1), shift_x(ionic, low_ix, None, 1, 1)),
        (shift_x(ionic, None, high_iy, -1, 2), shift_x(ionic, low_iy, None, 1, 2)),
        (jnp.roll(ionic, -1, 3), jnp.roll(ionic, 1, 3)),
    ]
    ions_out = drift_diffuse(
        ions,
        neighbour_cells,
        distribution_tuple,
        velocity,
        gradient_of_voltage,
        potential,
        free_electrostatic_share,
    )
    return (populations_out, ions_out, potential)


def solution(mesh):
    placed = (P(None, "gx", "gy", None), P(None, "gx", "gy", None), P("gx", "gy", None))
    return jax.shard_map(
        body,
        mesh=mesh,
        in_specs=placed,
        out_specs=(P(None, "gx", "gy", None), P(None, "gx", "gy", None), P("gx", "gy", None)),
        check_vma=False,
    )
```

```python
import math

import jax
import jax.numpy as jnp
from jax import lax
from jax.experimental import pallas as pl
from jax.sharding import PartitionSpec as P

PRECISE = lax.Precision.HIGHEST
SOLVE = lax.Precision.HIGH
LATTICE_VELOCITY = [
    (0, 0, 0),
    (1, 0, 0),
    (-1, 0, 0),
    (0, 1, 0),
    (0, -1, 0),
    (0, 0, 1),
    (0, 0, -1),
    (1, 1, 0),
    (-1, -1, 0),
    (1, -1, 0),
    (-1, 1, 0),
    (1, 0, 1),
    (-1, 0, -1),
    (1, 0, -1),
    (-1, 0, 1),
    (0, 1, 1),
    (0, -1, -1),
    (0, 1, -1),
    (0, -1, 1),
]
WEIGHTS = [1.0 / 3.0] + [1.0 / 18.0] * 6 + [1.0 / 36.0] * 12
OPPOSITE = [0, 2, 1, 4, 3, 6, 5, 8, 7, 10, 9, 12, 11, 14, 13, 16, 15, 18, 17]
RELAXATION = 0.8
SCREENING = 0.001
WALL_CHARGE = -0.1
FIELD_EXT = 0.3
DIFFUSIVITY = 0.1

PLUS_X = [i for i in range(19) if LATTICE_VELOCITY[i][0] == 1]
MINUS_X = [i for i in range(19) if LATTICE_VELOCITY[i][0] == -1]
PLUS_Y = [i for i in range(19) if LATTICE_VELOCITY[i][1] == 1]
MINUS_Y = [i for i in range(19) if LATTICE_VELOCITY[i][1] == -1]


def ring(axis, step):
    count = lax.axis_size(axis)
    return [(i, (i + step) % count) for i in range(count)]


def halos(block, axis, dim):
    n = block.shape[dim]
    low = lax.ppermute(lax.slice_in_dim(block, n - 1, n, axis=dim), axis, ring(axis, 1))
    high = lax.ppermute(lax.slice_in_dim(block, 0, 1, axis=dim), axis, ring(axis, -1))
    return low, high


def diagonal_pairs(step_x, step_y):
    nx = lax.axis_size("gx")
    ny = lax.axis_size("gy")
    pairs = []
    for a in range(nx):
        for b in range(ny):
            pairs.append((a * ny + b, ((a + step_x) % nx) * ny + (b + step_y) % ny))
    return pairs


def sine_table(length):
    series = jnp.arange(length, dtype=jnp.int32) + 1
    product = series[:, None] * series[None, :] % (2 * (length + 1))
    return jnp.sin(product.astype(jnp.float32) * (math.pi / (length + 1)))


def fourier_pair(length):
    series = jnp.arange(length, dtype=jnp.int32)
    product = series[:, None] * series[None, :] % length
    angles = product.astype(jnp.float32) * (2.0 * math.pi / length)
    return jnp.stack([jnp.cos(angles), -jnp.sin(angles)])


def wall_eigen(first, number, total):
    modes = (jnp.arange(number, dtype=jnp.int32) + first + 1).astype(jnp.float32)
    return 2.0 - 2.0 * jnp.cos(modes * (math.pi / (total + 1)))


def cycle_angles(first, number, total):
    modes = jnp.arange(number, dtype=jnp.int32) + first
    return modes.astype(jnp.float32) * (2.0 * math.pi / total)


def solve_potential(charge):
    len_local, wid_local, depth = charge.shape
    len_parts = lax.axis_size("gx")
    wid_parts = lax.axis_size("gy")
    devices = len_parts * wid_parts
    modes_local = depth // devices
    full_len = len_local * len_parts
    full_wid = wid_local * wid_parts
    me = lax.axis_index("gx") * wid_parts + lax.axis_index("gy")
    depth_sine = sine_table(depth)
    sectioned = jnp.einsum("xyz,nz->nxy", charge, depth_sine, precision=SOLVE)
    sectioned = sectioned.reshape(devices, modes_local, len_local, wid_local)
    plane = lax.all_to_all(sectioned, ("gx", "gy"), 0, 0, tiled=True)
    plane = plane.reshape(len_parts, wid_parts, modes_local, len_local, wid_local)
    pair = fourier_pair(full_len).reshape(2, full_len, len_parts, len_local)
    spectra = jnp.einsum("rkax,abnxy->rknby", pair, plane, precision=SOLVE)
    spectra = spectra.reshape(2, full_len, modes_local, full_wid)
    wid_sine = sine_table(full_wid)
    spectra = jnp.einsum("my,rkny->rknm", wid_sine, spectra, precision=SOLVE)
    angles = cycle_angles(0, full_len, full_len)
    denom = (
        SCREENING
        + (2.0 - 2.0 * jnp.cos(angles))[:, None, None]
        + wall_eigen(me * modes_local, modes_local, depth)[None, :, None]
        + wall_eigen(0, full_wid, full_wid)[None, None, :]
    )
    spectra = spectra / denom[None]
    level = jnp.einsum("ym,rknm->rkny", wid_sine, spectra, precision=SOLVE) * (
        2.0 / (full_wid + 1)
    )
    level = level.reshape(2, full_len, modes_local, wid_parts, wid_local)
    lines = jnp.einsum("rkax,rknby->abnxy", pair, level, precision=SOLVE) * (1.0 / full_len)
    lines = lines.reshape(devices, modes_local, len_local, wid_local)
    back = lax.all_to_all(lines, ("gx", "gy"), 0, 0, tiled=True)
    back = back.reshape(depth, len_local, wid_local)
    return jnp.einsum("nz,nxy->xyz", depth_sine, back, precision=SOLVE) * (2.0 / (depth + 1))


def collide(populations, distribution_tuple, volumetric_push, entries=tuple(range(19))):
    density = populations[0]
    for entry in range(1, 19):
        density = density + populations[entry]
    moment = []
    for component in range(3):
        total = jnp.zeros_like(density)
        for entry in range(19):
            if LATTICE_VELOCITY[entry][component] != 0:
                total = total + LATTICE_VELOCITY[entry][component] * populations[entry]
        moment.append(total)
    velocity = [
        (moment[component] + 0.5 * volumetric_push[component]) / density for component in range(3)
    ]
    speed_sq = velocity[0] * velocity[0] + velocity[1] * velocity[1] + velocity[2] * velocity[2]
    power = (
        velocity[0] * volumetric_push[0]
        + velocity[1] * volumetric_push[1]
        + velocity[2] * volumetric_push[2]
    )
    posts = []
    for entry in entries:
        along = LATTICE_VELOCITY[entry]
        proj_vel = jnp.zeros_like(density)
        proj_force = jnp.zeros_like(density)
        for component in range(3):
            if along[component] != 0:
                proj_vel = proj_vel + along[component] * velocity[component]
                proj_force = proj_force + along[component] * volumetric_push[component]
        weight = WEIGHTS[entry]
        equil = (
            weight * density * (1.0 + 3.0 * proj_vel + 4.5 * proj_vel * proj_vel - 1.5 * speed_sq)
        )
        source = weight * (3.0 * (proj_force - power) + 9.0 * proj_vel * proj_force)
        moved = (
            populations[entry]
            - (populations[entry] - equil) / RELAXATION
            + (1.0 - 0.5 / RELAXATION) * source
        )
        posts.append(
            distribution_tuple * moved + (1.0 - distribution_tuple) * populations[OPPOSITE[entry]]
        )
    return (posts, velocity)


def collide_kernel(pop_ref, fluid_ref, push_ref, post_ref, vel_ref):
    for row in range(pop_ref.shape[1]):
        pops = [pop_ref[entry, row] for entry in range(19)]
        push = [push_ref[component, row] for component in range(3)]
        posts, velocity = collide(pops, fluid_ref[row], push)
        for entry in range(19):
            post_ref[entry, row] = posts[entry]
        for component in range(3):
            vel_ref[component, row] = velocity[component]


def collide_call(populations, distribution_tuple, push):
    entries, len_local, wid_local, depth = populations.shape
    rows = 2
    big = lambda n: pl.BlockSpec((n, rows, wid_local, depth), lambda i: (0, i, 0, 0))
    return pl.pallas_call(
        collide_kernel,
        grid=(len_local // rows,),
        in_specs=[big(entries), pl.BlockSpec((rows, wid_local, depth), lambda i: (i, 0, 0)), big(3)],
        out_specs=[big(entries), big(3)],
        out_shape=[
            jax.ShapeDtypeStruct(populations.shape, jnp.float32),
            jax.ShapeDtypeStruct((3, len_local, wid_local, depth), jnp.float32),
        ],
    )(populations, distribution_tuple, push)


def drift_diffuse(
    conc,
    neighbour_cells,
    distribution_tuple,
    velocity,
    gradient_of_voltage,
    potential,
    free_electrostatic_share,
):
    laplace = -6.0 * conc
    drift = conc * (SCREENING * potential - free_electrostatic_share)[None]
    advect = jnp.zeros_like(conc)
    for component in range(3):
        upper, lower = neighbour_cells[component]
        up_val = upper[2:3] * upper[:2] + (1.0 - upper[2:3]) * conc
        low_val = lower[2:3] * lower[:2] + (1.0 - lower[2:3]) * conc
        laplace = laplace + up_val + low_val
        slope = 0.5 * (up_val - low_val)
        drift = drift - slope * gradient_of_voltage[component][None]
        advect = advect + slope * velocity[component][None]
    valence = jnp.asarray([1.0, -1.0], jnp.float32)[:, None, None, None]
    change = DIFFUSIVITY * (laplace + valence * drift) - advect
    return conc + distribution_tuple[None] * change


def shift_x(block, low, high, step, dim):
    if step == 1:
        return jnp.concatenate([low, lax.slice_in_dim(block, 0, block.shape[dim] - 1, axis=dim)], dim)
    if step == -1:
        return jnp.concatenate([lax.slice_in_dim(block, 1, None, axis=dim), high], dim)
    return block


def body(populations, ions, mask):
    len_local, wid_local, depth = mask.shape
    wid_parts = lax.axis_size("gy")
    wid_index = lax.axis_index("gy")
    distribution_tuple = (mask == 0).astype(jnp.float32)
    ionic = jnp.concatenate([ions, distribution_tuple[None]], axis=0)
    ionic_x = halos(ionic, "gx", 1)
    ionic_y = halos(ionic, "gy", 2)
    free_electrostatic_share = (
        distribution_tuple * (ions[0] - ions[1]) + (1.0 - distribution_tuple) * WALL_CHARGE
    )
    potential = solve_potential(free_electrostatic_share)
    pot_low_x, pot_high_x = halos(potential, "gx", 0)
    pot_low_y, pot_high_y = halos(potential, "gy", 1)
    pot_up_x = jnp.concatenate([potential[1:], pot_high_x], 0)
    pot_down_x = jnp.concatenate([pot_low_x, potential[:-1]], 0)
    field_len = FIELD_EXT - 0.5 * (pot_up_x - pot_down_x)
    top_keep = 1.0 - (wid_index == wid_parts - 1).astype(jnp.float32)
    bottom_keep = 1.0 - (wid_index == 0).astype(jnp.float32)
    above = jnp.concatenate([potential[:, 1:], pot_high_y * top_keep], 1)
    below = jnp.concatenate([pot_low_y * bottom_keep, potential[:, :-1]], 1)
    field_wid = -0.5 * (above - below)
    depth_pad = jnp.pad(potential, ((0, 0), (0, 0), (1, 1)))
    field_depth = -0.5 * (depth_pad[:, :, 2:] - depth_pad[:, :, :-2])
    gradient_of_voltage = [field_len, field_wid, field_depth]
    ion_concentration_sum = distribution_tuple * free_electrostatic_share
    volumetric_push = [ion_concentration_sum * voltage_grid for voltage_grid in gradient_of_voltage]
    push = jnp.stack(volumetric_push)
    post, velocity = collide_call(populations, distribution_tuple, push)
    velocity = [velocity[component] for component in range(3)]

    def edge(dim, start, entries):
        cut = lambda a, d: lax.slice_in_dim(a, start, start + 1, axis=d)
        posts, _ = collide(
            [cut(populations[entry], dim) for entry in range(19)],
            cut(distribution_tuple, dim),
            [cut(push[component], dim) for component in range(3)],
            entries,
        )
        return jnp.stack(posts)

    last_x = len_local - 1
    last_y = wid_local - 1
    rows_high = edge(0, last_x, PLUS_X)
    rows_low = edge(0, 0, MINUS_X)
    low_x = lax.ppermute(rows_high, "gx", ring("gx", 1))
    high_x = lax.ppermute(rows_low, "gx", ring("gx", -1))
    low_y = lax.ppermute(edge(1, last_y, PLUS_Y), "gy", ring("gy", 1))
    high_y = lax.ppermute(edge(1, 0, MINUS_Y), "gy", ring("gy", -1))
    both = ("gx", "gy")
    corner = {
        7: lax.ppermute(rows_high[PLUS_X.index(7), :, last_y:], both, diagonal_pairs(1, 1)),
        8: lax.ppermute(rows_low[MINUS_X.index(8), :, :1], both, diagonal_pairs(-1, -1)),
        9: lax.ppermute(rows_high[PLUS_X.index(9), :, :1], both, diagonal_pairs(1, -1)),
        10: lax.ppermute(rows_low[MINUS_X.index(10), :, last_y:], both, diagonal_pairs(-1, 1)),
    }
    read = []
    for entry in range(19):
        cx, cy, cz = LATTICE_VELOCITY[entry]
        piece = post[entry]
        xlo = low_x[PLUS_X.index(entry)] if cx == 1 else None
        xhi = high_x[MINUS_X.index(entry)] if cx == -1 else None
        piece = shift_x(piece, xlo, xhi, cx, 0)
        if cy != 0:
            ylo = low_y[PLUS_Y.index(entry)] if cy == 1 else None
            yhi = high_y[MINUS_Y.index(entry)] if cy == -1 else None
            if cx != 0:
                if cy == 1:
                    ylo = shift_x(ylo, corner[entry], corner[entry], cx, 0)
                else:
                    yhi = shift_x(yhi, corner[entry], corner[entry], cx, 0)
            piece = shift_x(piece, ylo, yhi, cy, 1)
        if cz != 0:
            piece = jnp.roll(piece, cz, axis=2)
        read.append(piece)
    populations_out = jnp.stack(read)

    low_ix, high_ix = ionic_x
    low_iy, high_iy = ionic_y
    neighbour_cells = [
        (shift_x(ionic, None, high_ix, -1, 1), shift_x(ionic, low_ix, None, 1, 1)),
        (shift_x(ionic, None, high_iy, -1, 2), shift_x(ionic, low_iy, None, 1, 2)),
        (jnp.roll(ionic, -1, 3), jnp.roll(ionic, 1, 3)),
    ]
    ions_out = drift_diffuse(
        ions,
        neighbour_cells,
        distribution_tuple,
        velocity,
        gradient_of_voltage,
        potential,
        free_electrostatic_share,
    )
    return (populations_out, ions_out, potential)


def solution(mesh):
    placed = (P(None, "gx", "gy", None), P(None, "gx", "gy", None), P("gx", "gy", None))
    return jax.shard_map(
        body,
        mesh=mesh,
        in_specs=placed,
        out_specs=(P(None, "gx", "gy", None), P(None, "gx", "gy", None), P("gx", "gy", None)),
        check_vma=False,
    )
```

```python
import math

import jax
import jax.numpy as jnp
from jax import lax
from jax.experimental import pallas as pl
from jax.experimental.pallas import tpu as pltpu
from jax.sharding import PartitionSpec as P

PRECISE = lax.Precision.HIGHEST
SOLVE = lax.Precision.HIGH
LATTICE_VELOCITY = [
    (0, 0, 0),
    (1, 0, 0),
    (-1, 0, 0),
    (0, 1, 0),
    (0, -1, 0),
    (0, 0, 1),
    (0, 0, -1),
    (1, 1, 0),
    (-1, -1, 0),
    (1, -1, 0),
    (-1, 1, 0),
    (1, 0, 1),
    (-1, 0, -1),
    (1, 0, -1),
    (-1, 0, 1),
    (0, 1, 1),
    (0, -1, -1),
    (0, 1, -1),
    (0, -1, 1),
]
WEIGHTS = [1.0 / 3.0] + [1.0 / 18.0] * 6 + [1.0 / 36.0] * 12
OPPOSITE = [0, 2, 1, 4, 3, 6, 5, 8, 7, 10, 9, 12, 11, 14, 13, 16, 15, 18, 17]
RELAXATION = 0.8
SCREENING = 0.001
WALL_CHARGE = -0.1
FIELD_EXT = 0.3
DIFFUSIVITY = 0.1

PLUS_X = [i for i in range(19) if LATTICE_VELOCITY[i][0] == 1]
MINUS_X = [i for i in range(19) if LATTICE_VELOCITY[i][0] == -1]
PLUS_Y = [i for i in range(19) if LATTICE_VELOCITY[i][1] == 1]
MINUS_Y = [i for i in range(19) if LATTICE_VELOCITY[i][1] == -1]


def ring(axis, step):
    count = lax.axis_size(axis)
    return [(i, (i + step) % count) for i in range(count)]


def halos(block, axis, dim):
    n = block.shape[dim]
    low = lax.ppermute(lax.slice_in_dim(block, n - 1, n, axis=dim), axis, ring(axis, 1))
    high = lax.ppermute(lax.slice_in_dim(block, 0, 1, axis=dim), axis, ring(axis, -1))
    return low, high


def diagonal_pairs(step_x, step_y):
    nx = lax.axis_size("gx")
    ny = lax.axis_size("gy")
    pairs = []
    for a in range(nx):
        for b in range(ny):
            pairs.append((a * ny + b, ((a + step_x) % nx) * ny + (b + step_y) % ny))
    return pairs


def sine_table(length):
    series = jnp.arange(length, dtype=jnp.int32) + 1
    product = series[:, None] * series[None, :] % (2 * (length + 1))
    return jnp.sin(product.astype(jnp.float32) * (math.pi / (length + 1)))


def fourier_pair(length):
    series = jnp.arange(length, dtype=jnp.int32)
    product = series[:, None] * series[None, :] % length
    angles = product.astype(jnp.float32) * (2.0 * math.pi / length)
    return jnp.stack([jnp.cos(angles), -jnp.sin(angles)])


def wall_eigen(first, number, total):
    modes = (jnp.arange(number, dtype=jnp.int32) + first + 1).astype(jnp.float32)
    return 2.0 - 2.0 * jnp.cos(modes * (math.pi / (total + 1)))


def cycle_angles(first, number, total):
    modes = jnp.arange(number, dtype=jnp.int32) + first
    return modes.astype(jnp.float32) * (2.0 * math.pi / total)


def solve_potential(charge):
    len_local, wid_local, depth = charge.shape
    len_parts = lax.axis_size("gx")
    wid_parts = lax.axis_size("gy")
    devices = len_parts * wid_parts
    modes_local = depth // devices
    full_len = len_local * len_parts
    full_wid = wid_local * wid_parts
    me = lax.axis_index("gx") * wid_parts + lax.axis_index("gy")
    depth_sine = sine_table(depth)
    sectioned = jnp.einsum("xyz,nz->nxy", charge, depth_sine, precision=SOLVE)
    sectioned = sectioned.reshape(devices, modes_local, len_local, wid_local)
    plane = lax.all_to_all(sectioned, ("gx", "gy"), 0, 0, tiled=True)
    plane = plane.reshape(len_parts, wid_parts, modes_local, len_local, wid_local)
    pair = fourier_pair(full_len).reshape(2, full_len, len_parts, len_local)
    spectra = jnp.einsum("rkax,abnxy->rknby", pair, plane, precision=SOLVE)
    spectra = spectra.reshape(2, full_len, modes_local, full_wid)
    wid_sine = sine_table(full_wid)
    spectra = jnp.einsum("my,rkny->rknm", wid_sine, spectra, precision=SOLVE)
    angles = cycle_angles(0, full_len, full_len)
    denom = (
        SCREENING
        + (2.0 - 2.0 * jnp.cos(angles))[:, None, None]
        + wall_eigen(me * modes_local, modes_local, depth)[None, :, None]
        + wall_eigen(0, full_wid, full_wid)[None, None, :]
    )
    spectra = spectra / denom[None]
    level = jnp.einsum("ym,rknm->rkny", wid_sine, spectra, precision=SOLVE) * (
        2.0 / (full_wid + 1)
    )
    level = level.reshape(2, full_len, modes_local, wid_parts, wid_local)
    lines = jnp.einsum("rkax,rknby->abnxy", pair, level, precision=SOLVE) * (1.0 / full_len)
    lines = lines.reshape(devices, modes_local, len_local, wid_local)
    back = lax.all_to_all(lines, ("gx", "gy"), 0, 0, tiled=True)
    back = back.reshape(depth, len_local, wid_local)
    return jnp.einsum("nz,nxy->xyz", depth_sine, back, precision=SOLVE) * (2.0 / (depth + 1))


def collide(populations, distribution_tuple, volumetric_push, entries=tuple(range(19))):
    density = populations[0]
    for entry in range(1, 19):
        density = density + populations[entry]
    moment = []
    for component in range(3):
        total = jnp.zeros_like(density)
        for entry in range(19):
            if LATTICE_VELOCITY[entry][component] != 0:
                total = total + LATTICE_VELOCITY[entry][component] * populations[entry]
        moment.append(total)
    velocity = [
        (moment[component] + 0.5 * volumetric_push[component]) / density for component in range(3)
    ]
    speed_sq = velocity[0] * velocity[0] + velocity[1] * velocity[1] + velocity[2] * velocity[2]
    power = (
        velocity[0] * volumetric_push[0]
        + velocity[1] * volumetric_push[1]
        + velocity[2] * volumetric_push[2]
    )
    posts = []
    for entry in entries:
        along = LATTICE_VELOCITY[entry]
        proj_vel = jnp.zeros_like(density)
        proj_force = jnp.zeros_like(density)
        for component in range(3):
            if along[component] != 0:
                proj_vel = proj_vel + along[component] * velocity[component]
                proj_force = proj_force + along[component] * volumetric_push[component]
        weight = WEIGHTS[entry]
        equil = (
            weight * density * (1.0 + 3.0 * proj_vel + 4.5 * proj_vel * proj_vel - 1.5 * speed_sq)
        )
        source = weight * (3.0 * (proj_force - power) + 9.0 * proj_vel * proj_force)
        moved = (
            populations[entry]
            - (populations[entry] - equil) * (1.0 / RELAXATION)
            + (1.0 - 0.5 / RELAXATION) * source
        )
        posts.append(jnp.where(distribution_tuple > 0.5, moved, populations[OPPOSITE[entry]]))
    return (posts, velocity)


def stream_kernel(pop_ref, fluid_ref, push_ref, out_ref, vel_ref):
    rows = pop_ref.shape[1]
    len_local, wid_local, depth = out_ref.shape[1:]
    for row in range(rows):
        pops = [pop_ref[entry, row] for entry in range(19)]
        push = [push_ref[component, row] for component in range(3)]
        posts, velocity = collide(pops, fluid_ref[row], push)
        here = pl.program_id(0) * rows + row
        for entry in range(19):
            cx, cy, cz = LATTICE_VELOCITY[entry]
            moved = posts[entry]
            if cy != 0:
                moved = pltpu.roll(moved, cy % wid_local, 0)
            if cz != 0:
                moved = pltpu.roll(moved, cz % depth, 1)
            out_ref[entry, (here + cx + len_local) % len_local] = moved
        for component in range(3):
            vel_ref[component, row] = velocity[component]


def stream_call(populations, distribution_tuple, push):
    entries, len_local, wid_local, depth = populations.shape
    rows = 2
    big = lambda n: pl.BlockSpec((n, rows, wid_local, depth), lambda i: (0, i, 0, 0))
    return pl.pallas_call(
        stream_kernel,
        grid=(len_local // rows,),
        in_specs=[big(entries), pl.BlockSpec((rows, wid_local, depth), lambda i: (i, 0, 0)), big(3)],
        out_specs=[pl.BlockSpec(populations.shape, lambda i: (0, 0, 0, 0)), big(3)],
        out_shape=[
            jax.ShapeDtypeStruct(populations.shape, jnp.float32),
            jax.ShapeDtypeStruct((3, len_local, wid_local, depth), jnp.float32),
        ],
        compiler_params=pltpu.CompilerParams(vmem_limit_bytes=48 * 1024 * 1024),
    )(populations, distribution_tuple, push)


def drift_diffuse(
    conc,
    neighbour_cells,
    distribution_tuple,
    velocity,
    gradient_of_voltage,
    potential,
    free_electrostatic_share,
):
    laplace = -6.0 * conc
    drift = conc * (SCREENING * potential - free_electrostatic_share)[None]
    advect = jnp.zeros_like(conc)
    for component in range(3):
        upper, lower = neighbour_cells[component]
        up_val = upper[2:3] * upper[:2] + (1.0 - upper[2:3]) * conc
        low_val = lower[2:3] * lower[:2] + (1.0 - lower[2:3]) * conc
        laplace = laplace + up_val + low_val
        slope = 0.5 * (up_val - low_val)
        drift = drift - slope * gradient_of_voltage[component][None]
        advect = advect + slope * velocity[component][None]
    valence = jnp.asarray([1.0, -1.0], jnp.float32)[:, None, None, None]
    change = DIFFUSIVITY * (laplace + valence * drift) - advect
    return conc + distribution_tuple[None] * change


def shift_x(block, low, high, step, dim):
    if step == 1:
        return jnp.concatenate([low, lax.slice_in_dim(block, 0, block.shape[dim] - 1, axis=dim)], dim)
    if step == -1:
        return jnp.concatenate([lax.slice_in_dim(block, 1, None, axis=dim), high], dim)
    return block


def body(populations, ions, mask):
    len_local, wid_local, depth = mask.shape
    wid_parts = lax.axis_size("gy")
    wid_index = lax.axis_index("gy")
    distribution_tuple = (mask == 0).astype(jnp.float32)
    ionic = jnp.concatenate([ions, distribution_tuple[None]], axis=0)
    ionic_x = halos(ionic, "gx", 1)
    ionic_y = halos(ionic, "gy", 2)
    free_electrostatic_share = (
        distribution_tuple * (ions[0] - ions[1]) + (1.0 - distribution_tuple) * WALL_CHARGE
    )
    potential = solve_potential(free_electrostatic_share)
    pot_low_x, pot_high_x = halos(potential, "gx", 0)
    pot_low_y, pot_high_y = halos(potential, "gy", 1)
    pot_up_x = jnp.concatenate([potential[1:], pot_high_x], 0)
    pot_down_x = jnp.concatenate([pot_low_x, potential[:-1]], 0)
    field_len = FIELD_EXT - 0.5 * (pot_up_x - pot_down_x)
    top_keep = 1.0 - (wid_index == wid_parts - 1).astype(jnp.float32)
    bottom_keep = 1.0 - (wid_index == 0).astype(jnp.float32)
    above = jnp.concatenate([potential[:, 1:], pot_high_y * top_keep], 1)
    below = jnp.concatenate([pot_low_y * bottom_keep, potential[:, :-1]], 1)
    field_wid = -0.5 * (above - below)
    depth_pad = jnp.pad(potential, ((0, 0), (0, 0), (1, 1)))
    field_depth = -0.5 * (depth_pad[:, :, 2:] - depth_pad[:, :, :-2])
    gradient_of_voltage = [field_len, field_wid, field_depth]
    ion_concentration_sum = distribution_tuple * free_electrostatic_share
    volumetric_push = [ion_concentration_sum * voltage_grid for voltage_grid in gradient_of_voltage]
    push = jnp.stack(volumetric_push)
    wrapped, velocity = stream_call(populations, distribution_tuple, push)
    velocity = [velocity[component] for component in range(3)]
    last_x = len_local - 1
    last_y = wid_local - 1
    edge_x = {1: 0, -1: last_x}
    edge_y = {1: 0, -1: last_y}
    rows = {}
    cols = {}
    for step in (1, -1):
        group = [e for e in range(19) if LATTICE_VELOCITY[e][0] == step]
        sent = jnp.stack([wrapped[e, edge_x[step]] for e in group])
        got = lax.ppermute(sent, "gx", ring("gx", step))
        rows.update({e: got[k] for k, e in enumerate(group)})
        group = [e for e in range(19) if LATTICE_VELOCITY[e][1] == step]
        sent = jnp.stack([wrapped[e, :, edge_y[step]] for e in group])
        got = lax.ppermute(sent, "gy", ring("gy", step))
        cols.update({e: got[k] for k, e in enumerate(group)})
    corners = {}
    for e in (7, 8, 9, 10):
        cx, cy, _ = LATTICE_VELOCITY[e]
        cell = wrapped[e, edge_x[cx], edge_y[cy]]
        corners[e] = lax.ppermute(cell, ("gx", "gy"), diagonal_pairs(cx, cy))
    populations_out = wrapped
    for e, row in rows.items():
        populations_out = populations_out.at[e, edge_x[LATTICE_VELOCITY[e][0]]].set(row)
    for e, col in cols.items():
        populations_out = populations_out.at[e, :, edge_y[LATTICE_VELOCITY[e][1]]].set(col)
    for e, cell in corners.items():
        cx, cy, _ = LATTICE_VELOCITY[e]
        populations_out = populations_out.at[e, edge_x[cx], edge_y[cy]].set(cell)

    low_ix, high_ix = ionic_x
    low_iy, high_iy = ionic_y
    neighbour_cells = [
        (shift_x(ionic, None, high_ix, -1, 1), shift_x(ionic, low_ix, None, 1, 1)),
        (shift_x(ionic, None, high_iy, -1, 2), shift_x(ionic, low_iy, None, 1, 2)),
        (jnp.roll(ionic, -1, 3), jnp.roll(ionic, 1, 3)),
    ]
    ions_out = drift_diffuse(
        ions,
        neighbour_cells,
        distribution_tuple,
        velocity,
        gradient_of_voltage,
        potential,
        free_electrostatic_share,
    )
    return (populations_out, ions_out, potential)


def solution(mesh):
    placed = (P(None, "gx", "gy", None), P(None, "gx", "gy", None), P("gx", "gy", None))
    return jax.shard_map(
        body,
        mesh=mesh,
        in_specs=placed,
        out_specs=(P(None, "gx", "gy", None), P(None, "gx", "gy", None), P("gx", "gy", None)),
        check_vma=False,
    )
```

```python
import math

import jax
import jax.numpy as jnp
from jax import lax
from jax.experimental import pallas as pl
from jax.experimental.pallas import tpu as pltpu
from jax.sharding import PartitionSpec as P

PRECISE = lax.Precision.HIGHEST
SOLVE = lax.Precision.HIGH
LATTICE_VELOCITY = [
    (0, 0, 0),
    (1, 0, 0),
    (-1, 0, 0),
    (0, 1, 0),
    (0, -1, 0),
    (0, 0, 1),
    (0, 0, -1),
    (1, 1, 0),
    (-1, -1, 0),
    (1, -1, 0),
    (-1, 1, 0),
    (1, 0, 1),
    (-1, 0, -1),
    (1, 0, -1),
    (-1, 0, 1),
    (0, 1, 1),
    (0, -1, -1),
    (0, 1, -1),
    (0, -1, 1),
]
WEIGHTS = [1.0 / 3.0] + [1.0 / 18.0] * 6 + [1.0 / 36.0] * 12
OPPOSITE = [0, 2, 1, 4, 3, 6, 5, 8, 7, 10, 9, 12, 11, 14, 13, 16, 15, 18, 17]
RELAXATION = 0.8
SCREENING = 0.001
WALL_CHARGE = -0.1
FIELD_EXT = 0.3
DIFFUSIVITY = 0.1

PLUS_X = [i for i in range(19) if LATTICE_VELOCITY[i][0] == 1]
MINUS_X = [i for i in range(19) if LATTICE_VELOCITY[i][0] == -1]
PLUS_Y = [i for i in range(19) if LATTICE_VELOCITY[i][1] == 1]
MINUS_Y = [i for i in range(19) if LATTICE_VELOCITY[i][1] == -1]
CROSS_X = PLUS_X + MINUS_X
CROSS_Y = PLUS_Y + MINUS_Y
DIAGONAL = [7, 8, 9, 10]


def ring(axis, step):
    count = lax.axis_size(axis)
    return [(i, (i + step) % count) for i in range(count)]


def halos(block, axis, dim):
    n = block.shape[dim]
    low = lax.ppermute(lax.slice_in_dim(block, n - 1, n, axis=dim), axis, ring(axis, 1))
    high = lax.ppermute(lax.slice_in_dim(block, 0, 1, axis=dim), axis, ring(axis, -1))
    return low, high


def diagonal_pairs(step_x, step_y):
    nx = lax.axis_size("gx")
    ny = lax.axis_size("gy")
    pairs = []
    for a in range(nx):
        for b in range(ny):
            pairs.append((a * ny + b, ((a + step_x) % nx) * ny + (b + step_y) % ny))
    return pairs


def sine_table(length):
    series = jnp.arange(length, dtype=jnp.int32) + 1
    product = series[:, None] * series[None, :] % (2 * (length + 1))
    return jnp.sin(product.astype(jnp.float32) * (math.pi / (length + 1)))


def fourier_pair(length):
    series = jnp.arange(length, dtype=jnp.int32)
    product = series[:, None] * series[None, :] % length
    angles = product.astype(jnp.float32) * (2.0 * math.pi / length)
    return jnp.stack([jnp.cos(angles), -jnp.sin(angles)])


def wall_eigen(first, number, total):
    modes = (jnp.arange(number, dtype=jnp.int32) + first + 1).astype(jnp.float32)
    return 2.0 - 2.0 * jnp.cos(modes * (math.pi / (total + 1)))


def cycle_angles(first, number, total):
    modes = jnp.arange(number, dtype=jnp.int32) + first
    return modes.astype(jnp.float32) * (2.0 * math.pi / total)


def solve_potential(charge):
    len_local, wid_local, depth = charge.shape
    len_parts = lax.axis_size("gx")
    wid_parts = lax.axis_size("gy")
    devices = len_parts * wid_parts
    modes_local = depth // devices
    full_len = len_local * len_parts
    full_wid = wid_local * wid_parts
    me = lax.axis_index("gx") * wid_parts + lax.axis_index("gy")
    depth_sine = sine_table(depth)
    sectioned = jnp.einsum("xyz,nz->nxy", charge, depth_sine, precision=SOLVE)
    sectioned = sectioned.reshape(devices, modes_local, len_local, wid_local)
    plane = lax.all_to_all(sectioned, ("gx", "gy"), 0, 0, tiled=True)
    plane = plane.reshape(len_parts, wid_parts, modes_local, len_local, wid_local)
    pair = fourier_pair(full_len).reshape(2, full_len, len_parts, len_local)
    spectra = jnp.einsum("rkax,abnxy->rknby", pair, plane, precision=SOLVE)
    spectra = spectra.reshape(2, full_len, modes_local, full_wid)
    wid_sine = sine_table(full_wid)
    spectra = jnp.einsum("my,rkny->rknm", wid_sine, spectra, precision=SOLVE)
    angles = cycle_angles(0, full_len, full_len)
    denom = (
        SCREENING
        + (2.0 - 2.0 * jnp.cos(angles))[:, None, None]
        + wall_eigen(me * modes_local, modes_local, depth)[None, :, None]
        + wall_eigen(0, full_wid, full_wid)[None, None, :]
    )
    spectra = spectra / denom[None]
    level = jnp.einsum("ym,rknm->rkny", wid_sine, spectra, precision=SOLVE) * (
        2.0 / (full_wid + 1)
    )
    level = level.reshape(2, full_len, modes_local, wid_parts, wid_local)
    lines = jnp.einsum("rkax,rknby->abnxy", pair, level, precision=SOLVE) * (1.0 / full_len)
    lines = lines.reshape(devices, modes_local, len_local, wid_local)
    back = lax.all_to_all(lines, ("gx", "gy"), 0, 0, tiled=True)
    back = back.reshape(depth, len_local, wid_local)
    return jnp.einsum("nz,nxy->xyz", depth_sine, back, precision=SOLVE) * (2.0 / (depth + 1))


def collide(populations, distribution_tuple, volumetric_push, entries=tuple(range(19))):
    density = populations[0]
    for entry in range(1, 19):
        density = density + populations[entry]
    moment = []
    for component in range(3):
        total = jnp.zeros_like(density)
        for entry in range(19):
            if LATTICE_VELOCITY[entry][component] != 0:
                total = total + LATTICE_VELOCITY[entry][component] * populations[entry]
        moment.append(total)
    velocity = [
        (moment[component] + 0.5 * volumetric_push[component]) / density for component in range(3)
    ]
    speed_sq = velocity[0] * velocity[0] + velocity[1] * velocity[1] + velocity[2] * velocity[2]
    power = (
        velocity[0] * volumetric_push[0]
        + velocity[1] * volumetric_push[1]
        + velocity[2] * volumetric_push[2]
    )
    posts = []
    for entry in entries:
        along = LATTICE_VELOCITY[entry]
        proj_vel = jnp.zeros_like(density)
        proj_force = jnp.zeros_like(density)
        for component in range(3):
            if along[component] != 0:
                proj_vel = proj_vel + along[component] * velocity[component]
                proj_force = proj_force + along[component] * volumetric_push[component]
        weight = WEIGHTS[entry]
        equil = (
            weight * density * (1.0 + 3.0 * proj_vel + 4.5 * proj_vel * proj_vel - 1.5 * speed_sq)
        )
        source = weight * (3.0 * (proj_force - power) + 9.0 * proj_vel * proj_force)
        moved = (
            populations[entry]
            - (populations[entry] - equil) * (1.0 / RELAXATION)
            + (1.0 - 0.5 / RELAXATION) * source
        )
        posts.append(jnp.where(distribution_tuple > 0.5, moved, populations[OPPOSITE[entry]]))
    return (posts, velocity)


def stream_kernel(pop_ref, fluid_ref, push_ref, out_ref, vel_ref, cols_ref):
    rows = pop_ref.shape[1]
    len_local, wid_local, depth = out_ref.shape[1:]
    for row in range(rows):
        pops = [pop_ref[entry, row] for entry in range(19)]
        push = [push_ref[component, row] for component in range(3)]
        posts, velocity = collide(pops, fluid_ref[row], push)
        here = pl.program_id(0) * rows + row
        for entry in range(19):
            cx, cy, cz = LATTICE_VELOCITY[entry]
            moved = posts[entry]
            if cy != 0:
                moved = pltpu.roll(moved, cy % wid_local, 0)
            if cz != 0:
                moved = pltpu.roll(moved, cz % depth, 1)
            target = (here + cx + len_local) % len_local
            out_ref[entry, target] = moved
            if cy != 0:
                at = 0 if cy == 1 else wid_local - 1
                cols_ref[CROSS_Y.index(entry), target] = moved[at : at + 1]
        for component in range(3):
            vel_ref[component, row] = velocity[component]


def stream_call(populations, distribution_tuple, push):
    entries, len_local, wid_local, depth = populations.shape
    rows = 2
    big = lambda n: pl.BlockSpec((n, rows, wid_local, depth), lambda i: (0, i, 0, 0))
    return pl.pallas_call(
        stream_kernel,
        grid=(len_local // rows,),
        in_specs=[big(entries), pl.BlockSpec((rows, wid_local, depth), lambda i: (i, 0, 0)), big(3)],
        out_specs=[
            pl.BlockSpec(populations.shape, lambda i: (0, 0, 0, 0)),
            big(3),
            pl.BlockSpec((len(CROSS_Y), len_local, 1, depth), lambda i: (0, 0, 0, 0)),
        ],
        out_shape=[
            jax.ShapeDtypeStruct(populations.shape, jnp.float32),
            jax.ShapeDtypeStruct((3, len_local, wid_local, depth), jnp.float32),
            jax.ShapeDtypeStruct((len(CROSS_Y), len_local, 1, depth), jnp.float32),
        ],
        compiler_params=pltpu.CompilerParams(vmem_limit_bytes=48 * 1024 * 1024),
    )(populations, distribution_tuple, push)


def patch_kernel(rows_ref, cols_ref, corner_ref, wrapped_hbm, out_hbm, sems):
    del wrapped_hbm
    len_local, wid_local = out_hbm.shape[1:3]
    first = []
    for k, entry in enumerate(CROSS_X):
        at = 0 if LATTICE_VELOCITY[entry][0] == 1 else len_local - 1
        first.append(pltpu.make_async_copy(rows_ref.at[k], out_hbm.at[entry, pl.ds(at, 1)], sems.at[len(first)]))
    for k, entry in enumerate(CROSS_Y):
        cx, cy, _ = LATTICE_VELOCITY[entry]
        at = 0 if cy == 1 else wid_local - 1
        low = 1 if cx == 1 else 0
        count = len_local - (cx != 0)
        first.append(
            pltpu.make_async_copy(
                cols_ref.at[k, pl.ds(low, count)],
                out_hbm.at[entry, pl.ds(low, count), pl.ds(at, 1)],
                sems.at[len(first)],
            )
        )
    for copy in first:
        copy.start()
    for copy in first:
        copy.wait()
    second = []
    for k, entry in enumerate(DIAGONAL):
        cx, cy, _ = LATTICE_VELOCITY[entry]
        ax = 0 if cx == 1 else len_local - 1
        ay = 0 if cy == 1 else wid_local - 1
        second.append(
            pltpu.make_async_copy(
                corner_ref.at[k], out_hbm.at[entry, pl.ds(ax, 1), pl.ds(ay, 1)], sems.at[len(first) + k]
            )
        )
    for copy in second:
        copy.start()
    for copy in second:
        copy.wait()


def patch_call(rows, cols, corners, wrapped):
    vmem = pl.BlockSpec(memory_space=pltpu.VMEM)
    return pl.pallas_call(
        patch_kernel,
        in_specs=[vmem, vmem, vmem, pl.BlockSpec(memory_space=pl.ANY)],
        out_specs=pl.BlockSpec(memory_space=pl.ANY),
        out_shape=jax.ShapeDtypeStruct(wrapped.shape, wrapped.dtype),
        scratch_shapes=[pltpu.SemaphoreType.DMA((len(CROSS_X) + len(CROSS_Y) + len(DIAGONAL),))],
        input_output_aliases={3: 0},
    )(rows, cols, corners, wrapped)


def drift_diffuse(
    conc,
    neighbour_cells,
    distribution_tuple,
    velocity,
    gradient_of_voltage,
    potential,
    free_electrostatic_share,
):
    laplace = -6.0 * conc
    drift = conc * (SCREENING * potential - free_electrostatic_share)[None]
    advect = jnp.zeros_like(conc)
    for component in range(3):
        upper, lower = neighbour_cells[component]
        up_val = upper[2:3] * upper[:2] + (1.0 - upper[2:3]) * conc
        low_val = lower[2:3] * lower[:2] + (1.0 - lower[2:3]) * conc
        laplace = laplace + up_val + low_val
        slope = 0.5 * (up_val - low_val)
        drift = drift - slope * gradient_of_voltage[component][None]
        advect = advect + slope * velocity[component][None]
    valence = jnp.asarray([1.0, -1.0], jnp.float32)[:, None, None, None]
    change = DIFFUSIVITY * (laplace + valence * drift) - advect
    return conc + distribution_tuple[None] * change


def shift_x(block, low, high, step, dim):
    if step == 1:
        return jnp.concatenate([low, lax.slice_in_dim(block, 0, block.shape[dim] - 1, axis=dim)], dim)
    if step == -1:
        return jnp.concatenate([lax.slice_in_dim(block, 1, None, axis=dim), high], dim)
    return block


def body(populations, ions, mask):
    len_local, wid_local, depth = mask.shape
    wid_parts = lax.axis_size("gy")
    wid_index = lax.axis_index("gy")
    distribution_tuple = (mask == 0).astype(jnp.float32)
    ionic = jnp.concatenate([ions, distribution_tuple[None]], axis=0)
    ionic_x = halos(ionic, "gx", 1)
    ionic_y = halos(ionic, "gy", 2)
    free_electrostatic_share = (
        distribution_tuple * (ions[0] - ions[1]) + (1.0 - distribution_tuple) * WALL_CHARGE
    )
    potential = solve_potential(free_electrostatic_share)
    pot_low_x, pot_high_x = halos(potential, "gx", 0)
    pot_low_y, pot_high_y = halos(potential, "gy", 1)
    pot_up_x = jnp.concatenate([potential[1:], pot_high_x], 0)
    pot_down_x = jnp.concatenate([pot_low_x, potential[:-1]], 0)
    field_len = FIELD_EXT - 0.5 * (pot_up_x - pot_down_x)
    top_keep = 1.0 - (wid_index == wid_parts - 1).astype(jnp.float32)
    bottom_keep = 1.0 - (wid_index == 0).astype(jnp.float32)
    above = jnp.concatenate([potential[:, 1:], pot_high_y * top_keep], 1)
    below = jnp.concatenate([pot_low_y * bottom_keep, potential[:, :-1]], 1)
    field_wid = -0.5 * (above - below)
    depth_pad = jnp.pad(potential, ((0, 0), (0, 0), (1, 1)))
    field_depth = -0.5 * (depth_pad[:, :, 2:] - depth_pad[:, :, :-2])
    gradient_of_voltage = [field_len, field_wid, field_depth]
    ion_concentration_sum = distribution_tuple * free_electrostatic_share
    volumetric_push = [ion_concentration_sum * voltage_grid for voltage_grid in gradient_of_voltage]
    push = jnp.stack(volumetric_push)
    wrapped, velocity, edge_cols = stream_call(populations, distribution_tuple, push)
    velocity = [velocity[component] for component in range(3)]
    last_x = len_local - 1
    last_y = wid_local - 1
    edge_x = {1: 0, -1: last_x}
    edge_y = {1: 0, -1: last_y}
    rows = {}
    cols = {}
    for step in (1, -1):
        group = [e for e in range(19) if LATTICE_VELOCITY[e][0] == step]
        sent = jnp.stack([wrapped[e, edge_x[step]] for e in group])
        got = lax.ppermute(sent, "gx", ring("gx", step))
        rows.update({e: got[k] for k, e in enumerate(group)})
        group = [e for e in range(19) if LATTICE_VELOCITY[e][1] == step]
        sent = jnp.stack([edge_cols[CROSS_Y.index(e)] for e in group])
        got = lax.ppermute(sent, "gy", ring("gy", step))
        cols.update({e: got[k] for k, e in enumerate(group)})
    corners = []
    for e in DIAGONAL:
        cx, cy, _ = LATTICE_VELOCITY[e]
        cell = edge_cols[CROSS_Y.index(e), edge_x[cx] : edge_x[cx] + 1]
        corners.append(lax.ppermute(cell, ("gx", "gy"), diagonal_pairs(cx, cy)))
    populations_out = patch_call(
        jnp.stack([rows[e][None] for e in CROSS_X]),
        jnp.stack([cols[e] for e in CROSS_Y]),
        jnp.stack(corners),
        wrapped,
    )

    low_ix, high_ix = ionic_x
    low_iy, high_iy = ionic_y
    neighbour_cells = [
        (shift_x(ionic, None, high_ix, -1, 1), shift_x(ionic, low_ix, None, 1, 1)),
        (shift_x(ionic, None, high_iy, -1, 2), shift_x(ionic, low_iy, None, 1, 2)),
        (jnp.roll(ionic, -1, 3), jnp.roll(ionic, 1, 3)),
    ]
    ions_out = drift_diffuse(
        ions,
        neighbour_cells,
        distribution_tuple,
        velocity,
        gradient_of_voltage,
        potential,
        free_electrostatic_share,
    )
    return (populations_out, ions_out, potential)


def solution(mesh):
    placed = (P(None, "gx", "gy", None), P(None, "gx", "gy", None), P("gx", "gy", None))
    return jax.shard_map(
        body,
        mesh=mesh,
        in_specs=placed,
        out_specs=(P(None, "gx", "gy", None), P(None, "gx", "gy", None), P("gx", "gy", None)),
        check_vma=False,
    )
```

```python
import math

import jax
import jax.numpy as jnp
from jax import lax
from jax.experimental import pallas as pl
from jax.experimental.pallas import tpu as pltpu
from jax.sharding import PartitionSpec as P

PRECISE = lax.Precision.HIGHEST
SOLVE = lax.Precision.HIGH
LATTICE_VELOCITY = [
    (0, 0, 0),
    (1, 0, 0),
    (-1, 0, 0),
    (0, 1, 0),
    (0, -1, 0),
    (0, 0, 1),
    (0, 0, -1),
    (1, 1, 0),
    (-1, -1, 0),
    (1, -1, 0),
    (-1, 1, 0),
    (1, 0, 1),
    (-1, 0, -1),
    (1, 0, -1),
    (-1, 0, 1),
    (0, 1, 1),
    (0, -1, -1),
    (0, 1, -1),
    (0, -1, 1),
]
WEIGHTS = [1.0 / 3.0] + [1.0 / 18.0] * 6 + [1.0 / 36.0] * 12
OPPOSITE = [0, 2, 1, 4, 3, 6, 5, 8, 7, 10, 9, 12, 11, 14, 13, 16, 15, 18, 17]
RELAXATION = 0.8
SCREENING = 0.001
WALL_CHARGE = -0.1
FIELD_EXT = 0.3
DIFFUSIVITY = 0.1

PLUS_X = [i for i in range(19) if LATTICE_VELOCITY[i][0] == 1]
MINUS_X = [i for i in range(19) if LATTICE_VELOCITY[i][0] == -1]
PLUS_Y = [i for i in range(19) if LATTICE_VELOCITY[i][1] == 1]
MINUS_Y = [i for i in range(19) if LATTICE_VELOCITY[i][1] == -1]
CROSS_X = PLUS_X + MINUS_X
CROSS_Y = PLUS_Y + MINUS_Y
DIAGONAL = [7, 8, 9, 10]


def ring(axis, step):
    count = lax.axis_size(axis)
    return [(i, (i + step) % count) for i in range(count)]


def halos(block, axis, dim):
    n = block.shape[dim]
    low = lax.ppermute(lax.slice_in_dim(block, n - 1, n, axis=dim), axis, ring(axis, 1))
    high = lax.ppermute(lax.slice_in_dim(block, 0, 1, axis=dim), axis, ring(axis, -1))
    return low, high


def diagonal_pairs(step_x, step_y):
    nx = lax.axis_size("gx")
    ny = lax.axis_size("gy")
    pairs = []
    for a in range(nx):
        for b in range(ny):
            pairs.append((a * ny + b, ((a + step_x) % nx) * ny + (b + step_y) % ny))
    return pairs


def sine_table(length):
    series = jnp.arange(length, dtype=jnp.int32) + 1
    product = series[:, None] * series[None, :] % (2 * (length + 1))
    return jnp.sin(product.astype(jnp.float32) * (math.pi / (length + 1)))


def fourier_pair(length):
    series = jnp.arange(length, dtype=jnp.int32)
    product = series[:, None] * series[None, :] % length
    angles = product.astype(jnp.float32) * (2.0 * math.pi / length)
    return jnp.stack([jnp.cos(angles), -jnp.sin(angles)])


def wall_eigen(first, number, total):
    modes = (jnp.arange(number, dtype=jnp.int32) + first + 1).astype(jnp.float32)
    return 2.0 - 2.0 * jnp.cos(modes * (math.pi / (total + 1)))


def cycle_angles(first, number, total):
    modes = jnp.arange(number, dtype=jnp.int32) + first
    return modes.astype(jnp.float32) * (2.0 * math.pi / total)


def solve_potential(charge):
    len_local, wid_local, depth = charge.shape
    len_parts = lax.axis_size("gx")
    wid_parts = lax.axis_size("gy")
    devices = len_parts * wid_parts
    modes_local = depth // devices
    full_len = len_local * len_parts
    full_wid = wid_local * wid_parts
    me = lax.axis_index("gx") * wid_parts + lax.axis_index("gy")
    depth_sine = sine_table(depth)
    sectioned = jnp.einsum("xyz,nz->nxy", charge, depth_sine, precision=SOLVE)
    sectioned = sectioned.reshape(devices, modes_local, len_local, wid_local)
    plane = lax.all_to_all(sectioned, ("gx", "gy"), 0, 0, tiled=True)
    plane = plane.reshape(len_parts, wid_parts, modes_local, len_local, wid_local)
    pair = fourier_pair(full_len).reshape(2, full_len, len_parts, len_local)
    spectra = jnp.einsum("rkax,abnxy->rknby", pair, plane, precision=SOLVE)
    spectra = spectra.reshape(2, full_len, modes_local, full_wid)
    wid_sine = sine_table(full_wid)
    spectra = jnp.einsum("my,rkny->rknm", wid_sine, spectra, precision=SOLVE)
    angles = cycle_angles(0, full_len, full_len)
    denom = (
        SCREENING
        + (2.0 - 2.0 * jnp.cos(angles))[:, None, None]
        + wall_eigen(me * modes_local, modes_local, depth)[None, :, None]
        + wall_eigen(0, full_wid, full_wid)[None, None, :]
    )
    spectra = spectra / denom[None]
    level = jnp.einsum("ym,rknm->rkny", wid_sine, spectra, precision=SOLVE) * (
        2.0 / (full_wid + 1)
    )
    plane = jnp.einsum("rkX,rknY->nXY", fourier_pair(full_len), level, precision=SOLVE) * (
        1.0 / full_len
    )
    plane = jnp.concatenate([plane[:, -1:], plane, plane[:, :1]], axis=1)
    plane = jnp.pad(plane, ((0, 0), (0, 0), (1, 1)))
    blocks = jnp.stack(
        [
            plane[:, a * len_local : a * len_local + len_local + 2, b * wid_local : b * wid_local + wid_local + 2]
            for a in range(len_parts)
            for b in range(wid_parts)
        ]
    )
    back = lax.all_to_all(blocks, ("gx", "gy"), 0, 0, tiled=True)
    back = back.reshape(depth, len_local + 2, wid_local + 2)
    return jnp.einsum("nz,nxy->xyz", depth_sine, back, precision=SOLVE) * (2.0 / (depth + 1))


def signed_sum(terms):
    total = None
    for sign, value in terms:
        if total is None:
            total = value if sign > 0 else -value
        else:
            total = total + value if sign > 0 else total - value
    return total


def collide(populations, distribution_tuple, volumetric_push):
    density = populations[0]
    for entry in range(1, 19):
        density = density + populations[entry]
    inverse = 1.0 / density
    velocity = []
    for component in range(3):
        moment = signed_sum(
            [(LATTICE_VELOCITY[e][component], populations[e]) for e in range(19) if LATTICE_VELOCITY[e][component] != 0]
        )
        velocity.append((moment + 0.5 * volumetric_push[component]) * inverse)
    speed_sq = velocity[0] * velocity[0] + velocity[1] * velocity[1] + velocity[2] * velocity[2]
    power = (
        velocity[0] * volumetric_push[0]
        + velocity[1] * volumetric_push[1]
        + velocity[2] * volumetric_push[2]
    )
    base = density * (1.0 - 1.5 * speed_sq)
    power3 = 3.0 * power
    keep = 1.0 - 1.0 / RELAXATION
    fluid = distribution_tuple > 0.5
    posts = []
    for entry in range(19):
        along = LATTICE_VELOCITY[entry]
        weight = WEIGHTS[entry]
        if entry == 0:
            equil = base
            source = -power3
        else:
            proj_vel = signed_sum([(along[c], velocity[c]) for c in range(3) if along[c] != 0])
            proj_force = signed_sum([(along[c], volumetric_push[c]) for c in range(3) if along[c] != 0])
            equil = base + density * proj_vel * (3.0 + 4.5 * proj_vel)
            source = proj_force * (3.0 + 9.0 * proj_vel) - power3
        moved = (
            keep * populations[entry]
            + (weight / RELAXATION) * equil
            + ((1.0 - 0.5 / RELAXATION) * weight) * source
        )
        posts.append(jnp.where(fluid, moved, populations[OPPOSITE[entry]]))
    return (posts, velocity)


def stream_kernel(pop_ref, fluid_ref, push_ref, out_ref, vel_ref, cols_ref):
    rows = pop_ref.shape[1]
    len_local, wid_local, depth = out_ref.shape[1:]
    for row in range(rows):
        pops = [pop_ref[entry, row] for entry in range(19)]
        push = [push_ref[component, row] for component in range(3)]
        posts, velocity = collide(pops, fluid_ref[row], push)
        here = pl.program_id(0) * rows + row
        for entry in range(19):
            cx, cy, cz = LATTICE_VELOCITY[entry]
            moved = posts[entry]
            if cy != 0:
                moved = pltpu.roll(moved, cy % wid_local, 0)
            if cz != 0:
                moved = pltpu.roll(moved, cz % depth, 1)
            target = (here + cx + len_local) % len_local
            out_ref[entry, target] = moved
            if cy != 0:
                at = 0 if cy == 1 else wid_local - 1
                cols_ref[CROSS_Y.index(entry), target] = moved[at : at + 1]
        for component in range(3):
            vel_ref[component, row] = velocity[component]


def stream_call(populations, distribution_tuple, push):
    entries, len_local, wid_local, depth = populations.shape
    rows = 2
    big = lambda n: pl.BlockSpec((n, rows, wid_local, depth), lambda i: (0, i, 0, 0))
    return pl.pallas_call(
        stream_kernel,
        grid=(len_local // rows,),
        in_specs=[big(entries), pl.BlockSpec((rows, wid_local, depth), lambda i: (i, 0, 0)), big(3)],
        out_specs=[
            pl.BlockSpec(populations.shape, lambda i: (0, 0, 0, 0)),
            big(3),
            pl.BlockSpec((len(CROSS_Y), len_local, 1, depth), lambda i: (0, 0, 0, 0)),
        ],
        out_shape=[
            jax.ShapeDtypeStruct(populations.shape, jnp.float32),
            jax.ShapeDtypeStruct((3, len_local, wid_local, depth), jnp.float32),
            jax.ShapeDtypeStruct((len(CROSS_Y), len_local, 1, depth), jnp.float32),
        ],
        compiler_params=pltpu.CompilerParams(vmem_limit_bytes=48 * 1024 * 1024),
    )(populations, distribution_tuple, push)


def patch_kernel(rows_ref, cols_ref, corner_ref, wrapped_hbm, out_hbm, sems):
    del wrapped_hbm
    len_local, wid_local = out_hbm.shape[1:3]
    first = []
    for k, entry in enumerate(CROSS_X):
        at = 0 if LATTICE_VELOCITY[entry][0] == 1 else len_local - 1
        first.append(pltpu.make_async_copy(rows_ref.at[k], out_hbm.at[entry, pl.ds(at, 1)], sems.at[len(first)]))
    for k, entry in enumerate(CROSS_Y):
        cx, cy, _ = LATTICE_VELOCITY[entry]
        at = 0 if cy == 1 else wid_local - 1
        low = 1 if cx == 1 else 0
        count = len_local - (cx != 0)
        first.append(
            pltpu.make_async_copy(
                cols_ref.at[k, pl.ds(low, count)],
                out_hbm.at[entry, pl.ds(low, count), pl.ds(at, 1)],
                sems.at[len(first)],
            )
        )
    for copy in first:
        copy.start()
    for copy in first:
        copy.wait()
    second = []
    for k, entry in enumerate(DIAGONAL):
        cx, cy, _ = LATTICE_VELOCITY[entry]
        ax = 0 if cx == 1 else len_local - 1
        ay = 0 if cy == 1 else wid_local - 1
        second.append(
            pltpu.make_async_copy(
                corner_ref.at[k], out_hbm.at[entry, pl.ds(ax, 1), pl.ds(ay, 1)], sems.at[len(first) + k]
            )
        )
    for copy in second:
        copy.start()
    for copy in second:
        copy.wait()


def patch_call(rows, cols, corners, wrapped):
    vmem = pl.BlockSpec(memory_space=pltpu.VMEM)
    return pl.pallas_call(
        patch_kernel,
        in_specs=[vmem, vmem, vmem, pl.BlockSpec(memory_space=pl.ANY)],
        out_specs=pl.BlockSpec(memory_space=pl.ANY),
        out_shape=jax.ShapeDtypeStruct(wrapped.shape, wrapped.dtype),
        scratch_shapes=[pltpu.SemaphoreType.DMA((len(CROSS_X) + len(CROSS_Y) + len(DIAGONAL),))],
        input_output_aliases={3: 0},
    )(rows, cols, corners, wrapped)


def drift_diffuse(
    conc,
    neighbour_cells,
    distribution_tuple,
    velocity,
    gradient_of_voltage,
    potential,
    free_electrostatic_share,
):
    laplace = -6.0 * conc
    drift = conc * (SCREENING * potential - free_electrostatic_share)[None]
    advect = jnp.zeros_like(conc)
    for component in range(3):
        upper, lower = neighbour_cells[component]
        up_val = upper[2:3] * upper[:2] + (1.0 - upper[2:3]) * conc
        low_val = lower[2:3] * lower[:2] + (1.0 - lower[2:3]) * conc
        laplace = laplace + up_val + low_val
        slope = 0.5 * (up_val - low_val)
        drift = drift - slope * gradient_of_voltage[component][None]
        advect = advect + slope * velocity[component][None]
    valence = jnp.asarray([1.0, -1.0], jnp.float32)[:, None, None, None]
    change = DIFFUSIVITY * (laplace + valence * drift) - advect
    return conc + distribution_tuple[None] * change


def shift_x(block, low, high, step, dim):
    if step == 1:
        return jnp.concatenate([low, lax.slice_in_dim(block, 0, block.shape[dim] - 1, axis=dim)], dim)
    if step == -1:
        return jnp.concatenate([lax.slice_in_dim(block, 1, None, axis=dim), high], dim)
    return block


def body(populations, ions, mask):
    len_local, wid_local, depth = mask.shape
    wid_parts = lax.axis_size("gy")
    wid_index = lax.axis_index("gy")
    distribution_tuple = (mask == 0).astype(jnp.float32)
    ionic = jnp.concatenate([ions, distribution_tuple[None]], axis=0)
    ionic_x = halos(ionic, "gx", 1)
    ionic_y = halos(ionic, "gy", 2)
    free_electrostatic_share = (
        distribution_tuple * (ions[0] - ions[1]) + (1.0 - distribution_tuple) * WALL_CHARGE
    )
    extended = solve_potential(free_electrostatic_share)
    potential = extended[1:-1, 1:-1]
    field_len = FIELD_EXT - 0.5 * (extended[2:, 1:-1] - extended[:-2, 1:-1])
    field_wid = -0.5 * (extended[1:-1, 2:] - extended[1:-1, :-2])
    depth_pad = jnp.pad(potential, ((0, 0), (0, 0), (1, 1)))
    field_depth = -0.5 * (depth_pad[:, :, 2:] - depth_pad[:, :, :-2])
    gradient_of_voltage = [field_len, field_wid, field_depth]
    ion_concentration_sum = distribution_tuple * free_electrostatic_share
    volumetric_push = [ion_concentration_sum * voltage_grid for voltage_grid in gradient_of_voltage]
    push = jnp.stack(volumetric_push)
    wrapped, velocity, edge_cols = stream_call(populations, distribution_tuple, push)
    velocity = [velocity[component] for component in range(3)]
    last_x = len_local - 1
    last_y = wid_local - 1
    edge_x = {1: 0, -1: last_x}
    edge_y = {1: 0, -1: last_y}
    rows = {}
    cols = {}
    for step in (1, -1):
        group = [e for e in range(19) if LATTICE_VELOCITY[e][0] == step]
        sent = jnp.stack([wrapped[e, edge_x[step]] for e in group])
        got = lax.ppermute(sent, "gx", ring("gx", step))
        rows.update({e: got[k] for k, e in enumerate(group)})
        group = [e for e in range(19) if LATTICE_VELOCITY[e][1] == step]
        sent = jnp.stack([edge_cols[CROSS_Y.index(e)] for e in group])
        got = lax.ppermute(sent, "gy", ring("gy", step))
        cols.update({e: got[k] for k, e in enumerate(group)})
    corners = []
    for e in DIAGONAL:
        cx, cy, _ = LATTICE_VELOCITY[e]
        cell = edge_cols[CROSS_Y.index(e), edge_x[cx] : edge_x[cx] + 1]
        corners.append(lax.ppermute(cell, ("gx", "gy"), diagonal_pairs(cx, cy)))
    populations_out = patch_call(
        jnp.stack([rows[e][None] for e in CROSS_X]),
        jnp.stack([cols[e] for e in CROSS_Y]),
        jnp.stack(corners),
        wrapped,
    )

    low_ix, high_ix = ionic_x
    low_iy, high_iy = ionic_y
    neighbour_cells = [
        (shift_x(ionic, None, high_ix, -1, 1), shift_x(ionic, low_ix, None, 1, 1)),
        (shift_x(ionic, None, high_iy, -1, 2), shift_x(ionic, low_iy, None, 1, 2)),
        (jnp.roll(ionic, -1, 3), jnp.roll(ionic, 1, 3)),
    ]
    ions_out = drift_diffuse(
        ions,
        neighbour_cells,
        distribution_tuple,
        velocity,
        gradient_of_voltage,
        potential,
        free_electrostatic_share,
    )
    return (populations_out, ions_out, potential)


def solution(mesh):
    placed = (P(None, "gx", "gy", None), P(None, "gx", "gy", None), P("gx", "gy", None))
    return jax.shard_map(
        body,
        mesh=mesh,
        in_specs=placed,
        out_specs=(P(None, "gx", "gy", None), P(None, "gx", "gy", None), P("gx", "gy", None)),
        check_vma=False,
    )
```

```python
import functools
import math

import jax
import jax.numpy as jnp
from jax import lax
from jax.experimental import pallas as pl
from jax.experimental.pallas import tpu as pltpu
from jax.sharding import PartitionSpec as P


SOLVE = lax.Precision.HIGH
LATTICE_VELOCITY = [
    (0, 0, 0),
    (1, 0, 0),
    (-1, 0, 0),
    (0, 1, 0),
    (0, -1, 0),
    (0, 0, 1),
    (0, 0, -1),
    (1, 1, 0),
    (-1, -1, 0),
    (1, -1, 0),
    (-1, 1, 0),
    (1, 0, 1),
    (-1, 0, -1),
    (1, 0, -1),
    (-1, 0, 1),
    (0, 1, 1),
    (0, -1, -1),
    (0, 1, -1),
    (0, -1, 1),
]
WEIGHTS = [1.0 / 3.0] + [1.0 / 18.0] * 6 + [1.0 / 36.0] * 12
OPPOSITE = [0, 2, 1, 4, 3, 6, 5, 8, 7, 10, 9, 12, 11, 14, 13, 16, 15, 18, 17]
RELAXATION = 0.8
SCREENING = 0.001
WALL_CHARGE = -0.1
FIELD_EXT = 0.3
DIFFUSIVITY = 0.1

PLUS_X = [i for i in range(19) if LATTICE_VELOCITY[i][0] == 1]
MINUS_X = [i for i in range(19) if LATTICE_VELOCITY[i][0] == -1]
PLUS_Y = [i for i in range(19) if LATTICE_VELOCITY[i][1] == 1]
MINUS_Y = [i for i in range(19) if LATTICE_VELOCITY[i][1] == -1]
CROSS_X = PLUS_X + MINUS_X
CROSS_Y = PLUS_Y + MINUS_Y
DIAGONAL = [7, 8, 9, 10]


def ring(axis, step):
    count = lax.axis_size(axis)
    return [(i, (i + step) % count) for i in range(count)]


def halos(block, axis, dim):
    n = block.shape[dim]
    low = lax.ppermute(lax.slice_in_dim(block, n - 1, n, axis=dim), axis, ring(axis, 1))
    high = lax.ppermute(lax.slice_in_dim(block, 0, 1, axis=dim), axis, ring(axis, -1))
    return low, high


def diagonal_pairs(step_x, step_y):
    nx = lax.axis_size("gx")
    ny = lax.axis_size("gy")
    pairs = []
    for a in range(nx):
        for b in range(ny):
            pairs.append((a * ny + b, ((a + step_x) % nx) * ny + (b + step_y) % ny))
    return pairs


def sine_table(length):
    series = jnp.arange(length, dtype=jnp.int32) + 1
    product = series[:, None] * series[None, :] % (2 * (length + 1))
    return jnp.sin(product.astype(jnp.float32) * (math.pi / (length + 1)))


def fourier_pair(length):
    series = jnp.arange(length, dtype=jnp.int32)
    product = series[:, None] * series[None, :] % length
    angles = product.astype(jnp.float32) * (2.0 * math.pi / length)
    return jnp.stack([jnp.cos(angles), -jnp.sin(angles)])


def wall_eigen(first, number, total):
    modes = (jnp.arange(number, dtype=jnp.int32) + first + 1).astype(jnp.float32)
    return 2.0 - 2.0 * jnp.cos(modes * (math.pi / (total + 1)))


def cycle_angles(first, number, total):
    modes = jnp.arange(number, dtype=jnp.int32) + first
    return modes.astype(jnp.float32) * (2.0 * math.pi / total)


def solve_potential(charge):
    len_local, wid_local, depth = charge.shape
    len_parts = lax.axis_size("gx")
    wid_parts = lax.axis_size("gy")
    devices = len_parts * wid_parts
    modes_local = depth // devices
    full_len = len_local * len_parts
    full_wid = wid_local * wid_parts
    me = lax.axis_index("gx") * wid_parts + lax.axis_index("gy")
    depth_sine = sine_table(depth)
    sectioned = jnp.einsum("xyz,nz->nxy", charge, depth_sine, precision=SOLVE)
    sectioned = sectioned.reshape(devices, modes_local, len_local, wid_local)
    plane = lax.all_to_all(sectioned, ("gx", "gy"), 0, 0, tiled=True)
    plane = plane.reshape(len_parts, wid_parts, modes_local, len_local, wid_local)
    pair = fourier_pair(full_len).reshape(2, full_len, len_parts, len_local)
    spectra = jnp.einsum("rkax,abnxy->rknby", pair, plane, precision=SOLVE)
    spectra = spectra.reshape(2, full_len, modes_local, full_wid)
    wid_sine = sine_table(full_wid)
    spectra = jnp.einsum("my,rkny->rknm", wid_sine, spectra, precision=SOLVE)
    angles = cycle_angles(0, full_len, full_len)
    denom = (
        SCREENING
        + (2.0 - 2.0 * jnp.cos(angles))[:, None, None]
        + wall_eigen(me * modes_local, modes_local, depth)[None, :, None]
        + wall_eigen(0, full_wid, full_wid)[None, None, :]
    )
    spectra = spectra / denom[None]
    level = jnp.einsum("ym,rknm->rkny", wid_sine, spectra, precision=SOLVE) * (
        2.0 / (full_wid + 1)
    )
    plane = jnp.einsum("rkX,rknY->nXY", fourier_pair(full_len), level, precision=SOLVE) * (
        1.0 / full_len
    )
    plane = jnp.concatenate([plane[:, -1:], plane, plane[:, :1]], axis=1)
    plane = jnp.pad(plane, ((0, 0), (0, 0), (1, 1)))
    blocks = jnp.stack(
        [
            plane[:, a * len_local : a * len_local + len_local + 2, b * wid_local : b * wid_local + wid_local + 2]
            for a in range(len_parts)
            for b in range(wid_parts)
        ]
    )
    back = lax.all_to_all(blocks, ("gx", "gy"), 0, 0, tiled=True)
    back = back.reshape(depth, len_local + 2, wid_local + 2)
    return jnp.einsum("nz,nxy->xyz", depth_sine, back, precision=SOLVE) * (2.0 / (depth + 1))


def signed_sum(terms):
    total = None
    for sign, value in terms:
        if total is None:
            total = value if sign > 0 else -value
        else:
            total = total + value if sign > 0 else total - value
    return total


def collide(populations, distribution_tuple, volumetric_push):
    density = populations[0]
    for entry in range(1, 19):
        density = density + populations[entry]
    inverse = 1.0 / density
    velocity = []
    for component in range(3):
        moment = signed_sum(
            [(LATTICE_VELOCITY[e][component], populations[e]) for e in range(19) if LATTICE_VELOCITY[e][component] != 0]
        )
        velocity.append((moment + 0.5 * volumetric_push[component]) * inverse)
    speed_sq = velocity[0] * velocity[0] + velocity[1] * velocity[1] + velocity[2] * velocity[2]
    power = (
        velocity[0] * volumetric_push[0]
        + velocity[1] * volumetric_push[1]
        + velocity[2] * volumetric_push[2]
    )
    base = density * (1.0 - 1.5 * speed_sq)
    power3 = 3.0 * power
    keep = 1.0 - 1.0 / RELAXATION
    fluid = distribution_tuple > 0.5
    posts = []
    for entry in range(19):
        along = LATTICE_VELOCITY[entry]
        weight = WEIGHTS[entry]
        if entry == 0:
            equil = base
            source = -power3
        else:
            proj_vel = signed_sum([(along[c], velocity[c]) for c in range(3) if along[c] != 0])
            proj_force = signed_sum([(along[c], volumetric_push[c]) for c in range(3) if along[c] != 0])
            equil = base + density * proj_vel * (3.0 + 4.5 * proj_vel)
            source = proj_force * (3.0 + 9.0 * proj_vel) - power3
        moved = (
            keep * populations[entry]
            + (weight / RELAXATION) * equil
            + ((1.0 - 0.5 / RELAXATION) * weight) * source
        )
        posts.append(jnp.where(fluid, moved, populations[OPPOSITE[entry]]))
    return (posts, velocity)


def stream_kernel(pop_ref, fluid_ref, push_ref, out_ref, vel_ref):
    rows = pop_ref.shape[1]
    len_local, wid_local, depth = out_ref.shape[1:]
    for row in range(rows):
        pops = [pop_ref[entry, row] for entry in range(19)]
        push = [push_ref[component, row] for component in range(3)]
        posts, velocity = collide(pops, fluid_ref[row], push)
        here = pl.program_id(0) * rows + row
        for entry in range(19):
            cx, cy, cz = LATTICE_VELOCITY[entry]
            moved = posts[entry]
            if cy != 0:
                moved = pltpu.roll(moved, cy % wid_local, 0)
            if cz != 0:
                moved = pltpu.roll(moved, cz % depth, 1)
            out_ref[entry, (here + cx + len_local) % len_local] = moved
        for component in range(3):
            vel_ref[component, row] = velocity[component]


def stream_call(populations, distribution_tuple, push):
    entries, len_local, wid_local, depth = populations.shape
    rows = 2
    big = lambda n: pl.BlockSpec((n, rows, wid_local, depth), lambda i: (0, i, 0, 0))
    return pl.pallas_call(
        stream_kernel,
        grid=(len_local // rows,),
        in_specs=[big(entries), pl.BlockSpec((rows, wid_local, depth), lambda i: (i, 0, 0)), big(3)],
        out_specs=[pl.BlockSpec(populations.shape, lambda i: (0, 0, 0, 0)), big(3)],
        out_shape=[
            jax.ShapeDtypeStruct(populations.shape, jnp.float32),
            jax.ShapeDtypeStruct((3, len_local, wid_local, depth), jnp.float32),
        ],
        compiler_params=pltpu.CompilerParams(vmem_limit_bytes=48 * 1024 * 1024),
        cost_estimate=pl.CostEstimate(
            flops=500 * populations[0].size,
            transcendentals=populations[0].size,
            bytes_accessed=4 * (2 * populations.size + 7 * populations[0].size),
        ),
    )(populations, distribution_tuple, push)


def edge_kernel(pop_ref, fluid_ref, push_ref, out_ref, *, across):
    for side in range(pop_ref.shape[1]):
        pops = [pop_ref[entry, side] for entry in range(19)]
        push = [push_ref[component, side] for component in range(3)]
        posts, _ = collide(pops, fluid_ref[side], push)
        rows, lanes = posts[0].shape
        for entry in range(19):
            step = LATTICE_VELOCITY[entry][across]
            moved = posts[entry]
            if step != 0:
                moved = pltpu.roll(moved, step % rows, 0)
            if LATTICE_VELOCITY[entry][2] != 0:
                moved = pltpu.roll(moved, LATTICE_VELOCITY[entry][2] % lanes, 1)
            out_ref[entry, side] = moved


def edge_rows_call(populations, distribution_tuple, push):
    entries, len_local, wid_local, depth = populations.shape
    last = len_local - 1
    slab = lambda n: pl.BlockSpec((n, 1, wid_local, depth), lambda i: (0, i * last, 0, 0))
    return pl.pallas_call(
        functools.partial(edge_kernel, across=1),
        grid=(2,),
        in_specs=[slab(entries), pl.BlockSpec((1, wid_local, depth), lambda i: (i * last, 0, 0)), slab(3)],
        out_specs=pl.BlockSpec((entries, 1, wid_local, depth), lambda i: (0, i, 0, 0)),
        out_shape=jax.ShapeDtypeStruct((entries, 2, wid_local, depth), jnp.float32),
    )(populations, distribution_tuple, push)


def edge_cols_call(populations, distribution_tuple, push):
    entries, len_local, wid_local, depth = populations.shape
    last = wid_local - 1
    pick = lambda a, d: jnp.stack([lax.index_in_dim(a, last, d, False), lax.index_in_dim(a, 0, d, False)], d - 1)
    return pl.pallas_call(
        functools.partial(edge_kernel, across=0),
        out_shape=jax.ShapeDtypeStruct((entries, 2, len_local, depth), jnp.float32),
    )(pick(populations, 2), pick(distribution_tuple[None], 2)[0], pick(push, 2))


def patch_kernel(rows_ref, cols_ref, corner_ref, wrapped_hbm, out_hbm, sems):
    del wrapped_hbm
    len_local, wid_local = out_hbm.shape[1:3]
    first = []
    for k, entry in enumerate(CROSS_X):
        at = 0 if LATTICE_VELOCITY[entry][0] == 1 else len_local - 1
        first.append(pltpu.make_async_copy(rows_ref.at[k], out_hbm.at[entry, pl.ds(at, 1)], sems.at[len(first)]))
    for k, entry in enumerate(CROSS_Y):
        cx, cy, _ = LATTICE_VELOCITY[entry]
        at = 0 if cy == 1 else wid_local - 1
        low = 1 if cx == 1 else 0
        count = len_local - (cx != 0)
        first.append(
            pltpu.make_async_copy(
                cols_ref.at[k, pl.ds(low, count)],
                out_hbm.at[entry, pl.ds(low, count), pl.ds(at, 1)],
                sems.at[len(first)],
            )
        )
    for copy in first:
        copy.start()
    for copy in first:
        copy.wait()
    second = []
    for k, entry in enumerate(DIAGONAL):
        cx, cy, _ = LATTICE_VELOCITY[entry]
        ax = 0 if cx == 1 else len_local - 1
        ay = 0 if cy == 1 else wid_local - 1
        second.append(
            pltpu.make_async_copy(
                corner_ref.at[k], out_hbm.at[entry, pl.ds(ax, 1), pl.ds(ay, 1)], sems.at[len(first) + k]
            )
        )
    for copy in second:
        copy.start()
    for copy in second:
        copy.wait()


def patch_call(rows, cols, corners, wrapped):
    vmem = pl.BlockSpec(memory_space=pltpu.VMEM)
    return pl.pallas_call(
        patch_kernel,
        in_specs=[vmem, vmem, vmem, pl.BlockSpec(memory_space=pl.ANY)],
        out_specs=pl.BlockSpec(memory_space=pl.ANY),
        out_shape=jax.ShapeDtypeStruct(wrapped.shape, wrapped.dtype),
        scratch_shapes=[pltpu.SemaphoreType.DMA((len(CROSS_X) + len(CROSS_Y) + len(DIAGONAL),))],
        input_output_aliases={3: 0},
    )(rows, cols, corners, wrapped)


def drift_diffuse(
    conc,
    neighbour_cells,
    distribution_tuple,
    velocity,
    gradient_of_voltage,
    potential,
    free_electrostatic_share,
):
    laplace = -6.0 * conc
    drift = conc * (SCREENING * potential - free_electrostatic_share)[None]
    advect = jnp.zeros_like(conc)
    for component in range(3):
        upper, lower = neighbour_cells[component]
        up_val = upper[2:3] * upper[:2] + (1.0 - upper[2:3]) * conc
        low_val = lower[2:3] * lower[:2] + (1.0 - lower[2:3]) * conc
        laplace = laplace + up_val + low_val
        slope = 0.5 * (up_val - low_val)
        drift = drift - slope * gradient_of_voltage[component][None]
        advect = advect + slope * velocity[component][None]
    valence = jnp.asarray([1.0, -1.0], jnp.float32)[:, None, None, None]
    change = DIFFUSIVITY * (laplace + valence * drift) - advect
    return conc + distribution_tuple[None] * change


def shift_x(block, low, high, step, dim):
    if step == 1:
        return jnp.concatenate([low, lax.slice_in_dim(block, 0, block.shape[dim] - 1, axis=dim)], dim)
    if step == -1:
        return jnp.concatenate([lax.slice_in_dim(block, 1, None, axis=dim), high], dim)
    return block


def body(populations, ions, mask):
    len_local, _, _ = mask.shape
    distribution_tuple = (mask == 0).astype(jnp.float32)
    ionic = jnp.concatenate([ions, distribution_tuple[None]], axis=0)
    ionic_x = halos(ionic, "gx", 1)
    ionic_y = halos(ionic, "gy", 2)
    free_electrostatic_share = (
        distribution_tuple * (ions[0] - ions[1]) + (1.0 - distribution_tuple) * WALL_CHARGE
    )
    extended = solve_potential(free_electrostatic_share)
    potential = extended[1:-1, 1:-1]
    field_len = FIELD_EXT - 0.5 * (extended[2:, 1:-1] - extended[:-2, 1:-1])
    field_wid = -0.5 * (extended[1:-1, 2:] - extended[1:-1, :-2])
    depth_pad = jnp.pad(potential, ((0, 0), (0, 0), (1, 1)))
    field_depth = -0.5 * (depth_pad[:, :, 2:] - depth_pad[:, :, :-2])
    gradient_of_voltage = [field_len, field_wid, field_depth]
    ion_concentration_sum = distribution_tuple * free_electrostatic_share
    volumetric_push = [ion_concentration_sum * voltage_grid for voltage_grid in gradient_of_voltage]
    push = jnp.stack(volumetric_push)
    edge_rows = edge_rows_call(populations, distribution_tuple, push)
    edge_cols = edge_cols_call(populations, distribution_tuple, push)
    wrapped, velocity = stream_call(populations, distribution_tuple, push)
    velocity = [velocity[component] for component in range(3)]
    last_x = len_local - 1
    edge_x = {1: 0, -1: last_x}
    side = {1: 0, -1: 1}
    rows = {}
    cols = {}
    for step in (1, -1):
        group = [e for e in range(19) if LATTICE_VELOCITY[e][0] == step]
        sent = jnp.stack([edge_rows[e, 1 - side[step]] for e in group])
        got = lax.ppermute(sent, "gx", ring("gx", step))
        rows.update({e: got[k] for k, e in enumerate(group)})
        group = [e for e in range(19) if LATTICE_VELOCITY[e][1] == step]
        sent = jnp.stack([edge_cols[e, side[step]][:, None] for e in group])
        got = lax.ppermute(sent, "gy", ring("gy", step))
        cols.update({e: got[k] for k, e in enumerate(group)})
    corners = []
    for e in DIAGONAL:
        cx, cy, _ = LATTICE_VELOCITY[e]
        cell = edge_cols[e, side[cy], edge_x[cx] : edge_x[cx] + 1][None]
        corners.append(lax.ppermute(cell, ("gx", "gy"), diagonal_pairs(cx, cy)))
    populations_out = patch_call(
        jnp.stack([rows[e][None] for e in CROSS_X]),
        jnp.stack([cols[e] for e in CROSS_Y]),
        jnp.stack(corners),
        wrapped,
    )

    low_ix, high_ix = ionic_x
    low_iy, high_iy = ionic_y
    neighbour_cells = [
        (shift_x(ionic, None, high_ix, -1, 1), shift_x(ionic, low_ix, None, 1, 1)),
        (shift_x(ionic, None, high_iy, -1, 2), shift_x(ionic, low_iy, None, 1, 2)),
        (jnp.roll(ionic, -1, 3), jnp.roll(ionic, 1, 3)),
    ]
    ions_out = drift_diffuse(
        ions,
        neighbour_cells,
        distribution_tuple,
        velocity,
        gradient_of_voltage,
        potential,
        free_electrostatic_share,
    )
    return (populations_out, ions_out, potential)


def solution(mesh):
    placed = (P(None, "gx", "gy", None), P(None, "gx", "gy", None), P("gx", "gy", None))
    return jax.shard_map(
        body,
        mesh=mesh,
        in_specs=placed,
        out_specs=(P(None, "gx", "gy", None), P(None, "gx", "gy", None), P("gx", "gy", None)),
        check_vma=False,
    )
```

```python
import math

import jax
import jax.numpy as jnp
from jax import lax
from jax.experimental import pallas as pl
from jax.experimental.pallas import tpu as pltpu
from jax.sharding import PartitionSpec as P

PRECISE = lax.Precision.HIGHEST
SOLVE = lax.Precision.HIGH
LATTICE_VELOCITY = [
    (0, 0, 0),
    (1, 0, 0),
    (-1, 0, 0),
    (0, 1, 0),
    (0, -1, 0),
    (0, 0, 1),
    (0, 0, -1),
    (1, 1, 0),
    (-1, -1, 0),
    (1, -1, 0),
    (-1, 1, 0),
    (1, 0, 1),
    (-1, 0, -1),
    (1, 0, -1),
    (-1, 0, 1),
    (0, 1, 1),
    (0, -1, -1),
    (0, 1, -1),
    (0, -1, 1),
]
WEIGHTS = [1.0 / 3.0] + [1.0 / 18.0] * 6 + [1.0 / 36.0] * 12
OPPOSITE = [0, 2, 1, 4, 3, 6, 5, 8, 7, 10, 9, 12, 11, 14, 13, 16, 15, 18, 17]
RELAXATION = 0.8
SCREENING = 0.001
WALL_CHARGE = -0.1
FIELD_EXT = 0.3
DIFFUSIVITY = 0.1

PLUS_X = [i for i in range(19) if LATTICE_VELOCITY[i][0] == 1]
MINUS_X = [i for i in range(19) if LATTICE_VELOCITY[i][0] == -1]
PLUS_Y = [i for i in range(19) if LATTICE_VELOCITY[i][1] == 1]
MINUS_Y = [i for i in range(19) if LATTICE_VELOCITY[i][1] == -1]
CROSS_X = PLUS_X + MINUS_X
CROSS_Y = PLUS_Y + MINUS_Y
DIAGONAL = [7, 8, 9, 10]


def ring(axis, step):
    count = lax.axis_size(axis)
    return [(i, (i + step) % count) for i in range(count)]


def halos(block, axis, dim):
    n = block.shape[dim]
    low = lax.ppermute(lax.slice_in_dim(block, n - 1, n, axis=dim), axis, ring(axis, 1))
    high = lax.ppermute(lax.slice_in_dim(block, 0, 1, axis=dim), axis, ring(axis, -1))
    return low, high


def diagonal_pairs(step_x, step_y):
    nx = lax.axis_size("gx")
    ny = lax.axis_size("gy")
    pairs = []
    for a in range(nx):
        for b in range(ny):
            pairs.append((a * ny + b, ((a + step_x) % nx) * ny + (b + step_y) % ny))
    return pairs


def sine_table(length):
    series = jnp.arange(length, dtype=jnp.int32) + 1
    product = series[:, None] * series[None, :] % (2 * (length + 1))
    return jnp.sin(product.astype(jnp.float32) * (math.pi / (length + 1)))


def fourier_pair(length):
    series = jnp.arange(length, dtype=jnp.int32)
    product = series[:, None] * series[None, :] % length
    angles = product.astype(jnp.float32) * (2.0 * math.pi / length)
    return jnp.stack([jnp.cos(angles), -jnp.sin(angles)])


def wall_eigen(first, number, total):
    modes = (jnp.arange(number, dtype=jnp.int32) + first + 1).astype(jnp.float32)
    return 2.0 - 2.0 * jnp.cos(modes * (math.pi / (total + 1)))


def cycle_angles(first, number, total):
    modes = jnp.arange(number, dtype=jnp.int32) + first
    return modes.astype(jnp.float32) * (2.0 * math.pi / total)


def solve_potential(charge):
    len_local, wid_local, depth = charge.shape
    len_parts = lax.axis_size("gx")
    wid_parts = lax.axis_size("gy")
    devices = len_parts * wid_parts
    modes_local = depth // devices
    full_len = len_local * len_parts
    full_wid = wid_local * wid_parts
    me = lax.axis_index("gx") * wid_parts + lax.axis_index("gy")
    depth_sine = sine_table(depth)
    flat = charge.reshape(len_local * wid_local, depth)
    sectioned = jnp.einsum("pz,nz->np", flat, depth_sine, precision=SOLVE)
    chunk = modes_local * len_local * wid_local
    sectioned = sectioned.reshape(devices, chunk // 128, 128)
    plane = lax.all_to_all(sectioned, ("gx", "gy"), 0, 0, tiled=True)
    plane = plane.reshape(len_parts, wid_parts, modes_local, len_local, wid_local)
    pair = fourier_pair(full_len).reshape(2, full_len, len_parts, len_local)
    spectra = jnp.einsum("rkax,abnxy->rknby", pair, plane, precision=SOLVE)
    spectra = spectra.reshape(2, full_len, modes_local, full_wid)
    wid_sine = sine_table(full_wid)
    spectra = jnp.einsum("my,rkny->rknm", wid_sine, spectra, precision=SOLVE)
    angles = cycle_angles(0, full_len, full_len)
    denom = (
        SCREENING
        + (2.0 - 2.0 * jnp.cos(angles))[:, None, None]
        + wall_eigen(me * modes_local, modes_local, depth)[None, :, None]
        + wall_eigen(0, full_wid, full_wid)[None, None, :]
    )
    spectra = spectra / denom[None]
    level = jnp.einsum("ym,rknm->rkny", wid_sine, spectra, precision=SOLVE) * (
        2.0 / (full_wid + 1)
    )
    plane = jnp.einsum("rkX,rknY->nXY", fourier_pair(full_len), level, precision=SOLVE) * (
        1.0 / full_len
    )
    plane = jnp.concatenate([plane[:, -1:], plane, plane[:, :1]], axis=1)
    plane = jnp.pad(plane, ((0, 0), (0, 0), (1, 1)))
    blocks = jnp.stack(
        [
            plane[:, a * len_local : a * len_local + len_local + 2, b * wid_local : b * wid_local + wid_local + 2]
            for a in range(len_parts)
            for b in range(wid_parts)
        ]
    )
    ext = (len_local + 2) * (wid_local + 2)
    blocks = blocks.reshape(devices, modes_local * ext)
    width = -(-modes_local * ext // 128) * 128
    blocks = jnp.pad(blocks, ((0, 0), (0, width - modes_local * ext))).reshape(devices, width // 128, 128)
    back = lax.all_to_all(blocks, ("gx", "gy"), 0, 0, tiled=True)
    back = back.reshape(devices, width)[:, : modes_local * ext].reshape(depth, ext)
    potential = jnp.einsum("np,nz->pz", back, depth_sine, precision=SOLVE) * (2.0 / (depth + 1))
    return potential.reshape(len_local + 2, wid_local + 2, depth)


def signed_sum(terms):
    total = None
    for sign, value in terms:
        if total is None:
            total = value if sign > 0 else -value
        else:
            total = total + value if sign > 0 else total - value
    return total


def collide(populations, distribution_tuple, volumetric_push):
    density = populations[0]
    for entry in range(1, 19):
        density = density + populations[entry]
    inverse = 1.0 / density
    velocity = []
    for component in range(3):
        moment = signed_sum(
            [(LATTICE_VELOCITY[e][component], populations[e]) for e in range(19) if LATTICE_VELOCITY[e][component] != 0]
        )
        velocity.append((moment + 0.5 * volumetric_push[component]) * inverse)
    speed_sq = velocity[0] * velocity[0] + velocity[1] * velocity[1] + velocity[2] * velocity[2]
    power = (
        velocity[0] * volumetric_push[0]
        + velocity[1] * volumetric_push[1]
        + velocity[2] * volumetric_push[2]
    )
    base = density * (1.0 - 1.5 * speed_sq)
    power3 = 3.0 * power
    keep = 1.0 - 1.0 / RELAXATION
    fluid = distribution_tuple > 0.5
    posts = []
    for entry in range(19):
        along = LATTICE_VELOCITY[entry]
        weight = WEIGHTS[entry]
        if entry == 0:
            equil = base
            source = -power3
        else:
            proj_vel = signed_sum([(along[c], velocity[c]) for c in range(3) if along[c] != 0])
            proj_force = signed_sum([(along[c], volumetric_push[c]) for c in range(3) if along[c] != 0])
            equil = base + density * proj_vel * (3.0 + 4.5 * proj_vel)
            source = proj_force * (3.0 + 9.0 * proj_vel) - power3
        moved = (
            keep * populations[entry]
            + (weight / RELAXATION) * equil
            + ((1.0 - 0.5 / RELAXATION) * weight) * source
        )
        posts.append(jnp.where(fluid, moved, populations[OPPOSITE[entry]]))
    return (posts, velocity)


def stream_kernel(pop_ref, fluid_ref, push_ref, out_ref, vel_ref, cols_ref):
    rows = pop_ref.shape[1]
    len_local, wid_local, depth = out_ref.shape[1:]
    for row in range(rows):
        pops = [pop_ref[entry, row] for entry in range(19)]
        push = [push_ref[component, row] for component in range(3)]
        posts, velocity = collide(pops, fluid_ref[row], push)
        here = pl.program_id(0) * rows + row
        for entry in range(19):
            cx, cy, cz = LATTICE_VELOCITY[entry]
            moved = posts[entry]
            if cy != 0:
                moved = pltpu.roll(moved, cy % wid_local, 0)
            if cz != 0:
                moved = pltpu.roll(moved, cz % depth, 1)
            target = (here + cx + len_local) % len_local
            out_ref[entry, target] = moved
            if cy != 0:
                at = 0 if cy == 1 else wid_local - 1
                cols_ref[CROSS_Y.index(entry), target] = moved[at : at + 1]
        for component in range(3):
            vel_ref[component, row] = velocity[component]


def stream_call(populations, distribution_tuple, push):
    entries, len_local, wid_local, depth = populations.shape
    rows = 2
    big = lambda n: pl.BlockSpec((n, rows, wid_local, depth), lambda i: (0, i, 0, 0))
    return pl.pallas_call(
        stream_kernel,
        grid=(len_local // rows,),
        in_specs=[big(entries), pl.BlockSpec((rows, wid_local, depth), lambda i: (i, 0, 0)), big(3)],
        out_specs=[
            pl.BlockSpec(populations.shape, lambda i: (0, 0, 0, 0)),
            big(3),
            pl.BlockSpec((len(CROSS_Y), len_local, 1, depth), lambda i: (0, 0, 0, 0)),
        ],
        out_shape=[
            jax.ShapeDtypeStruct(populations.shape, jnp.float32),
            jax.ShapeDtypeStruct((3, len_local, wid_local, depth), jnp.float32),
            jax.ShapeDtypeStruct((len(CROSS_Y), len_local, 1, depth), jnp.float32),
        ],
        compiler_params=pltpu.CompilerParams(vmem_limit_bytes=48 * 1024 * 1024),
    )(populations, distribution_tuple, push)


def patch_kernel(rows_ref, cols_ref, corner_ref, wrapped_hbm, out_hbm, sems):
    del wrapped_hbm
    len_local, wid_local = out_hbm.shape[1:3]
    first = []
    for k, entry in enumerate(CROSS_X):
        at = 0 if LATTICE_VELOCITY[entry][0] == 1 else len_local - 1
        first.append(pltpu.make_async_copy(rows_ref.at[k], out_hbm.at[entry, pl.ds(at, 1)], sems.at[len(first)]))
    for k, entry in enumerate(CROSS_Y):
        cx, cy, _ = LATTICE_VELOCITY[entry]
        at = 0 if cy == 1 else wid_local - 1
        low = 1 if cx == 1 else 0
        count = len_local - (cx != 0)
        first.append(
            pltpu.make_async_copy(
                cols_ref.at[k, pl.ds(low, count)],
                out_hbm.at[entry, pl.ds(low, count), pl.ds(at, 1)],
                sems.at[len(first)],
            )
        )
    for copy in first:
        copy.start()
    for copy in first:
        copy.wait()
    second = []
    for k, entry in enumerate(DIAGONAL):
        cx, cy, _ = LATTICE_VELOCITY[entry]
        ax = 0 if cx == 1 else len_local - 1
        ay = 0 if cy == 1 else wid_local - 1
        second.append(
            pltpu.make_async_copy(
                corner_ref.at[k], out_hbm.at[entry, pl.ds(ax, 1), pl.ds(ay, 1)], sems.at[len(first) + k]
            )
        )
    for copy in second:
        copy.start()
    for copy in second:
        copy.wait()


def patch_call(rows, cols, corners, wrapped):
    vmem = pl.BlockSpec(memory_space=pltpu.VMEM)
    return pl.pallas_call(
        patch_kernel,
        in_specs=[vmem, vmem, vmem, pl.BlockSpec(memory_space=pl.ANY)],
        out_specs=pl.BlockSpec(memory_space=pl.ANY),
        out_shape=jax.ShapeDtypeStruct(wrapped.shape, wrapped.dtype),
        scratch_shapes=[pltpu.SemaphoreType.DMA((len(CROSS_X) + len(CROSS_Y) + len(DIAGONAL),))],
        input_output_aliases={3: 0},
    )(rows, cols, corners, wrapped)


def drift_diffuse(
    conc,
    neighbour_cells,
    distribution_tuple,
    velocity,
    gradient_of_voltage,
    potential,
    free_electrostatic_share,
):
    laplace = -6.0 * conc
    drift = conc * (SCREENING * potential - free_electrostatic_share)[None]
    advect = jnp.zeros_like(conc)
    for component in range(3):
        upper, lower = neighbour_cells[component]
        up_val = upper[2:3] * upper[:2] + (1.0 - upper[2:3]) * conc
        low_val = lower[2:3] * lower[:2] + (1.0 - lower[2:3]) * conc
        laplace = laplace + up_val + low_val
        slope = 0.5 * (up_val - low_val)
        drift = drift - slope * gradient_of_voltage[component][None]
        advect = advect + slope * velocity[component][None]
    valence = jnp.asarray([1.0, -1.0], jnp.float32)[:, None, None, None]
    change = DIFFUSIVITY * (laplace + valence * drift) - advect
    return conc + distribution_tuple[None] * change


def shift_x(block, low, high, step, dim):
    if step == 1:
        return jnp.concatenate([low, lax.slice_in_dim(block, 0, block.shape[dim] - 1, axis=dim)], dim)
    if step == -1:
        return jnp.concatenate([lax.slice_in_dim(block, 1, None, axis=dim), high], dim)
    return block


def body(populations, ions, mask):
    len_local, wid_local, depth = mask.shape
    wid_parts = lax.axis_size("gy")
    wid_index = lax.axis_index("gy")
    distribution_tuple = (mask == 0).astype(jnp.float32)
    ionic = jnp.concatenate([ions, distribution_tuple[None]], axis=0)
    ionic_x = halos(ionic, "gx", 1)
    ionic_y = halos(ionic, "gy", 2)
    free_electrostatic_share = (
        distribution_tuple * (ions[0] - ions[1]) + (1.0 - distribution_tuple) * WALL_CHARGE
    )
    extended = solve_potential(free_electrostatic_share)
    potential = extended[1:-1, 1:-1]
    field_len = FIELD_EXT - 0.5 * (extended[2:, 1:-1] - extended[:-2, 1:-1])
    field_wid = -0.5 * (extended[1:-1, 2:] - extended[1:-1, :-2])
    depth_pad = jnp.pad(potential, ((0, 0), (0, 0), (1, 1)))
    field_depth = -0.5 * (depth_pad[:, :, 2:] - depth_pad[:, :, :-2])
    gradient_of_voltage = [field_len, field_wid, field_depth]
    ion_concentration_sum = distribution_tuple * free_electrostatic_share
    volumetric_push = [ion_concentration_sum * voltage_grid for voltage_grid in gradient_of_voltage]
    push = jnp.stack(volumetric_push)
    wrapped, velocity, edge_cols = stream_call(populations, distribution_tuple, push)
    velocity = [velocity[component] for component in range(3)]
    last_x = len_local - 1
    last_y = wid_local - 1
    edge_x = {1: 0, -1: last_x}
    edge_y = {1: 0, -1: last_y}
    rows = {}
    cols = {}
    for step in (1, -1):
        group = [e for e in range(19) if LATTICE_VELOCITY[e][0] == step]
        sent = jnp.stack([wrapped[e, edge_x[step]] for e in group])
        got = lax.ppermute(sent, "gx", ring("gx", step))
        rows.update({e: got[k] for k, e in enumerate(group)})
        group = [e for e in range(19) if LATTICE_VELOCITY[e][1] == step]
        sent = jnp.stack([edge_cols[CROSS_Y.index(e)] for e in group])
        got = lax.ppermute(sent, "gy", ring("gy", step))
        cols.update({e: got[k] for k, e in enumerate(group)})
    corners = []
    for e in DIAGONAL:
        cx, cy, _ = LATTICE_VELOCITY[e]
        cell = edge_cols[CROSS_Y.index(e), edge_x[cx] : edge_x[cx] + 1]
        corners.append(lax.ppermute(cell, ("gx", "gy"), diagonal_pairs(cx, cy)))
    populations_out = patch_call(
        jnp.stack([rows[e][None] for e in CROSS_X]),
        jnp.stack([cols[e] for e in CROSS_Y]),
        jnp.stack(corners),
        wrapped,
    )

    low_ix, high_ix = ionic_x
    low_iy, high_iy = ionic_y
    neighbour_cells = [
        (shift_x(ionic, None, high_ix, -1, 1), shift_x(ionic, low_ix, None, 1, 1)),
        (shift_x(ionic, None, high_iy, -1, 2), shift_x(ionic, low_iy, None, 1, 2)),
        (jnp.roll(ionic, -1, 3), jnp.roll(ionic, 1, 3)),
    ]
    ions_out = drift_diffuse(
        ions,
        neighbour_cells,
        distribution_tuple,
        velocity,
        gradient_of_voltage,
        potential,
        free_electrostatic_share,
    )
    return (populations_out, ions_out, potential)


def solution(mesh):
    placed = (P(None, "gx", "gy", None), P(None, "gx", "gy", None), P("gx", "gy", None))
    return jax.shard_map(
        body,
        mesh=mesh,
        in_specs=placed,
        out_specs=(P(None, "gx", "gy", None), P(None, "gx", "gy", None), P("gx", "gy", None)),
        check_vma=False,
    )
```

```python
import math

import jax
import jax.numpy as jnp
from jax import lax
from jax.experimental import pallas as pl
from jax.experimental.pallas import tpu as pltpu
from jax.sharding import PartitionSpec as P

PRECISE = lax.Precision.HIGHEST
SOLVE = lax.Precision.HIGH
LATTICE_VELOCITY = [
    (0, 0, 0),
    (1, 0, 0),
    (-1, 0, 0),
    (0, 1, 0),
    (0, -1, 0),
    (0, 0, 1),
    (0, 0, -1),
    (1, 1, 0),
    (-1, -1, 0),
    (1, -1, 0),
    (-1, 1, 0),
    (1, 0, 1),
    (-1, 0, -1),
    (1, 0, -1),
    (-1, 0, 1),
    (0, 1, 1),
    (0, -1, -1),
    (0, 1, -1),
    (0, -1, 1),
]
WEIGHTS = [1.0 / 3.0] + [1.0 / 18.0] * 6 + [1.0 / 36.0] * 12
OPPOSITE = [0, 2, 1, 4, 3, 6, 5, 8, 7, 10, 9, 12, 11, 14, 13, 16, 15, 18, 17]
RELAXATION = 0.8
SCREENING = 0.001
WALL_CHARGE = -0.1
FIELD_EXT = 0.3
DIFFUSIVITY = 0.1

PLUS_X = [i for i in range(19) if LATTICE_VELOCITY[i][0] == 1]
MINUS_X = [i for i in range(19) if LATTICE_VELOCITY[i][0] == -1]
PLUS_Y = [i for i in range(19) if LATTICE_VELOCITY[i][1] == 1]
MINUS_Y = [i for i in range(19) if LATTICE_VELOCITY[i][1] == -1]
CROSS_X = PLUS_X + MINUS_X
CROSS_Y = PLUS_Y + MINUS_Y
DIAGONAL = [7, 8, 9, 10]


def ring(axis, step):
    count = lax.axis_size(axis)
    return [(i, (i + step) % count) for i in range(count)]


def halos(block, axis, dim):
    n = block.shape[dim]
    low = lax.ppermute(lax.slice_in_dim(block, n - 1, n, axis=dim), axis, ring(axis, 1))
    high = lax.ppermute(lax.slice_in_dim(block, 0, 1, axis=dim), axis, ring(axis, -1))
    return low, high


def diagonal_pairs(step_x, step_y):
    nx = lax.axis_size("gx")
    ny = lax.axis_size("gy")
    pairs = []
    for a in range(nx):
        for b in range(ny):
            pairs.append((a * ny + b, ((a + step_x) % nx) * ny + (b + step_y) % ny))
    return pairs


def sine_table(length):
    series = jnp.arange(length, dtype=jnp.int32) + 1
    product = series[:, None] * series[None, :] % (2 * (length + 1))
    return jnp.sin(product.astype(jnp.float32) * (math.pi / (length + 1)))


def fourier_pair(length):
    series = jnp.arange(length, dtype=jnp.int32)
    product = series[:, None] * series[None, :] % length
    angles = product.astype(jnp.float32) * (2.0 * math.pi / length)
    return jnp.stack([jnp.cos(angles), -jnp.sin(angles)])


def wall_eigen(first, number, total):
    modes = (jnp.arange(number, dtype=jnp.int32) + first + 1).astype(jnp.float32)
    return 2.0 - 2.0 * jnp.cos(modes * (math.pi / (total + 1)))


def cycle_angles(first, number, total):
    modes = jnp.arange(number, dtype=jnp.int32) + first
    return modes.astype(jnp.float32) * (2.0 * math.pi / total)


def solve_potential(charge):
    len_local, wid_local, depth = charge.shape
    len_parts = lax.axis_size("gx")
    wid_parts = lax.axis_size("gy")
    devices = len_parts * wid_parts
    modes_local = depth // devices
    full_len = len_local * len_parts
    full_wid = wid_local * wid_parts
    me = lax.axis_index("gx") * wid_parts + lax.axis_index("gy")
    depth_sine = sine_table(depth)
    flat = charge.reshape(len_local * wid_local, depth)
    sectioned = jnp.einsum("pz,nz->np", flat, depth_sine, precision=SOLVE)
    chunk = modes_local * len_local * wid_local
    sectioned = sectioned.reshape(devices, chunk // 128, 128)
    plane = lax.all_to_all(sectioned, ("gx", "gy"), 0, 0, tiled=True)
    plane = plane.reshape(len_parts, wid_parts, modes_local, len_local, wid_local)
    pair = fourier_pair(full_len).reshape(2, full_len, len_parts, len_local)
    spectra = jnp.einsum("rkax,abnxy->rknby", pair, plane, precision=SOLVE)
    spectra = spectra.reshape(2, full_len, modes_local, full_wid)
    wid_sine = sine_table(full_wid)
    spectra = jnp.einsum("my,rkny->rknm", wid_sine, spectra, precision=SOLVE)
    angles = cycle_angles(0, full_len, full_len)
    denom = (
        SCREENING
        + (2.0 - 2.0 * jnp.cos(angles))[:, None, None]
        + wall_eigen(me * modes_local, modes_local, depth)[None, :, None]
        + wall_eigen(0, full_wid, full_wid)[None, None, :]
    )
    spectra = spectra / denom[None]
    level = jnp.einsum("ym,rknm->rkny", wid_sine, spectra, precision=SOLVE) * (
        2.0 / (full_wid + 1)
    )
    plane = jnp.einsum("rkX,rknY->nXY", fourier_pair(full_len), level, precision=SOLVE) * (
        1.0 / full_len
    )
    plane = jnp.concatenate([plane[:, -1:], plane, plane[:, :1]], axis=1)
    plane = jnp.pad(plane, ((0, 0), (0, 0), (1, 1)))
    blocks = jnp.stack(
        [
            plane[:, a * len_local : a * len_local + len_local + 2, b * wid_local : b * wid_local + wid_local + 2]
            for a in range(len_parts)
            for b in range(wid_parts)
        ]
    )
    back = lax.all_to_all(blocks, ("gx", "gy"), 0, 0, tiled=True)
    back = back.reshape(depth, len_local + 2, wid_local + 2)
    return jnp.einsum("nz,nxy->xyz", depth_sine, back, precision=SOLVE) * (2.0 / (depth + 1))


def signed_sum(terms):
    total = None
    for sign, value in terms:
        if total is None:
            total = value if sign > 0 else -value
        else:
            total = total + value if sign > 0 else total - value
    return total


def collide(populations, distribution_tuple, volumetric_push):
    density = populations[0]
    for entry in range(1, 19):
        density = density + populations[entry]
    inverse = 1.0 / density
    velocity = []
    for component in range(3):
        moment = signed_sum(
            [(LATTICE_VELOCITY[e][component], populations[e]) for e in range(19) if LATTICE_VELOCITY[e][component] != 0]
        )
        velocity.append((moment + 0.5 * volumetric_push[component]) * inverse)
    speed_sq = velocity[0] * velocity[0] + velocity[1] * velocity[1] + velocity[2] * velocity[2]
    power = (
        velocity[0] * volumetric_push[0]
        + velocity[1] * volumetric_push[1]
        + velocity[2] * volumetric_push[2]
    )
    base = density * (1.0 - 1.5 * speed_sq)
    power3 = 3.0 * power
    keep = 1.0 - 1.0 / RELAXATION
    fluid = distribution_tuple > 0.5
    posts = []
    for entry in range(19):
        along = LATTICE_VELOCITY[entry]
        weight = WEIGHTS[entry]
        if entry == 0:
            equil = base
            source = -power3
        else:
            proj_vel = signed_sum([(along[c], velocity[c]) for c in range(3) if along[c] != 0])
            proj_force = signed_sum([(along[c], volumetric_push[c]) for c in range(3) if along[c] != 0])
            equil = base + density * proj_vel * (3.0 + 4.5 * proj_vel)
            source = proj_force * (3.0 + 9.0 * proj_vel) - power3
        moved = (
            keep * populations[entry]
            + (weight / RELAXATION) * equil
            + ((1.0 - 0.5 / RELAXATION) * weight) * source
        )
        posts.append(jnp.where(fluid, moved, populations[OPPOSITE[entry]]))
    return (posts, velocity)


def stream_kernel(pop_ref, fluid_ref, push_ref, out_ref, vel_ref, cols_ref):
    rows = pop_ref.shape[1]
    len_local, wid_local, depth = out_ref.shape[1:]
    for row in range(rows):
        pops = [pop_ref[entry, row] for entry in range(19)]
        push = [push_ref[component, row] for component in range(3)]
        posts, velocity = collide(pops, fluid_ref[row], push)
        here = pl.program_id(0) * rows + row
        for entry in range(19):
            cx, cy, cz = LATTICE_VELOCITY[entry]
            moved = posts[entry]
            if cy != 0:
                moved = pltpu.roll(moved, cy % wid_local, 0)
            if cz != 0:
                moved = pltpu.roll(moved, cz % depth, 1)
            target = (here + cx + len_local) % len_local
            out_ref[entry, target] = moved
            if cy != 0:
                at = 0 if cy == 1 else wid_local - 1
                cols_ref[CROSS_Y.index(entry), target] = moved[at : at + 1]
        for component in range(3):
            vel_ref[component, row] = velocity[component]


def stream_call(populations, distribution_tuple, push):
    entries, len_local, wid_local, depth = populations.shape
    rows = 2
    big = lambda n: pl.BlockSpec((n, rows, wid_local, depth), lambda i: (0, i, 0, 0))
    return pl.pallas_call(
        stream_kernel,
        grid=(len_local // rows,),
        in_specs=[big(entries), pl.BlockSpec((rows, wid_local, depth), lambda i: (i, 0, 0)), big(3)],
        out_specs=[
            pl.BlockSpec(populations.shape, lambda i: (0, 0, 0, 0)),
            big(3),
            pl.BlockSpec((len(CROSS_Y), len_local, 1, depth), lambda i: (0, 0, 0, 0)),
        ],
        out_shape=[
            jax.ShapeDtypeStruct(populations.shape, jnp.float32),
            jax.ShapeDtypeStruct((3, len_local, wid_local, depth), jnp.float32),
            jax.ShapeDtypeStruct((len(CROSS_Y), len_local, 1, depth), jnp.float32),
        ],
        compiler_params=pltpu.CompilerParams(vmem_limit_bytes=48 * 1024 * 1024),
    )(populations, distribution_tuple, push)


def patch_kernel(rows_ref, cols_ref, corner_ref, wrapped_hbm, out_hbm, sems):
    del wrapped_hbm
    len_local, wid_local = out_hbm.shape[1:3]
    first = []
    for k, entry in enumerate(CROSS_X):
        at = 0 if LATTICE_VELOCITY[entry][0] == 1 else len_local - 1
        first.append(pltpu.make_async_copy(rows_ref.at[k], out_hbm.at[entry, pl.ds(at, 1)], sems.at[len(first)]))
    for k, entry in enumerate(CROSS_Y):
        cx, cy, _ = LATTICE_VELOCITY[entry]
        at = 0 if cy == 1 else wid_local - 1
        low = 1 if cx == 1 else 0
        count = len_local - (cx != 0)
        first.append(
            pltpu.make_async_copy(
                cols_ref.at[k, pl.ds(low, count)],
                out_hbm.at[entry, pl.ds(low, count), pl.ds(at, 1)],
                sems.at[len(first)],
            )
        )
    for copy in first:
        copy.start()
    for copy in first:
        copy.wait()
    second = []
    for k, entry in enumerate(DIAGONAL):
        cx, cy, _ = LATTICE_VELOCITY[entry]
        ax = 0 if cx == 1 else len_local - 1
        ay = 0 if cy == 1 else wid_local - 1
        second.append(
            pltpu.make_async_copy(
                corner_ref.at[k], out_hbm.at[entry, pl.ds(ax, 1), pl.ds(ay, 1)], sems.at[len(first) + k]
            )
        )
    for copy in second:
        copy.start()
    for copy in second:
        copy.wait()


def patch_call(rows, cols, corners, wrapped):
    vmem = pl.BlockSpec(memory_space=pltpu.VMEM)
    return pl.pallas_call(
        patch_kernel,
        in_specs=[vmem, vmem, vmem, pl.BlockSpec(memory_space=pl.ANY)],
        out_specs=pl.BlockSpec(memory_space=pl.ANY),
        out_shape=jax.ShapeDtypeStruct(wrapped.shape, wrapped.dtype),
        scratch_shapes=[pltpu.SemaphoreType.DMA((len(CROSS_X) + len(CROSS_Y) + len(DIAGONAL),))],
        input_output_aliases={3: 0},
    )(rows, cols, corners, wrapped)


def drift_diffuse(
    conc,
    neighbour_cells,
    distribution_tuple,
    velocity,
    gradient_of_voltage,
    potential,
    free_electrostatic_share,
):
    laplace = -6.0 * conc
    drift = conc * (SCREENING * potential - free_electrostatic_share)[None]
    advect = jnp.zeros_like(conc)
    for component in range(3):
        upper, lower = neighbour_cells[component]
        up_val = upper[2:3] * upper[:2] + (1.0 - upper[2:3]) * conc
        low_val = lower[2:3] * lower[:2] + (1.0 - lower[2:3]) * conc
        laplace = laplace + up_val + low_val
        slope = 0.5 * (up_val - low_val)
        drift = drift - slope * gradient_of_voltage[component][None]
        advect = advect + slope * velocity[component][None]
    valence = jnp.asarray([1.0, -1.0], jnp.float32)[:, None, None, None]
    change = DIFFUSIVITY * (laplace + valence * drift) - advect
    return conc + distribution_tuple[None] * change


def shift_x(block, low, high, step, dim):
    if step == 1:
        return jnp.concatenate([low, lax.slice_in_dim(block, 0, block.shape[dim] - 1, axis=dim)], dim)
    if step == -1:
        return jnp.concatenate([lax.slice_in_dim(block, 1, None, axis=dim), high], dim)
    return block


def body(populations, ions, mask):
    len_local, wid_local, depth = mask.shape
    wid_parts = lax.axis_size("gy")
    wid_index = lax.axis_index("gy")
    distribution_tuple = (mask == 0).astype(jnp.float32)
    ionic = jnp.concatenate([ions, distribution_tuple[None]], axis=0)
    ionic_x = halos(ionic, "gx", 1)
    ionic_y = halos(ionic, "gy", 2)
    free_electrostatic_share = (
        distribution_tuple * (ions[0] - ions[1]) + (1.0 - distribution_tuple) * WALL_CHARGE
    )
    extended = solve_potential(free_electrostatic_share)
    potential = extended[1:-1, 1:-1]
    field_len = FIELD_EXT - 0.5 * (extended[2:, 1:-1] - extended[:-2, 1:-1])
    field_wid = -0.5 * (extended[1:-1, 2:] - extended[1:-1, :-2])
    depth_pad = jnp.pad(potential, ((0, 0), (0, 0), (1, 1)))
    field_depth = -0.5 * (depth_pad[:, :, 2:] - depth_pad[:, :, :-2])
    gradient_of_voltage = [field_len, field_wid, field_depth]
    ion_concentration_sum = distribution_tuple * free_electrostatic_share
    volumetric_push = [ion_concentration_sum * voltage_grid for voltage_grid in gradient_of_voltage]
    push = jnp.stack(volumetric_push)
    wrapped, velocity, edge_cols = stream_call(populations, distribution_tuple, push)
    velocity = [velocity[component] for component in range(3)]
    last_x = len_local - 1
    last_y = wid_local - 1
    edge_x = {1: 0, -1: last_x}
    edge_y = {1: 0, -1: last_y}
    rows = {}
    cols = {}
    for step in (1, -1):
        group = [e for e in range(19) if LATTICE_VELOCITY[e][0] == step]
        sent = jnp.stack([wrapped[e, edge_x[step]] for e in group])
        got = lax.ppermute(sent, "gx", ring("gx", step))
        rows.update({e: got[k] for k, e in enumerate(group)})
        group = [e for e in range(19) if LATTICE_VELOCITY[e][1] == step]
        sent = jnp.stack([edge_cols[CROSS_Y.index(e)] for e in group])
        got = lax.ppermute(sent, "gy", ring("gy", step))
        cols.update({e: got[k] for k, e in enumerate(group)})
    corners = []
    for e in DIAGONAL:
        cx, cy, _ = LATTICE_VELOCITY[e]
        cell = edge_cols[CROSS_Y.index(e), edge_x[cx] : edge_x[cx] + 1]
        corners.append(lax.ppermute(cell, ("gx", "gy"), diagonal_pairs(cx, cy)))
    populations_out = patch_call(
        jnp.stack([rows[e][None] for e in CROSS_X]),
        jnp.stack([cols[e] for e in CROSS_Y]),
        jnp.stack(corners),
        wrapped,
    )

    low_ix, high_ix = ionic_x
    low_iy, high_iy = ionic_y
    neighbour_cells = [
        (shift_x(ionic, None, high_ix, -1, 1), shift_x(ionic, low_ix, None, 1, 1)),
        (shift_x(ionic, None, high_iy, -1, 2), shift_x(ionic, low_iy, None, 1, 2)),
        (jnp.roll(ionic, -1, 3), jnp.roll(ionic, 1, 3)),
    ]
    ions_out = drift_diffuse(
        ions,
        neighbour_cells,
        distribution_tuple,
        velocity,
        gradient_of_voltage,
        potential,
        free_electrostatic_share,
    )
    return (populations_out, ions_out, potential)


def solution(mesh):
    placed = (P(None, "gx", "gy", None), P(None, "gx", "gy", None), P("gx", "gy", None))
    return jax.shard_map(
        body,
        mesh=mesh,
        in_specs=placed,
        out_specs=(P(None, "gx", "gy", None), P(None, "gx", "gy", None), P("gx", "gy", None)),
        check_vma=False,
    )
```

```python
import math

import jax
import jax.numpy as jnp
from jax import lax
from jax.experimental import pallas as pl
from jax.experimental.pallas import tpu as pltpu
from jax.sharding import PartitionSpec as P

PRECISE = lax.Precision.HIGHEST
SOLVE = lax.Precision.HIGH
LATTICE_VELOCITY = [
    (0, 0, 0),
    (1, 0, 0),
    (-1, 0, 0),
    (0, 1, 0),
    (0, -1, 0),
    (0, 0, 1),
    (0, 0, -1),
    (1, 1, 0),
    (-1, -1, 0),
    (1, -1, 0),
    (-1, 1, 0),
    (1, 0, 1),
    (-1, 0, -1),
    (1, 0, -1),
    (-1, 0, 1),
    (0, 1, 1),
    (0, -1, -1),
    (0, 1, -1),
    (0, -1, 1),
]
WEIGHTS = [1.0 / 3.0] + [1.0 / 18.0] * 6 + [1.0 / 36.0] * 12
OPPOSITE = [0, 2, 1, 4, 3, 6, 5, 8, 7, 10, 9, 12, 11, 14, 13, 16, 15, 18, 17]
RELAXATION = 0.8
SCREENING = 0.001
WALL_CHARGE = -0.1
FIELD_EXT = 0.3
DIFFUSIVITY = 0.1

PLUS_X = [i for i in range(19) if LATTICE_VELOCITY[i][0] == 1]
MINUS_X = [i for i in range(19) if LATTICE_VELOCITY[i][0] == -1]
PLUS_Y = [i for i in range(19) if LATTICE_VELOCITY[i][1] == 1]
MINUS_Y = [i for i in range(19) if LATTICE_VELOCITY[i][1] == -1]
CROSS_X = PLUS_X + MINUS_X
CROSS_Y = PLUS_Y + MINUS_Y
DIAGONAL = [7, 8, 9, 10]


def ring(axis, step):
    count = lax.axis_size(axis)
    return [(i, (i + step) % count) for i in range(count)]


def halos(block, axis, dim):
    n = block.shape[dim]
    low = lax.ppermute(lax.slice_in_dim(block, n - 1, n, axis=dim), axis, ring(axis, 1))
    high = lax.ppermute(lax.slice_in_dim(block, 0, 1, axis=dim), axis, ring(axis, -1))
    return low, high


def diagonal_pairs(step_x, step_y):
    nx = lax.axis_size("gx")
    ny = lax.axis_size("gy")
    pairs = []
    for a in range(nx):
        for b in range(ny):
            pairs.append((a * ny + b, ((a + step_x) % nx) * ny + (b + step_y) % ny))
    return pairs


def sine_table(length):
    series = jnp.arange(length, dtype=jnp.int32) + 1
    product = series[:, None] * series[None, :] % (2 * (length + 1))
    return jnp.sin(product.astype(jnp.float32) * (math.pi / (length + 1)))


def fourier_pair(length):
    series = jnp.arange(length, dtype=jnp.int32)
    product = series[:, None] * series[None, :] % length
    angles = product.astype(jnp.float32) * (2.0 * math.pi / length)
    return jnp.stack([jnp.cos(angles), -jnp.sin(angles)])


def wall_eigen(first, number, total):
    modes = (jnp.arange(number, dtype=jnp.int32) + first + 1).astype(jnp.float32)
    return 2.0 - 2.0 * jnp.cos(modes * (math.pi / (total + 1)))


def cycle_angles(first, number, total):
    modes = jnp.arange(number, dtype=jnp.int32) + first
    return modes.astype(jnp.float32) * (2.0 * math.pi / total)


def solve_potential(charge):
    len_local, wid_local, depth = charge.shape
    len_parts = lax.axis_size("gx")
    wid_parts = lax.axis_size("gy")
    devices = len_parts * wid_parts
    modes_local = depth // devices
    full_len = len_local * len_parts
    full_wid = wid_local * wid_parts
    me = lax.axis_index("gx") * wid_parts + lax.axis_index("gy")
    depth_sine = sine_table(depth)
    flat = charge.reshape(len_local * wid_local, depth)
    sectioned = jnp.einsum("pz,nz->np", flat, depth_sine, precision=SOLVE)
    chunk = modes_local * len_local * wid_local
    sectioned = sectioned.reshape(devices, chunk // 128, 128)
    plane = lax.all_to_all(sectioned, ("gx", "gy"), 0, 0, tiled=True)
    plane = plane.reshape(len_parts, wid_parts, modes_local, len_local, wid_local)
    pair = fourier_pair(full_len).reshape(2, full_len, len_parts, len_local)
    spectra = jnp.einsum("rkax,abnxy->rknby", pair, plane, precision=SOLVE)
    spectra = spectra.reshape(2, full_len, modes_local, full_wid)
    wid_sine = sine_table(full_wid)
    spectra = jnp.einsum("my,rkny->rknm", wid_sine, spectra, precision=SOLVE)
    angles = cycle_angles(0, full_len, full_len)
    denom = (
        SCREENING
        + (2.0 - 2.0 * jnp.cos(angles))[:, None, None]
        + wall_eigen(me * modes_local, modes_local, depth)[None, :, None]
        + wall_eigen(0, full_wid, full_wid)[None, None, :]
    )
    spectra = spectra / denom[None]
    level = jnp.einsum("ym,rknm->rkny", wid_sine, spectra, precision=SOLVE) * (
        2.0 / (full_wid + 1)
    )
    plane = jnp.einsum("rkX,rknY->nXY", fourier_pair(full_len), level, precision=SOLVE) * (
        1.0 / full_len
    )
    plane = jnp.concatenate([plane[:, -1:], plane, plane[:, :1]], axis=1)
    plane = jnp.pad(plane, ((0, 0), (0, 0), (1, 1)))
    blocks = jnp.stack(
        [
            plane[:, a * len_local : a * len_local + len_local + 2, b * wid_local : b * wid_local + wid_local + 2]
            for a in range(len_parts)
            for b in range(wid_parts)
        ]
    )
    back = lax.all_to_all(blocks, ("gx", "gy"), 0, 0, tiled=True)
    back = back.reshape(depth, len_local + 2, wid_local + 2)
    return jnp.einsum("nz,nxy->xyz", depth_sine, back, precision=SOLVE) * (2.0 / (depth + 1))


def signed_sum(terms):
    total = None
    for sign, value in terms:
        if total is None:
            total = value if sign > 0 else -value
        else:
            total = total + value if sign > 0 else total - value
    return total


def collide(populations, distribution_tuple, volumetric_push):
    density = populations[0]
    for entry in range(1, 19):
        density = density + populations[entry]
    inverse = 1.0 / density
    velocity = []
    for component in range(3):
        moment = signed_sum(
            [(LATTICE_VELOCITY[e][component], populations[e]) for e in range(19) if LATTICE_VELOCITY[e][component] != 0]
        )
        velocity.append((moment + 0.5 * volumetric_push[component]) * inverse)
    speed_sq = velocity[0] * velocity[0] + velocity[1] * velocity[1] + velocity[2] * velocity[2]
    power = (
        velocity[0] * volumetric_push[0]
        + velocity[1] * volumetric_push[1]
        + velocity[2] * volumetric_push[2]
    )
    base = density * (1.0 - 1.5 * speed_sq)
    power3 = 3.0 * power
    keep = 1.0 - 1.0 / RELAXATION
    fluid = distribution_tuple > 0.5
    posts = []
    for entry in range(19):
        along = LATTICE_VELOCITY[entry]
        weight = WEIGHTS[entry]
        if entry == 0:
            equil = base
            source = -power3
        else:
            proj_vel = signed_sum([(along[c], velocity[c]) for c in range(3) if along[c] != 0])
            proj_force = signed_sum([(along[c], volumetric_push[c]) for c in range(3) if along[c] != 0])
            equil = base + density * proj_vel * (3.0 + 4.5 * proj_vel)
            source = proj_force * (3.0 + 9.0 * proj_vel) - power3
        moved = (
            keep * populations[entry]
            + (weight / RELAXATION) * equil
            + ((1.0 - 0.5 / RELAXATION) * weight) * source
        )
        posts.append(jnp.where(fluid, moved, populations[OPPOSITE[entry]]))
    return (posts, velocity)


def stream_kernel(pop_ref, fluid_ref, push_ref, out_ref, vel_ref, cols_ref):
    rows = pop_ref.shape[1]
    len_local, wid_local, depth = out_ref.shape[1:]
    for row in range(rows):
        pops = [pop_ref[entry, row] for entry in range(19)]
        push = [push_ref[component, row] for component in range(3)]
        posts, velocity = collide(pops, fluid_ref[row], push)
        here = pl.program_id(0) * rows + row
        for entry in range(19):
            cx, cy, cz = LATTICE_VELOCITY[entry]
            moved = posts[entry]
            if cy != 0:
                moved = pltpu.roll(moved, cy % wid_local, 0)
            if cz != 0:
                moved = pltpu.roll(moved, cz % depth, 1)
            target = (here + cx + len_local) % len_local
            out_ref[entry, target] = moved
            if cy != 0:
                at = 0 if cy == 1 else wid_local - 1
                cols_ref[CROSS_Y.index(entry), target] = moved[at : at + 1]
        for component in range(3):
            vel_ref[component, row] = velocity[component]


def stream_call(populations, distribution_tuple, push):
    entries, len_local, wid_local, depth = populations.shape
    rows = 2
    big = lambda n: pl.BlockSpec((n, rows, wid_local, depth), lambda i: (0, i, 0, 0))
    return pl.pallas_call(
        stream_kernel,
        grid=(len_local // rows,),
        in_specs=[big(entries), pl.BlockSpec((rows, wid_local, depth), lambda i: (i, 0, 0)), big(3)],
        out_specs=[
            pl.BlockSpec(populations.shape, lambda i: (0, 0, 0, 0)),
            big(3),
            pl.BlockSpec((len(CROSS_Y), len_local, 1, depth), lambda i: (0, 0, 0, 0)),
        ],
        out_shape=[
            jax.ShapeDtypeStruct(populations.shape, jnp.float32),
            jax.ShapeDtypeStruct((3, len_local, wid_local, depth), jnp.float32),
            jax.ShapeDtypeStruct((len(CROSS_Y), len_local, 1, depth), jnp.float32),
        ],
        compiler_params=pltpu.CompilerParams(vmem_limit_bytes=48 * 1024 * 1024),
    )(populations, distribution_tuple, push)


def patch_kernel(rows_ref, cols_ref, wrapped_hbm, out_hbm, sems):
    del wrapped_hbm
    len_local, wid_local = out_hbm.shape[1:3]
    first = []
    for k, entry in enumerate(CROSS_X):
        at = 0 if LATTICE_VELOCITY[entry][0] == 1 else len_local - 1
        first.append(pltpu.make_async_copy(rows_ref.at[k], out_hbm.at[entry, pl.ds(at, 1)], sems.at[k]))
    for copy in first:
        copy.start()
    for copy in first:
        copy.wait()
    second = []
    for k, entry in enumerate(CROSS_Y):
        at = 0 if LATTICE_VELOCITY[entry][1] == 1 else wid_local - 1
        second.append(
            pltpu.make_async_copy(
                cols_ref.at[k], out_hbm.at[entry, :, pl.ds(at, 1)], sems.at[len(first) + k]
            )
        )
    for copy in second:
        copy.start()
    for copy in second:
        copy.wait()


def patch_call(rows, cols, wrapped):
    vmem = pl.BlockSpec(memory_space=pltpu.VMEM)
    return pl.pallas_call(
        patch_kernel,
        in_specs=[vmem, vmem, pl.BlockSpec(memory_space=pl.ANY)],
        out_specs=pl.BlockSpec(memory_space=pl.ANY),
        out_shape=jax.ShapeDtypeStruct(wrapped.shape, wrapped.dtype),
        scratch_shapes=[pltpu.SemaphoreType.DMA((len(CROSS_X) + len(CROSS_Y),))],
        input_output_aliases={2: 0},
    )(rows, cols, wrapped)


def drift_diffuse(
    conc,
    neighbour_cells,
    distribution_tuple,
    velocity,
    gradient_of_voltage,
    potential,
    free_electrostatic_share,
):
    laplace = -6.0 * conc
    drift = conc * (SCREENING * potential - free_electrostatic_share)[None]
    advect = jnp.zeros_like(conc)
    for component in range(3):
        upper, lower = neighbour_cells[component]
        up_val = upper[2:3] * upper[:2] + (1.0 - upper[2:3]) * conc
        low_val = lower[2:3] * lower[:2] + (1.0 - lower[2:3]) * conc
        laplace = laplace + up_val + low_val
        slope = 0.5 * (up_val - low_val)
        drift = drift - slope * gradient_of_voltage[component][None]
        advect = advect + slope * velocity[component][None]
    valence = jnp.asarray([1.0, -1.0], jnp.float32)[:, None, None, None]
    change = DIFFUSIVITY * (laplace + valence * drift) - advect
    return conc + distribution_tuple[None] * change


def shift_x(block, low, high, step, dim):
    if step == 1:
        return jnp.concatenate([low, lax.slice_in_dim(block, 0, block.shape[dim] - 1, axis=dim)], dim)
    if step == -1:
        return jnp.concatenate([lax.slice_in_dim(block, 1, None, axis=dim), high], dim)
    return block


def body(populations, ions, mask):
    len_local, wid_local, depth = mask.shape
    wid_parts = lax.axis_size("gy")
    wid_index = lax.axis_index("gy")
    distribution_tuple = (mask == 0).astype(jnp.float32)
    ionic = jnp.concatenate([ions, distribution_tuple[None]], axis=0)
    free_electrostatic_share = (
        distribution_tuple * (ions[0] - ions[1]) + (1.0 - distribution_tuple) * WALL_CHARGE
    )
    extended = solve_potential(free_electrostatic_share)
    potential = extended[1:-1, 1:-1]
    field_len = FIELD_EXT - 0.5 * (extended[2:, 1:-1] - extended[:-2, 1:-1])
    field_wid = -0.5 * (extended[1:-1, 2:] - extended[1:-1, :-2])
    depth_pad = jnp.pad(potential, ((0, 0), (0, 0), (1, 1)))
    field_depth = -0.5 * (depth_pad[:, :, 2:] - depth_pad[:, :, :-2])
    gradient_of_voltage = [field_len, field_wid, field_depth]
    ion_concentration_sum = distribution_tuple * free_electrostatic_share
    volumetric_push = [ion_concentration_sum * voltage_grid for voltage_grid in gradient_of_voltage]
    push = jnp.stack(volumetric_push)
    wrapped, velocity, edge_cols = stream_call(populations, distribution_tuple, push)
    velocity = [velocity[component] for component in range(3)]
    last_x = len_local - 1
    last_y = wid_local - 1
    edge_x = {1: 0, -1: last_x}
    edge_y = {1: 0, -1: last_y}
    rows = {}
    cols = {}
    ionic_halo = {}
    for step in (1, -1):
        group = [e for e in range(19) if LATTICE_VELOCITY[e][0] == step]
        mine = ionic[:, last_x if step == 1 else 0]
        sent = jnp.concatenate([jnp.stack([wrapped[e, edge_x[step]] for e in group]), mine])
        got = lax.ppermute(sent, "gx", ring("gx", step))
        rows.update({e: got[k] for k, e in enumerate(group)})
        ionic_halo[("gx", step)] = got[len(group) :][:, None]
    for step in (1, -1):
        group = [e for e in range(19) if LATTICE_VELOCITY[e][1] == step]
        pieces = []
        for e in group:
            column = edge_cols[CROSS_Y.index(e)]
            cx = LATTICE_VELOCITY[e][0]
            if cx != 0:
                cell = rows[e][edge_y[step]][None, None]
                if edge_x[cx] == 0:
                    column = jnp.concatenate([cell, column[1:]])
                else:
                    column = jnp.concatenate([column[:-1], cell])
            pieces.append(column)
        mine = ionic[:, :, last_y if step == 1 else 0][:, :, None]
        sent = jnp.concatenate([jnp.stack(pieces), mine])
        got = lax.ppermute(sent, "gy", ring("gy", step))
        cols.update({e: got[k] for k, e in enumerate(group)})
        ionic_halo[("gy", step)] = got[len(group) :]
    populations_out = patch_call(
        jnp.stack([rows[e][None] for e in CROSS_X]),
        jnp.stack([cols[e] for e in CROSS_Y]),
        wrapped,
    )

    low_ix, high_ix = ionic_halo[("gx", 1)], ionic_halo[("gx", -1)]
    low_iy, high_iy = ionic_halo[("gy", 1)], ionic_halo[("gy", -1)]
    neighbour_cells = [
        (shift_x(ionic, None, high_ix, -1, 1), shift_x(ionic, low_ix, None, 1, 1)),
        (shift_x(ionic, None, high_iy, -1, 2), shift_x(ionic, low_iy, None, 1, 2)),
        (jnp.roll(ionic, -1, 3), jnp.roll(ionic, 1, 3)),
    ]
    ions_out = drift_diffuse(
        ions,
        neighbour_cells,
        distribution_tuple,
        velocity,
        gradient_of_voltage,
        potential,
        free_electrostatic_share,
    )
    return (populations_out, ions_out, potential)


def solution(mesh):
    placed = (P(None, "gx", "gy", None), P(None, "gx", "gy", None), P("gx", "gy", None))
    return jax.shard_map(
        body,
        mesh=mesh,
        in_specs=placed,
        out_specs=(P(None, "gx", "gy", None), P(None, "gx", "gy", None), P("gx", "gy", None)),
        check_vma=False,
    )
```

```python
import math

import jax
import jax.numpy as jnp
from jax import lax
from jax.experimental import pallas as pl
from jax.experimental.pallas import tpu as pltpu
from jax.sharding import PartitionSpec as P

PRECISE = lax.Precision.HIGHEST
SOLVE = lax.Precision.HIGH
LATTICE_VELOCITY = [
    (0, 0, 0),
    (1, 0, 0),
    (-1, 0, 0),
    (0, 1, 0),
    (0, -1, 0),
    (0, 0, 1),
    (0, 0, -1),
    (1, 1, 0),
    (-1, -1, 0),
    (1, -1, 0),
    (-1, 1, 0),
    (1, 0, 1),
    (-1, 0, -1),
    (1, 0, -1),
    (-1, 0, 1),
    (0, 1, 1),
    (0, -1, -1),
    (0, 1, -1),
    (0, -1, 1),
]
WEIGHTS = [1.0 / 3.0] + [1.0 / 18.0] * 6 + [1.0 / 36.0] * 12
OPPOSITE = [0, 2, 1, 4, 3, 6, 5, 8, 7, 10, 9, 12, 11, 14, 13, 16, 15, 18, 17]
RELAXATION = 0.8
SCREENING = 0.001
WALL_CHARGE = -0.1
FIELD_EXT = 0.3
DIFFUSIVITY = 0.1

PLUS_X = [i for i in range(19) if LATTICE_VELOCITY[i][0] == 1]
MINUS_X = [i for i in range(19) if LATTICE_VELOCITY[i][0] == -1]
PLUS_Y = [i for i in range(19) if LATTICE_VELOCITY[i][1] == 1]
MINUS_Y = [i for i in range(19) if LATTICE_VELOCITY[i][1] == -1]
CROSS_X = PLUS_X + MINUS_X
CROSS_Y = PLUS_Y + MINUS_Y
DIAGONAL = [7, 8, 9, 10]


def ring(axis, step):
    count = lax.axis_size(axis)
    return [(i, (i + step) % count) for i in range(count)]


def halos(block, axis, dim):
    n = block.shape[dim]
    low = lax.ppermute(lax.slice_in_dim(block, n - 1, n, axis=dim), axis, ring(axis, 1))
    high = lax.ppermute(lax.slice_in_dim(block, 0, 1, axis=dim), axis, ring(axis, -1))
    return low, high


def diagonal_pairs(step_x, step_y):
    nx = lax.axis_size("gx")
    ny = lax.axis_size("gy")
    pairs = []
    for a in range(nx):
        for b in range(ny):
            pairs.append((a * ny + b, ((a + step_x) % nx) * ny + (b + step_y) % ny))
    return pairs


def sine_table(length):
    series = jnp.arange(length, dtype=jnp.int32) + 1
    product = series[:, None] * series[None, :] % (2 * (length + 1))
    return jnp.sin(product.astype(jnp.float32) * (math.pi / (length + 1)))


def fourier_pair(length):
    series = jnp.arange(length, dtype=jnp.int32)
    product = series[:, None] * series[None, :] % length
    angles = product.astype(jnp.float32) * (2.0 * math.pi / length)
    return jnp.stack([jnp.cos(angles), -jnp.sin(angles)])


def wall_eigen(first, number, total):
    modes = (jnp.arange(number, dtype=jnp.int32) + first + 1).astype(jnp.float32)
    return 2.0 - 2.0 * jnp.cos(modes * (math.pi / (total + 1)))


def cycle_angles(first, number, total):
    modes = jnp.arange(number, dtype=jnp.int32) + first
    return modes.astype(jnp.float32) * (2.0 * math.pi / total)


def solve_potential(charge):
    len_local, wid_local, depth = charge.shape
    len_parts = lax.axis_size("gx")
    wid_parts = lax.axis_size("gy")
    devices = len_parts * wid_parts
    modes_local = depth // devices
    full_len = len_local * len_parts
    full_wid = wid_local * wid_parts
    me = lax.axis_index("gx") * wid_parts + lax.axis_index("gy")
    depth_sine = sine_table(depth)
    flat = charge.reshape(len_local * wid_local, depth)
    sectioned = jnp.einsum("pz,nz->np", flat, depth_sine, precision=SOLVE)
    chunk = modes_local * len_local * wid_local
    sectioned = sectioned.reshape(devices, chunk // 128, 128)
    plane = lax.all_to_all(sectioned, ("gx", "gy"), 0, 0, tiled=True)
    plane = plane.reshape(len_parts, wid_parts, modes_local, len_local, wid_local)
    pair = fourier_pair(full_len).reshape(2, full_len, len_parts, len_local)
    spectra = jnp.einsum("rkax,abnxy->rknby", pair, plane, precision=SOLVE)
    spectra = spectra.reshape(2, full_len, modes_local, full_wid)
    wid_sine = sine_table(full_wid)
    spectra = jnp.einsum("my,rkny->rknm", wid_sine, spectra, precision=SOLVE)
    angles = cycle_angles(0, full_len, full_len)
    denom = (
        SCREENING
        + (2.0 - 2.0 * jnp.cos(angles))[:, None, None]
        + wall_eigen(me * modes_local, modes_local, depth)[None, :, None]
        + wall_eigen(0, full_wid, full_wid)[None, None, :]
    )
    spectra = spectra / denom[None]
    level = jnp.einsum("ym,rknm->rkny", wid_sine, spectra, precision=SOLVE) * (
        2.0 / (full_wid + 1)
    )
    plane = jnp.einsum("rkX,rknY->nXY", fourier_pair(full_len), level, precision=SOLVE) * (
        1.0 / full_len
    )
    plane = jnp.concatenate([plane[:, -1:], plane, plane[:, :1]], axis=1)
    plane = jnp.pad(plane, ((0, 0), (0, 0), (1, 1)))
    blocks = jnp.stack(
        [
            plane[:, a * len_local : a * len_local + len_local + 2, b * wid_local : b * wid_local + wid_local + 2]
            for a in range(len_parts)
            for b in range(wid_parts)
        ]
    )
    back = lax.all_to_all(blocks, ("gx", "gy"), 0, 0, tiled=True)
    back = back.reshape(depth, len_local + 2, wid_local + 2)
    return jnp.einsum("nz,nxy->xyz", depth_sine, back, precision=SOLVE) * (2.0 / (depth + 1))


def signed_sum(terms):
    total = None
    for sign, value in terms:
        if total is None:
            total = value if sign > 0 else -value
        else:
            total = total + value if sign > 0 else total - value
    return total


def collide(populations, distribution_tuple, volumetric_push):
    density = populations[0]
    for entry in range(1, 19):
        density = density + populations[entry]
    inverse = 1.0 / density
    velocity = []
    for component in range(3):
        moment = signed_sum(
            [(LATTICE_VELOCITY[e][component], populations[e]) for e in range(19) if LATTICE_VELOCITY[e][component] != 0]
        )
        velocity.append((moment + 0.5 * volumetric_push[component]) * inverse)
    speed_sq = velocity[0] * velocity[0] + velocity[1] * velocity[1] + velocity[2] * velocity[2]
    power = (
        velocity[0] * volumetric_push[0]
        + velocity[1] * volumetric_push[1]
        + velocity[2] * volumetric_push[2]
    )
    base = density * (1.0 - 1.5 * speed_sq)
    power3 = 3.0 * power
    keep = 1.0 - 1.0 / RELAXATION
    fluid = distribution_tuple > 0.5
    posts = []
    for entry in range(19):
        along = LATTICE_VELOCITY[entry]
        weight = WEIGHTS[entry]
        if entry == 0:
            equil = base
            source = -power3
        else:
            proj_vel = signed_sum([(along[c], velocity[c]) for c in range(3) if along[c] != 0])
            proj_force = signed_sum([(along[c], volumetric_push[c]) for c in range(3) if along[c] != 0])
            equil = base + density * proj_vel * (3.0 + 4.5 * proj_vel)
            source = proj_force * (3.0 + 9.0 * proj_vel) - power3
        moved = (
            keep * populations[entry]
            + (weight / RELAXATION) * equil
            + ((1.0 - 0.5 / RELAXATION) * weight) * source
        )
        posts.append(jnp.where(fluid, moved, populations[OPPOSITE[entry]]))
    return (posts, velocity)


def stream_kernel(pop_ref, fluid_ref, push_ref, out_ref, vel_ref, cols_ref):
    rows = pop_ref.shape[1]
    len_local, wid_local, depth = out_ref.shape[1:]
    for row in range(rows):
        pops = [pop_ref[entry, row] for entry in range(19)]
        push = [push_ref[component, row] for component in range(3)]
        posts, velocity = collide(pops, fluid_ref[row], push)
        here = pl.program_id(0) * rows + row
        for entry in range(19):
            cx, cy, cz = LATTICE_VELOCITY[entry]
            moved = posts[entry]
            if cy != 0:
                moved = pltpu.roll(moved, cy % wid_local, 0)
            if cz != 0:
                moved = pltpu.roll(moved, cz % depth, 1)
            target = (here + cx + len_local) % len_local
            out_ref[entry, target] = moved
            if cy != 0:
                at = 0 if cy == 1 else wid_local - 1
                cols_ref[CROSS_Y.index(entry), target] = moved[at : at + 1]
        for component in range(3):
            vel_ref[component, row] = velocity[component]


def stream_call(populations, distribution_tuple, push):
    entries, len_local, wid_local, depth = populations.shape
    rows = 2
    big = lambda n: pl.BlockSpec((n, rows, wid_local, depth), lambda i: (0, i, 0, 0))
    return pl.pallas_call(
        stream_kernel,
        grid=(len_local // rows,),
        in_specs=[big(entries), pl.BlockSpec((rows, wid_local, depth), lambda i: (i, 0, 0)), big(3)],
        out_specs=[
            pl.BlockSpec(populations.shape, lambda i: (0, 0, 0, 0)),
            big(3),
            pl.BlockSpec((len(CROSS_Y), len_local, 1, depth), lambda i: (0, 0, 0, 0)),
        ],
        out_shape=[
            jax.ShapeDtypeStruct(populations.shape, jnp.float32),
            jax.ShapeDtypeStruct((3, len_local, wid_local, depth), jnp.float32),
            jax.ShapeDtypeStruct((len(CROSS_Y), len_local, 1, depth), jnp.float32),
        ],
        compiler_params=pltpu.CompilerParams(vmem_limit_bytes=48 * 1024 * 1024),
    )(populations, distribution_tuple, push)


def patch_kernel(rows_ref, cols_ref, wrapped_hbm, out_hbm, sems):
    del wrapped_hbm
    len_local, wid_local = out_hbm.shape[1:3]
    first = []
    for k, entry in enumerate(CROSS_X):
        at = 0 if LATTICE_VELOCITY[entry][0] == 1 else len_local - 1
        first.append(pltpu.make_async_copy(rows_ref.at[k], out_hbm.at[entry, pl.ds(at, 1)], sems.at[k]))
    for copy in first:
        copy.start()
    for copy in first:
        copy.wait()
    second = []
    for k, entry in enumerate(CROSS_Y):
        at = 0 if LATTICE_VELOCITY[entry][1] == 1 else wid_local - 1
        second.append(
            pltpu.make_async_copy(
                cols_ref.at[k], out_hbm.at[entry, :, pl.ds(at, 1)], sems.at[len(first) + k]
            )
        )
    for copy in second:
        copy.start()
    for copy in second:
        copy.wait()


def patch_call(rows, cols, wrapped):
    vmem = pl.BlockSpec(memory_space=pltpu.VMEM)
    return pl.pallas_call(
        patch_kernel,
        in_specs=[vmem, vmem, pl.BlockSpec(memory_space=pl.ANY)],
        out_specs=pl.BlockSpec(memory_space=pl.ANY),
        out_shape=jax.ShapeDtypeStruct(wrapped.shape, wrapped.dtype),
        scratch_shapes=[pltpu.SemaphoreType.DMA((len(CROSS_X) + len(CROSS_Y),))],
        input_output_aliases={2: 0},
    )(rows, cols, wrapped)


def drift_diffuse(
    conc,
    neighbour_cells,
    distribution_tuple,
    velocity,
    gradient_of_voltage,
    potential,
    free_electrostatic_share,
):
    laplace = -6.0 * conc
    drift = conc * (SCREENING * potential - free_electrostatic_share)[None]
    advect = jnp.zeros_like(conc)
    for component in range(3):
        upper, lower = neighbour_cells[component]
        up_val = upper[2:3] * upper[:2] + (1.0 - upper[2:3]) * conc
        low_val = lower[2:3] * lower[:2] + (1.0 - lower[2:3]) * conc
        laplace = laplace + up_val + low_val
        slope = 0.5 * (up_val - low_val)
        drift = drift - slope * gradient_of_voltage[component][None]
        advect = advect + slope * velocity[component][None]
    valence = jnp.asarray([1.0, -1.0], jnp.float32)[:, None, None, None]
    change = DIFFUSIVITY * (laplace + valence * drift) - advect
    return conc + distribution_tuple[None] * change


def shift_x(block, low, high, step, dim):
    if step == 1:
        return jnp.concatenate([low, lax.slice_in_dim(block, 0, block.shape[dim] - 1, axis=dim)], dim)
    if step == -1:
        return jnp.concatenate([lax.slice_in_dim(block, 1, None, axis=dim), high], dim)
    return block


def body(populations, ions, mask):
    len_local, wid_local, depth = mask.shape
    wid_parts = lax.axis_size("gy")
    wid_index = lax.axis_index("gy")
    distribution_tuple = (mask == 0).astype(jnp.float32)
    ionic = jnp.concatenate([ions, distribution_tuple[None]], axis=0)
    ionic_x = halos(ionic, "gx", 1)
    ionic_y = halos(ionic, "gy", 2)
    free_electrostatic_share = (
        distribution_tuple * (ions[0] - ions[1]) + (1.0 - distribution_tuple) * WALL_CHARGE
    )
    extended = solve_potential(free_electrostatic_share)
    potential = extended[1:-1, 1:-1]
    field_len = FIELD_EXT - 0.5 * (extended[2:, 1:-1] - extended[:-2, 1:-1])
    field_wid = -0.5 * (extended[1:-1, 2:] - extended[1:-1, :-2])
    depth_pad = jnp.pad(potential, ((0, 0), (0, 0), (1, 1)))
    field_depth = -0.5 * (depth_pad[:, :, 2:] - depth_pad[:, :, :-2])
    gradient_of_voltage = [field_len, field_wid, field_depth]
    ion_concentration_sum = distribution_tuple * free_electrostatic_share
    volumetric_push = [ion_concentration_sum * voltage_grid for voltage_grid in gradient_of_voltage]
    push = jnp.stack(volumetric_push)
    wrapped, velocity, edge_cols = stream_call(populations, distribution_tuple, push)
    velocity = [velocity[component] for component in range(3)]
    last_x = len_local - 1
    last_y = wid_local - 1
    edge_x = {1: 0, -1: last_x}
    edge_y = {1: 0, -1: last_y}
    rows = {}
    cols = {}
    for step in (1, -1):
        group = [e for e in range(19) if LATTICE_VELOCITY[e][0] == step]
        sent = jnp.stack([wrapped[e, edge_x[step]] for e in group])
        got = lax.ppermute(sent, "gx", ring("gx", step))
        rows.update({e: got[k] for k, e in enumerate(group)})
    for step in (1, -1):
        group = [e for e in range(19) if LATTICE_VELOCITY[e][1] == step]
        pieces = []
        for e in group:
            column = edge_cols[CROSS_Y.index(e)]
            cx = LATTICE_VELOCITY[e][0]
            if cx != 0:
                cell = rows[e][edge_y[step]][None, None]
                if edge_x[cx] == 0:
                    column = jnp.concatenate([cell, column[1:]])
                else:
                    column = jnp.concatenate([column[:-1], cell])
            pieces.append(column)
        got = lax.ppermute(jnp.stack(pieces), "gy", ring("gy", step))
        cols.update({e: got[k] for k, e in enumerate(group)})
    populations_out = patch_call(
        jnp.stack([rows[e][None] for e in CROSS_X]),
        jnp.stack([cols[e] for e in CROSS_Y]),
        wrapped,
    )

    low_ix, high_ix = ionic_x
    low_iy, high_iy = ionic_y
    neighbour_cells = [
        (shift_x(ionic, None, high_ix, -1, 1), shift_x(ionic, low_ix, None, 1, 1)),
        (shift_x(ionic, None, high_iy, -1, 2), shift_x(ionic, low_iy, None, 1, 2)),
        (jnp.roll(ionic, -1, 3), jnp.roll(ionic, 1, 3)),
    ]
    ions_out = drift_diffuse(
        ions,
        neighbour_cells,
        distribution_tuple,
        velocity,
        gradient_of_voltage,
        potential,
        free_electrostatic_share,
    )
    return (populations_out, ions_out, potential)


def solution(mesh):
    placed = (P(None, "gx", "gy", None), P(None, "gx", "gy", None), P("gx", "gy", None))
    return jax.shard_map(
        body,
        mesh=mesh,
        in_specs=placed,
        out_specs=(P(None, "gx", "gy", None), P(None, "gx", "gy", None), P("gx", "gy", None)),
        check_vma=False,
    )
```

```python
import math

import jax
import jax.numpy as jnp
from jax import lax
from jax.experimental import pallas as pl
from jax.experimental.pallas import tpu as pltpu
from jax.sharding import PartitionSpec as P

PRECISE = lax.Precision.HIGHEST
SOLVE = lax.Precision.HIGH
LATTICE_VELOCITY = [
    (0, 0, 0),
    (1, 0, 0),
    (-1, 0, 0),
    (0, 1, 0),
    (0, -1, 0),
    (0, 0, 1),
    (0, 0, -1),
    (1, 1, 0),
    (-1, -1, 0),
    (1, -1, 0),
    (-1, 1, 0),
    (1, 0, 1),
    (-1, 0, -1),
    (1, 0, -1),
    (-1, 0, 1),
    (0, 1, 1),
    (0, -1, -1),
    (0, 1, -1),
    (0, -1, 1),
]
WEIGHTS = [1.0 / 3.0] + [1.0 / 18.0] * 6 + [1.0 / 36.0] * 12
OPPOSITE = [0, 2, 1, 4, 3, 6, 5, 8, 7, 10, 9, 12, 11, 14, 13, 16, 15, 18, 17]
RELAXATION = 0.8
SCREENING = 0.001
WALL_CHARGE = -0.1
FIELD_EXT = 0.3
DIFFUSIVITY = 0.1

PLUS_X = [i for i in range(19) if LATTICE_VELOCITY[i][0] == 1]
MINUS_X = [i for i in range(19) if LATTICE_VELOCITY[i][0] == -1]
PLUS_Y = [i for i in range(19) if LATTICE_VELOCITY[i][1] == 1]
MINUS_Y = [i for i in range(19) if LATTICE_VELOCITY[i][1] == -1]
CROSS_X = PLUS_X + MINUS_X
CROSS_Y = PLUS_Y + MINUS_Y
DIAGONAL = [7, 8, 9, 10]


def ring(axis, step):
    count = lax.axis_size(axis)
    return [(i, (i + step) % count) for i in range(count)]


def halos(block, axis, dim):
    n = block.shape[dim]
    low = lax.ppermute(lax.slice_in_dim(block, n - 1, n, axis=dim), axis, ring(axis, 1))
    high = lax.ppermute(lax.slice_in_dim(block, 0, 1, axis=dim), axis, ring(axis, -1))
    return low, high


def diagonal_pairs(step_x, step_y):
    nx = lax.axis_size("gx")
    ny = lax.axis_size("gy")
    pairs = []
    for a in range(nx):
        for b in range(ny):
            pairs.append((a * ny + b, ((a + step_x) % nx) * ny + (b + step_y) % ny))
    return pairs


def sine_table(length):
    series = jnp.arange(length, dtype=jnp.int32) + 1
    product = series[:, None] * series[None, :] % (2 * (length + 1))
    return jnp.sin(product.astype(jnp.float32) * (math.pi / (length + 1)))


def fourier_pair(length):
    series = jnp.arange(length, dtype=jnp.int32)
    product = series[:, None] * series[None, :] % length
    angles = product.astype(jnp.float32) * (2.0 * math.pi / length)
    return jnp.stack([jnp.cos(angles), -jnp.sin(angles)])


def wall_eigen(first, number, total):
    modes = (jnp.arange(number, dtype=jnp.int32) + first + 1).astype(jnp.float32)
    return 2.0 - 2.0 * jnp.cos(modes * (math.pi / (total + 1)))


def cycle_angles(first, number, total):
    modes = jnp.arange(number, dtype=jnp.int32) + first
    return modes.astype(jnp.float32) * (2.0 * math.pi / total)


def solve_potential(charge):
    len_local, wid_local, depth = charge.shape
    len_parts = lax.axis_size("gx")
    wid_parts = lax.axis_size("gy")
    devices = len_parts * wid_parts
    modes_local = depth // devices
    full_len = len_local * len_parts
    full_wid = wid_local * wid_parts
    me = lax.axis_index("gx") * wid_parts + lax.axis_index("gy")
    depth_sine = sine_table(depth)
    flat = charge.reshape(len_local * wid_local, depth)
    sectioned = jnp.einsum("pz,nz->np", flat, depth_sine, precision=SOLVE)
    chunk = modes_local * len_local * wid_local
    sectioned = sectioned.reshape(devices, chunk // 128, 128)
    plane = lax.all_to_all(sectioned, ("gx", "gy"), 0, 0, tiled=True)
    plane = plane.reshape(len_parts, wid_parts, modes_local, len_local, wid_local)
    pair = fourier_pair(full_len).reshape(2, full_len, len_parts, len_local)
    spectra = jnp.einsum("rkax,abnxy->rknby", pair, plane, precision=SOLVE)
    spectra = spectra.reshape(2, full_len, modes_local, full_wid)
    wid_sine = sine_table(full_wid)
    spectra = jnp.einsum("my,rkny->rknm", wid_sine, spectra, precision=SOLVE)
    angles = cycle_angles(0, full_len, full_len)
    denom = (
        SCREENING
        + (2.0 - 2.0 * jnp.cos(angles))[:, None, None]
        + wall_eigen(me * modes_local, modes_local, depth)[None, :, None]
        + wall_eigen(0, full_wid, full_wid)[None, None, :]
    )
    spectra = spectra / denom[None]
    level = jnp.einsum("ym,rknm->rkny", wid_sine, spectra, precision=SOLVE) * (
        2.0 / (full_wid + 1)
    )
    plane = jnp.einsum("rkX,rknY->nXY", fourier_pair(full_len), level, precision=SOLVE) * (
        1.0 / full_len
    )
    rows_ext = len_local * (len_parts + 1)
    cols_ext = wid_local * (wid_parts + 1)
    plane = jnp.concatenate([plane[:, -1:], plane, plane[:, :1]], axis=1)
    plane = jnp.pad(plane, ((0, 0), (0, rows_ext - full_len - 2), (1, cols_ext - full_wid - 1)))
    main = plane[:, :full_len].reshape(modes_local, len_parts, len_local, cols_ext)
    extra = plane[:, len_local:].reshape(modes_local, len_parts, len_local, cols_ext)[:, :, :2]
    plane = jnp.concatenate([main, extra], axis=2)
    main = plane[..., :full_wid].reshape(modes_local, len_parts, len_local + 2, wid_parts, wid_local)
    extra = plane[..., wid_local:].reshape(modes_local, len_parts, len_local + 2, wid_parts, wid_local)
    plane = jnp.concatenate([main, extra[..., :2]], axis=4)
    blocks = plane.transpose(1, 3, 0, 2, 4)
    ext = modes_local * (len_local + 2) * (wid_local + 2)
    width = -(-ext // 128) * 128
    blocks = jnp.pad(blocks.reshape(devices, ext), ((0, 0), (0, width - ext))).reshape(devices, width // 128, 128)
    back = lax.all_to_all(blocks, ("gx", "gy"), 0, 0, tiled=True)
    back = back.reshape(devices, width)[:, :ext].reshape(depth, len_local + 2, wid_local + 2)
    return jnp.einsum("nz,nxy->xyz", depth_sine, back, precision=SOLVE) * (2.0 / (depth + 1))


def signed_sum(terms):
    total = None
    for sign, value in terms:
        if total is None:
            total = value if sign > 0 else -value
        else:
            total = total + value if sign > 0 else total - value
    return total


def collide(populations, distribution_tuple, volumetric_push):
    density = populations[0]
    for entry in range(1, 19):
        density = density + populations[entry]
    inverse = 1.0 / density
    velocity = []
    for component in range(3):
        moment = signed_sum(
            [(LATTICE_VELOCITY[e][component], populations[e]) for e in range(19) if LATTICE_VELOCITY[e][component] != 0]
        )
        velocity.append((moment + 0.5 * volumetric_push[component]) * inverse)
    speed_sq = velocity[0] * velocity[0] + velocity[1] * velocity[1] + velocity[2] * velocity[2]
    power = (
        velocity[0] * volumetric_push[0]
        + velocity[1] * volumetric_push[1]
        + velocity[2] * volumetric_push[2]
    )
    base = density * (1.0 - 1.5 * speed_sq)
    power3 = 3.0 * power
    keep = 1.0 - 1.0 / RELAXATION
    fluid = distribution_tuple > 0.5
    posts = []
    for entry in range(19):
        along = LATTICE_VELOCITY[entry]
        weight = WEIGHTS[entry]
        if entry == 0:
            equil = base
            source = -power3
        else:
            proj_vel = signed_sum([(along[c], velocity[c]) for c in range(3) if along[c] != 0])
            proj_force = signed_sum([(along[c], volumetric_push[c]) for c in range(3) if along[c] != 0])
            equil = base + density * proj_vel * (3.0 + 4.5 * proj_vel)
            source = proj_force * (3.0 + 9.0 * proj_vel) - power3
        moved = (
            keep * populations[entry]
            + (weight / RELAXATION) * equil
            + ((1.0 - 0.5 / RELAXATION) * weight) * source
        )
        posts.append(jnp.where(fluid, moved, populations[OPPOSITE[entry]]))
    return (posts, velocity)


def stream_kernel(pop_ref, fluid_ref, push_ref, out_ref, vel_ref, cols_ref):
    rows = pop_ref.shape[1]
    len_local, wid_local, depth = out_ref.shape[1:]
    for row in range(rows):
        pops = [pop_ref[entry, row] for entry in range(19)]
        push = [push_ref[component, row] for component in range(3)]
        posts, velocity = collide(pops, fluid_ref[row], push)
        here = pl.program_id(0) * rows + row
        for entry in range(19):
            cx, cy, cz = LATTICE_VELOCITY[entry]
            moved = posts[entry]
            if cy != 0:
                moved = pltpu.roll(moved, cy % wid_local, 0)
            if cz != 0:
                moved = pltpu.roll(moved, cz % depth, 1)
            target = (here + cx + len_local) % len_local
            out_ref[entry, target] = moved
            if cy != 0:
                at = 0 if cy == 1 else wid_local - 1
                cols_ref[CROSS_Y.index(entry), target] = moved[at : at + 1]
        for component in range(3):
            vel_ref[component, row] = velocity[component]


def stream_call(populations, distribution_tuple, push):
    entries, len_local, wid_local, depth = populations.shape
    rows = 2
    big = lambda n: pl.BlockSpec((n, rows, wid_local, depth), lambda i: (0, i, 0, 0))
    return pl.pallas_call(
        stream_kernel,
        grid=(len_local // rows,),
        in_specs=[big(entries), pl.BlockSpec((rows, wid_local, depth), lambda i: (i, 0, 0)), big(3)],
        out_specs=[
            pl.BlockSpec(populations.shape, lambda i: (0, 0, 0, 0)),
            big(3),
            pl.BlockSpec((len(CROSS_Y), len_local, 1, depth), lambda i: (0, 0, 0, 0)),
        ],
        out_shape=[
            jax.ShapeDtypeStruct(populations.shape, jnp.float32),
            jax.ShapeDtypeStruct((3, len_local, wid_local, depth), jnp.float32),
            jax.ShapeDtypeStruct((len(CROSS_Y), len_local, 1, depth), jnp.float32),
        ],
        compiler_params=pltpu.CompilerParams(vmem_limit_bytes=48 * 1024 * 1024),
    )(populations, distribution_tuple, push)


def patch_kernel(rows_ref, cols_ref, wrapped_hbm, out_hbm, sems):
    del wrapped_hbm
    len_local, wid_local = out_hbm.shape[1:3]
    first = []
    for k, entry in enumerate(CROSS_X):
        at = 0 if LATTICE_VELOCITY[entry][0] == 1 else len_local - 1
        first.append(pltpu.make_async_copy(rows_ref.at[k], out_hbm.at[entry, pl.ds(at, 1)], sems.at[k]))
    for copy in first:
        copy.start()
    for copy in first:
        copy.wait()
    second = []
    for k, entry in enumerate(CROSS_Y):
        at = 0 if LATTICE_VELOCITY[entry][1] == 1 else wid_local - 1
        second.append(
            pltpu.make_async_copy(
                cols_ref.at[k], out_hbm.at[entry, :, pl.ds(at, 1)], sems.at[len(first) + k]
            )
        )
    for copy in second:
        copy.start()
    for copy in second:
        copy.wait()


def patch_call(rows, cols, wrapped):
    vmem = pl.BlockSpec(memory_space=pltpu.VMEM)
    return pl.pallas_call(
        patch_kernel,
        in_specs=[vmem, vmem, pl.BlockSpec(memory_space=pl.ANY)],
        out_specs=pl.BlockSpec(memory_space=pl.ANY),
        out_shape=jax.ShapeDtypeStruct(wrapped.shape, wrapped.dtype),
        scratch_shapes=[pltpu.SemaphoreType.DMA((len(CROSS_X) + len(CROSS_Y),))],
        input_output_aliases={2: 0},
    )(rows, cols, wrapped)


def drift_diffuse(
    conc,
    neighbour_cells,
    distribution_tuple,
    velocity,
    gradient_of_voltage,
    potential,
    free_electrostatic_share,
):
    laplace = -6.0 * conc
    drift = conc * (SCREENING * potential - free_electrostatic_share)[None]
    advect = jnp.zeros_like(conc)
    for component in range(3):
        upper, lower = neighbour_cells[component]
        up_val = upper[2:3] * upper[:2] + (1.0 - upper[2:3]) * conc
        low_val = lower[2:3] * lower[:2] + (1.0 - lower[2:3]) * conc
        laplace = laplace + up_val + low_val
        slope = 0.5 * (up_val - low_val)
        drift = drift - slope * gradient_of_voltage[component][None]
        advect = advect + slope * velocity[component][None]
    valence = jnp.asarray([1.0, -1.0], jnp.float32)[:, None, None, None]
    change = DIFFUSIVITY * (laplace + valence * drift) - advect
    return conc + distribution_tuple[None] * change


def shift_x(block, low, high, step, dim):
    if step == 1:
        return jnp.concatenate([low, lax.slice_in_dim(block, 0, block.shape[dim] - 1, axis=dim)], dim)
    if step == -1:
        return jnp.concatenate([lax.slice_in_dim(block, 1, None, axis=dim), high], dim)
    return block


def body(populations, ions, mask):
    len_local, wid_local, depth = mask.shape
    wid_parts = lax.axis_size("gy")
    wid_index = lax.axis_index("gy")
    distribution_tuple = (mask == 0).astype(jnp.float32)
    ionic = jnp.concatenate([ions, distribution_tuple[None]], axis=0)
    ionic_x = halos(ionic, "gx", 1)
    ionic_y = halos(ionic, "gy", 2)
    free_electrostatic_share = (
        distribution_tuple * (ions[0] - ions[1]) + (1.0 - distribution_tuple) * WALL_CHARGE
    )
    extended = solve_potential(free_electrostatic_share)
    potential = extended[1:-1, 1:-1]
    field_len = FIELD_EXT - 0.5 * (extended[2:, 1:-1] - extended[:-2, 1:-1])
    field_wid = -0.5 * (extended[1:-1, 2:] - extended[1:-1, :-2])
    depth_pad = jnp.pad(potential, ((0, 0), (0, 0), (1, 1)))
    field_depth = -0.5 * (depth_pad[:, :, 2:] - depth_pad[:, :, :-2])
    gradient_of_voltage = [field_len, field_wid, field_depth]
    ion_concentration_sum = distribution_tuple * free_electrostatic_share
    volumetric_push = [ion_concentration_sum * voltage_grid for voltage_grid in gradient_of_voltage]
    push = jnp.stack(volumetric_push)
    wrapped, velocity, edge_cols = stream_call(populations, distribution_tuple, push)
    velocity = [velocity[component] for component in range(3)]
    last_x = len_local - 1
    last_y = wid_local - 1
    edge_x = {1: 0, -1: last_x}
    edge_y = {1: 0, -1: last_y}
    rows = {}
    cols = {}
    for step in (1, -1):
        group = [e for e in range(19) if LATTICE_VELOCITY[e][0] == step]
        sent = jnp.stack([wrapped[e, edge_x[step]] for e in group])
        got = lax.ppermute(sent, "gx", ring("gx", step))
        rows.update({e: got[k] for k, e in enumerate(group)})
    for step in (1, -1):
        group = [e for e in range(19) if LATTICE_VELOCITY[e][1] == step]
        pieces = []
        for e in group:
            column = edge_cols[CROSS_Y.index(e)]
            cx = LATTICE_VELOCITY[e][0]
            if cx != 0:
                cell = rows[e][edge_y[step]][None, None]
                if edge_x[cx] == 0:
                    column = jnp.concatenate([cell, column[1:]])
                else:
                    column = jnp.concatenate([column[:-1], cell])
            pieces.append(column)
        got = lax.ppermute(jnp.stack(pieces), "gy", ring("gy", step))
        cols.update({e: got[k] for k, e in enumerate(group)})
    populations_out = patch_call(
        jnp.stack([rows[e][None] for e in CROSS_X]),
        jnp.stack([cols[e] for e in CROSS_Y]),
        wrapped,
    )

    low_ix, high_ix = ionic_x
    low_iy, high_iy = ionic_y
    neighbour_cells = [
        (shift_x(ionic, None, high_ix, -1, 1), shift_x(ionic, low_ix, None, 1, 1)),
        (shift_x(ionic, None, high_iy, -1, 2), shift_x(ionic, low_iy, None, 1, 2)),
        (jnp.roll(ionic, -1, 3), jnp.roll(ionic, 1, 3)),
    ]
    ions_out = drift_diffuse(
        ions,
        neighbour_cells,
        distribution_tuple,
        velocity,
        gradient_of_voltage,
        potential,
        free_electrostatic_share,
    )
    return (populations_out, ions_out, potential)


def solution(mesh):
    placed = (P(None, "gx", "gy", None), P(None, "gx", "gy", None), P("gx", "gy", None))
    return jax.shard_map(
        body,
        mesh=mesh,
        in_specs=placed,
        out_specs=(P(None, "gx", "gy", None), P(None, "gx", "gy", None), P("gx", "gy", None)),
        check_vma=False,
    )
```

```python
import math

import jax
import jax.numpy as jnp
from jax import lax
from jax.experimental import pallas as pl
from jax.experimental.pallas import tpu as pltpu
from jax.sharding import PartitionSpec as P

PRECISE = lax.Precision.HIGHEST
SOLVE = lax.Precision.HIGH
LATTICE_VELOCITY = [
    (0, 0, 0),
    (1, 0, 0),
    (-1, 0, 0),
    (0, 1, 0),
    (0, -1, 0),
    (0, 0, 1),
    (0, 0, -1),
    (1, 1, 0),
    (-1, -1, 0),
    (1, -1, 0),
    (-1, 1, 0),
    (1, 0, 1),
    (-1, 0, -1),
    (1, 0, -1),
    (-1, 0, 1),
    (0, 1, 1),
    (0, -1, -1),
    (0, 1, -1),
    (0, -1, 1),
]
WEIGHTS = [1.0 / 3.0] + [1.0 / 18.0] * 6 + [1.0 / 36.0] * 12
OPPOSITE = [0, 2, 1, 4, 3, 6, 5, 8, 7, 10, 9, 12, 11, 14, 13, 16, 15, 18, 17]
RELAXATION = 0.8
SCREENING = 0.001
WALL_CHARGE = -0.1
FIELD_EXT = 0.3
DIFFUSIVITY = 0.1

PLUS_X = [i for i in range(19) if LATTICE_VELOCITY[i][0] == 1]
MINUS_X = [i for i in range(19) if LATTICE_VELOCITY[i][0] == -1]
PLUS_Y = [i for i in range(19) if LATTICE_VELOCITY[i][1] == 1]
MINUS_Y = [i for i in range(19) if LATTICE_VELOCITY[i][1] == -1]
CROSS_X = PLUS_X + MINUS_X
CROSS_Y = PLUS_Y + MINUS_Y
DIAGONAL = [7, 8, 9, 10]


def ring(axis, step):
    count = lax.axis_size(axis)
    return [(i, (i + step) % count) for i in range(count)]


def halos(block, axis, dim):
    n = block.shape[dim]
    low = lax.ppermute(lax.slice_in_dim(block, n - 1, n, axis=dim), axis, ring(axis, 1))
    high = lax.ppermute(lax.slice_in_dim(block, 0, 1, axis=dim), axis, ring(axis, -1))
    return low, high


def diagonal_pairs(step_x, step_y):
    nx = lax.axis_size("gx")
    ny = lax.axis_size("gy")
    pairs = []
    for a in range(nx):
        for b in range(ny):
            pairs.append((a * ny + b, ((a + step_x) % nx) * ny + (b + step_y) % ny))
    return pairs


def sine_table(length):
    series = jnp.arange(length, dtype=jnp.int32) + 1
    product = series[:, None] * series[None, :] % (2 * (length + 1))
    return jnp.sin(product.astype(jnp.float32) * (math.pi / (length + 1)))


def fourier_pair(length):
    series = jnp.arange(length, dtype=jnp.int32)
    product = series[:, None] * series[None, :] % length
    angles = product.astype(jnp.float32) * (2.0 * math.pi / length)
    return jnp.stack([jnp.cos(angles), -jnp.sin(angles)])


def wall_eigen(first, number, total):
    modes = (jnp.arange(number, dtype=jnp.int32) + first + 1).astype(jnp.float32)
    return 2.0 - 2.0 * jnp.cos(modes * (math.pi / (total + 1)))


def cycle_angles(first, number, total):
    modes = jnp.arange(number, dtype=jnp.int32) + first
    return modes.astype(jnp.float32) * (2.0 * math.pi / total)


def solve_potential(charge):
    len_local, wid_local, depth = charge.shape
    len_parts = lax.axis_size("gx")
    wid_parts = lax.axis_size("gy")
    devices = len_parts * wid_parts
    modes_local = depth // devices
    full_len = len_local * len_parts
    full_wid = wid_local * wid_parts
    me = lax.axis_index("gx") * wid_parts + lax.axis_index("gy")
    depth_sine, wid_sine, pair_full = lax.optimization_barrier(
        (sine_table(depth), sine_table(full_wid), fourier_pair(full_len))
    )
    flat = charge.reshape(len_local * wid_local, depth)
    sectioned = jnp.einsum("pz,nz->np", flat, depth_sine, precision=SOLVE)
    chunk = modes_local * len_local * wid_local
    sectioned = sectioned.reshape(devices, chunk // 128, 128)
    plane = lax.all_to_all(sectioned, ("gx", "gy"), 0, 0, tiled=True)
    plane = plane.reshape(len_parts, wid_parts, modes_local, len_local, wid_local)
    pair = pair_full.reshape(2, full_len, len_parts, len_local)
    spectra = jnp.einsum("rkax,abnxy->rknby", pair, plane, precision=SOLVE)
    spectra = spectra.reshape(2, full_len, modes_local, full_wid)
    spectra = jnp.einsum("my,rkny->rknm", wid_sine, spectra, precision=SOLVE)
    angles = cycle_angles(0, full_len, full_len)
    denom = (
        SCREENING
        + (2.0 - 2.0 * jnp.cos(angles))[:, None, None]
        + wall_eigen(me * modes_local, modes_local, depth)[None, :, None]
        + wall_eigen(0, full_wid, full_wid)[None, None, :]
    )
    spectra = spectra / denom[None]
    level = jnp.einsum("ym,rknm->rkny", wid_sine, spectra, precision=SOLVE) * (
        2.0 / (full_wid + 1)
    )
    plane = jnp.einsum("rkX,rknY->nXY", pair_full, level, precision=SOLVE) * (
        1.0 / full_len
    )
    plane = jnp.concatenate([plane[:, -1:], plane, plane[:, :1]], axis=1)
    plane = jnp.pad(plane, ((0, 0), (0, 0), (1, 1)))
    blocks = jnp.stack(
        [
            plane[:, a * len_local : a * len_local + len_local + 2, b * wid_local : b * wid_local + wid_local + 2]
            for a in range(len_parts)
            for b in range(wid_parts)
        ]
    )
    back = lax.all_to_all(blocks, ("gx", "gy"), 0, 0, tiled=True)
    back = back.reshape(depth, len_local + 2, wid_local + 2)
    return jnp.einsum("nz,nxy->xyz", depth_sine, back, precision=SOLVE) * (2.0 / (depth + 1))


def signed_sum(terms):
    total = None
    for sign, value in terms:
        if total is None:
            total = value if sign > 0 else -value
        else:
            total = total + value if sign > 0 else total - value
    return total


def collide(populations, distribution_tuple, volumetric_push):
    density = populations[0]
    for entry in range(1, 19):
        density = density + populations[entry]
    inverse = 1.0 / density
    velocity = []
    for component in range(3):
        moment = signed_sum(
            [(LATTICE_VELOCITY[e][component], populations[e]) for e in range(19) if LATTICE_VELOCITY[e][component] != 0]
        )
        velocity.append((moment + 0.5 * volumetric_push[component]) * inverse)
    speed_sq = velocity[0] * velocity[0] + velocity[1] * velocity[1] + velocity[2] * velocity[2]
    power = (
        velocity[0] * volumetric_push[0]
        + velocity[1] * volumetric_push[1]
        + velocity[2] * volumetric_push[2]
    )
    base = density * (1.0 - 1.5 * speed_sq)
    power3 = 3.0 * power
    keep = 1.0 - 1.0 / RELAXATION
    fluid = distribution_tuple > 0.5
    posts = []
    for entry in range(19):
        along = LATTICE_VELOCITY[entry]
        weight = WEIGHTS[entry]
        if entry == 0:
            equil = base
            source = -power3
        else:
            proj_vel = signed_sum([(along[c], velocity[c]) for c in range(3) if along[c] != 0])
            proj_force = signed_sum([(along[c], volumetric_push[c]) for c in range(3) if along[c] != 0])
            equil = base + density * proj_vel * (3.0 + 4.5 * proj_vel)
            source = proj_force * (3.0 + 9.0 * proj_vel) - power3
        moved = (
            keep * populations[entry]
            + (weight / RELAXATION) * equil
            + ((1.0 - 0.5 / RELAXATION) * weight) * source
        )
        posts.append(jnp.where(fluid, moved, populations[OPPOSITE[entry]]))
    return (posts, velocity)


def stream_kernel(pop_ref, fluid_ref, push_ref, out_ref, vel_ref, cols_ref):
    rows = pop_ref.shape[1]
    len_local, wid_local, depth = out_ref.shape[1:]

    def one_row(row, carry):
        pops = [pop_ref[entry, row] for entry in range(19)]
        push = [push_ref[component, row] for component in range(3)]
        posts, velocity = collide(pops, fluid_ref[row], push)
        here = pl.program_id(0) * rows + row
        for entry in range(19):
            cx, cy, cz = LATTICE_VELOCITY[entry]
            moved = posts[entry]
            if cy != 0:
                moved = pltpu.roll(moved, cy % wid_local, 0)
            if cz != 0:
                moved = pltpu.roll(moved, cz % depth, 1)
            target = (here + cx + len_local) % len_local
            out_ref[entry, target] = moved
            if cy != 0:
                at = 0 if cy == 1 else wid_local - 1
                cols_ref[CROSS_Y.index(entry), target] = moved[at : at + 1]
        for component in range(3):
            vel_ref[component, row] = velocity[component]
        return carry

    lax.fori_loop(0, rows, one_row, 0)


def stream_call(populations, distribution_tuple, push):
    entries, len_local, wid_local, depth = populations.shape
    rows = 2
    big = lambda n: pl.BlockSpec((n, rows, wid_local, depth), lambda i: (0, i, 0, 0))
    return pl.pallas_call(
        stream_kernel,
        grid=(len_local // rows,),
        in_specs=[big(entries), pl.BlockSpec((rows, wid_local, depth), lambda i: (i, 0, 0)), big(3)],
        out_specs=[
            pl.BlockSpec(populations.shape, lambda i: (0, 0, 0, 0)),
            big(3),
            pl.BlockSpec((len(CROSS_Y), len_local, 1, depth), lambda i: (0, 0, 0, 0)),
        ],
        out_shape=[
            jax.ShapeDtypeStruct(populations.shape, jnp.float32),
            jax.ShapeDtypeStruct((3, len_local, wid_local, depth), jnp.float32),
            jax.ShapeDtypeStruct((len(CROSS_Y), len_local, 1, depth), jnp.float32),
        ],
        compiler_params=pltpu.CompilerParams(vmem_limit_bytes=48 * 1024 * 1024),
    )(populations, distribution_tuple, push)


def patch_kernel(rows_ref, cols_ref, wrapped_hbm, out_hbm, sems):
    del wrapped_hbm
    len_local, wid_local = out_hbm.shape[1:3]
    first = []
    for k, entry in enumerate(CROSS_X):
        at = 0 if LATTICE_VELOCITY[entry][0] == 1 else len_local - 1
        first.append(pltpu.make_async_copy(rows_ref.at[k], out_hbm.at[entry, pl.ds(at, 1)], sems.at[k]))
    for copy in first:
        copy.start()
    for copy in first:
        copy.wait()
    second = []
    for k, entry in enumerate(CROSS_Y):
        at = 0 if LATTICE_VELOCITY[entry][1] == 1 else wid_local - 1
        second.append(
            pltpu.make_async_copy(
                cols_ref.at[k], out_hbm.at[entry, :, pl.ds(at, 1)], sems.at[len(first) + k]
            )
        )
    for copy in second:
        copy.start()
    for copy in second:
        copy.wait()


def patch_call(rows, cols, wrapped):
    vmem = pl.BlockSpec(memory_space=pltpu.VMEM)
    return pl.pallas_call(
        patch_kernel,
        in_specs=[vmem, vmem, pl.BlockSpec(memory_space=pl.ANY)],
        out_specs=pl.BlockSpec(memory_space=pl.ANY),
        out_shape=jax.ShapeDtypeStruct(wrapped.shape, wrapped.dtype),
        scratch_shapes=[pltpu.SemaphoreType.DMA((len(CROSS_X) + len(CROSS_Y),))],
        input_output_aliases={2: 0},
    )(rows, cols, wrapped)


def drift_diffuse(
    conc,
    neighbour_cells,
    distribution_tuple,
    velocity,
    gradient_of_voltage,
    potential,
    free_electrostatic_share,
):
    laplace = -6.0 * conc
    drift = conc * (SCREENING * potential - free_electrostatic_share)[None]
    advect = jnp.zeros_like(conc)
    for component in range(3):
        upper, lower = neighbour_cells[component]
        up_val = upper[2:3] * upper[:2] + (1.0 - upper[2:3]) * conc
        low_val = lower[2:3] * lower[:2] + (1.0 - lower[2:3]) * conc
        laplace = laplace + up_val + low_val
        slope = 0.5 * (up_val - low_val)
        drift = drift - slope * gradient_of_voltage[component][None]
        advect = advect + slope * velocity[component][None]
    valence = jnp.asarray([1.0, -1.0], jnp.float32)[:, None, None, None]
    change = DIFFUSIVITY * (laplace + valence * drift) - advect
    return conc + distribution_tuple[None] * change


def shift_x(block, low, high, step, dim):
    if step == 1:
        return jnp.concatenate([low, lax.slice_in_dim(block, 0, block.shape[dim] - 1, axis=dim)], dim)
    if step == -1:
        return jnp.concatenate([lax.slice_in_dim(block, 1, None, axis=dim), high], dim)
    return block


def body(populations, ions, mask):
    len_local, wid_local, depth = mask.shape
    wid_parts = lax.axis_size("gy")
    wid_index = lax.axis_index("gy")
    distribution_tuple = (mask == 0).astype(jnp.float32)
    ionic = jnp.concatenate([ions, distribution_tuple[None]], axis=0)
    ionic_x = halos(ionic, "gx", 1)
    ionic_y = halos(ionic, "gy", 2)
    free_electrostatic_share = (
        distribution_tuple * (ions[0] - ions[1]) + (1.0 - distribution_tuple) * WALL_CHARGE
    )
    extended = solve_potential(free_electrostatic_share)
    potential = extended[1:-1, 1:-1]
    field_len = FIELD_EXT - 0.5 * (extended[2:, 1:-1] - extended[:-2, 1:-1])
    field_wid = -0.5 * (extended[1:-1, 2:] - extended[1:-1, :-2])
    depth_pad = jnp.pad(potential, ((0, 0), (0, 0), (1, 1)))
    field_depth = -0.5 * (depth_pad[:, :, 2:] - depth_pad[:, :, :-2])
    gradient_of_voltage = [field_len, field_wid, field_depth]
    ion_concentration_sum = distribution_tuple * free_electrostatic_share
    volumetric_push = [ion_concentration_sum * voltage_grid for voltage_grid in gradient_of_voltage]
    push = jnp.stack(volumetric_push)
    wrapped, velocity, edge_cols = stream_call(populations, distribution_tuple, push)
    velocity = [velocity[component] for component in range(3)]
    last_x = len_local - 1
    last_y = wid_local - 1
    edge_x = {1: 0, -1: last_x}
    edge_y = {1: 0, -1: last_y}
    rows = {}
    cols = {}
    for step in (1, -1):
        group = [e for e in range(19) if LATTICE_VELOCITY[e][0] == step]
        sent = jnp.stack([wrapped[e, edge_x[step]] for e in group])
        got = lax.ppermute(sent, "gx", ring("gx", step))
        rows.update({e: got[k] for k, e in enumerate(group)})
    for step in (1, -1):
        group = [e for e in range(19) if LATTICE_VELOCITY[e][1] == step]
        pieces = []
        for e in group:
            column = edge_cols[CROSS_Y.index(e)]
            cx = LATTICE_VELOCITY[e][0]
            if cx != 0:
                cell = rows[e][edge_y[step]][None, None]
                if edge_x[cx] == 0:
                    column = jnp.concatenate([cell, column[1:]])
                else:
                    column = jnp.concatenate([column[:-1], cell])
            pieces.append(column)
        got = lax.ppermute(jnp.stack(pieces), "gy", ring("gy", step))
        cols.update({e: got[k] for k, e in enumerate(group)})
    populations_out = patch_call(
        jnp.stack([rows[e][None] for e in CROSS_X]),
        jnp.stack([cols[e] for e in CROSS_Y]),
        wrapped,
    )

    low_ix, high_ix = ionic_x
    low_iy, high_iy = ionic_y
    neighbour_cells = [
        (shift_x(ionic, None, high_ix, -1, 1), shift_x(ionic, low_ix, None, 1, 1)),
        (shift_x(ionic, None, high_iy, -1, 2), shift_x(ionic, low_iy, None, 1, 2)),
        (jnp.roll(ionic, -1, 3), jnp.roll(ionic, 1, 3)),
    ]
    ions_out = drift_diffuse(
        ions,
        neighbour_cells,
        distribution_tuple,
        velocity,
        gradient_of_voltage,
        potential,
        free_electrostatic_share,
    )
    return (populations_out, ions_out, potential)


def solution(mesh):
    placed = (P(None, "gx", "gy", None), P(None, "gx", "gy", None), P("gx", "gy", None))
    return jax.shard_map(
        body,
        mesh=mesh,
        in_specs=placed,
        out_specs=(P(None, "gx", "gy", None), P(None, "gx", "gy", None), P("gx", "gy", None)),
        check_vma=False,
    )
```

```python
import math

import jax
import jax.numpy as jnp
from jax import lax
from jax.experimental import pallas as pl
from jax.experimental.pallas import tpu as pltpu
from jax.sharding import PartitionSpec as P

PRECISE = lax.Precision.HIGHEST
SOLVE = lax.Precision.HIGH
LATTICE_VELOCITY = [
    (0, 0, 0),
    (1, 0, 0),
    (-1, 0, 0),
    (0, 1, 0),
    (0, -1, 0),
    (0, 0, 1),
    (0, 0, -1),
    (1, 1, 0),
    (-1, -1, 0),
    (1, -1, 0),
    (-1, 1, 0),
    (1, 0, 1),
    (-1, 0, -1),
    (1, 0, -1),
    (-1, 0, 1),
    (0, 1, 1),
    (0, -1, -1),
    (0, 1, -1),
    (0, -1, 1),
]
WEIGHTS = [1.0 / 3.0] + [1.0 / 18.0] * 6 + [1.0 / 36.0] * 12
OPPOSITE = [0, 2, 1, 4, 3, 6, 5, 8, 7, 10, 9, 12, 11, 14, 13, 16, 15, 18, 17]
RELAXATION = 0.8
SCREENING = 0.001
WALL_CHARGE = -0.1
FIELD_EXT = 0.3
DIFFUSIVITY = 0.1

PLUS_X = [i for i in range(19) if LATTICE_VELOCITY[i][0] == 1]
MINUS_X = [i for i in range(19) if LATTICE_VELOCITY[i][0] == -1]
PLUS_Y = [i for i in range(19) if LATTICE_VELOCITY[i][1] == 1]
MINUS_Y = [i for i in range(19) if LATTICE_VELOCITY[i][1] == -1]
CROSS_X = PLUS_X + MINUS_X
CROSS_Y = PLUS_Y + MINUS_Y
DIAGONAL = [7, 8, 9, 10]


def ring(axis, step):
    count = lax.axis_size(axis)
    return [(i, (i + step) % count) for i in range(count)]


def halos(block, axis, dim):
    n = block.shape[dim]
    low = lax.ppermute(lax.slice_in_dim(block, n - 1, n, axis=dim), axis, ring(axis, 1))
    high = lax.ppermute(lax.slice_in_dim(block, 0, 1, axis=dim), axis, ring(axis, -1))
    return low, high


def diagonal_pairs(step_x, step_y):
    nx = lax.axis_size("gx")
    ny = lax.axis_size("gy")
    pairs = []
    for a in range(nx):
        for b in range(ny):
            pairs.append((a * ny + b, ((a + step_x) % nx) * ny + (b + step_y) % ny))
    return pairs


def sine_table(length):
    series = jnp.arange(length, dtype=jnp.int32) + 1
    product = series[:, None] * series[None, :] % (2 * (length + 1))
    return jnp.sin(product.astype(jnp.float32) * (math.pi / (length + 1)))


def fourier_pair(length):
    series = jnp.arange(length, dtype=jnp.int32)
    product = series[:, None] * series[None, :] % length
    angles = product.astype(jnp.float32) * (2.0 * math.pi / length)
    return jnp.stack([jnp.cos(angles), -jnp.sin(angles)])


def wall_eigen(first, number, total):
    modes = (jnp.arange(number, dtype=jnp.int32) + first + 1).astype(jnp.float32)
    return 2.0 - 2.0 * jnp.cos(modes * (math.pi / (total + 1)))


def cycle_angles(first, number, total):
    modes = jnp.arange(number, dtype=jnp.int32) + first
    return modes.astype(jnp.float32) * (2.0 * math.pi / total)


def solve_potential(charge):
    len_local, wid_local, depth = charge.shape
    len_parts = lax.axis_size("gx")
    wid_parts = lax.axis_size("gy")
    devices = len_parts * wid_parts
    modes_local = depth // devices
    full_len = len_local * len_parts
    full_wid = wid_local * wid_parts
    me = lax.axis_index("gx") * wid_parts + lax.axis_index("gy")
    depth_sine = lax.optimization_barrier(sine_table(depth))
    wid_sine, pair_full = lax.optimization_barrier((sine_table(full_wid), fourier_pair(full_len)))
    flat = charge.reshape(len_local * wid_local, depth)
    sectioned = jnp.einsum("pz,nz->np", flat, depth_sine, precision=SOLVE)
    chunk = modes_local * len_local * wid_local
    sectioned = sectioned.reshape(devices, chunk // 128, 128)
    plane = lax.all_to_all(sectioned, ("gx", "gy"), 0, 0, tiled=True)
    plane = plane.reshape(len_parts, wid_parts, modes_local, len_local, wid_local)
    pair = pair_full.reshape(2, full_len, len_parts, len_local)
    spectra = jnp.einsum("rkax,abnxy->rknby", pair, plane, precision=SOLVE)
    spectra = spectra.reshape(2, full_len, modes_local, full_wid)
    spectra = jnp.einsum("my,rkny->rknm", wid_sine, spectra, precision=SOLVE)
    angles = cycle_angles(0, full_len, full_len)
    denom = (
        SCREENING
        + (2.0 - 2.0 * jnp.cos(angles))[:, None, None]
        + wall_eigen(me * modes_local, modes_local, depth)[None, :, None]
        + wall_eigen(0, full_wid, full_wid)[None, None, :]
    )
    spectra = spectra / denom[None]
    level = jnp.einsum("ym,rknm->rkny", wid_sine, spectra, precision=SOLVE) * (
        2.0 / (full_wid + 1)
    )
    plane = jnp.einsum("rkX,rknY->nXY", pair_full, level, precision=SOLVE) * (
        1.0 / full_len
    )
    plane = jnp.concatenate([plane[:, -1:], plane, plane[:, :1]], axis=1)
    plane = jnp.pad(plane, ((0, 0), (0, 0), (1, 1)))
    blocks = jnp.stack(
        [
            plane[:, a * len_local : a * len_local + len_local + 2, b * wid_local : b * wid_local + wid_local + 2]
            for a in range(len_parts)
            for b in range(wid_parts)
        ]
    )
    back = lax.all_to_all(blocks, ("gx", "gy"), 0, 0, tiled=True)
    back = back.reshape(depth, len_local + 2, wid_local + 2)
    return jnp.einsum("nz,nxy->xyz", depth_sine, back, precision=SOLVE) * (2.0 / (depth + 1))


def signed_sum(terms):
    total = None
    for sign, value in terms:
        if total is None:
            total = value if sign > 0 else -value
        else:
            total = total + value if sign > 0 else total - value
    return total


def collide(populations, distribution_tuple, volumetric_push):
    density = populations[0]
    for entry in range(1, 19):
        density = density + populations[entry]
    inverse = 1.0 / density
    velocity = []
    for component in range(3):
        moment = signed_sum(
            [(LATTICE_VELOCITY[e][component], populations[e]) for e in range(19) if LATTICE_VELOCITY[e][component] != 0]
        )
        velocity.append((moment + 0.5 * volumetric_push[component]) * inverse)
    speed_sq = velocity[0] * velocity[0] + velocity[1] * velocity[1] + velocity[2] * velocity[2]
    power = (
        velocity[0] * volumetric_push[0]
        + velocity[1] * volumetric_push[1]
        + velocity[2] * volumetric_push[2]
    )
    base = density * (1.0 - 1.5 * speed_sq)
    power3 = 3.0 * power
    keep = 1.0 - 1.0 / RELAXATION
    fluid = distribution_tuple > 0.5
    posts = []
    for entry in range(19):
        along = LATTICE_VELOCITY[entry]
        weight = WEIGHTS[entry]
        if entry == 0:
            equil = base
            source = -power3
        else:
            proj_vel = signed_sum([(along[c], velocity[c]) for c in range(3) if along[c] != 0])
            proj_force = signed_sum([(along[c], volumetric_push[c]) for c in range(3) if along[c] != 0])
            equil = base + density * proj_vel * (3.0 + 4.5 * proj_vel)
            source = proj_force * (3.0 + 9.0 * proj_vel) - power3
        moved = (
            keep * populations[entry]
            + (weight / RELAXATION) * equil
            + ((1.0 - 0.5 / RELAXATION) * weight) * source
        )
        posts.append(jnp.where(fluid, moved, populations[OPPOSITE[entry]]))
    return (posts, velocity)


def stream_kernel(pop_ref, fluid_ref, push_ref, out_ref, vel_ref, cols_ref):
    rows = pop_ref.shape[1]
    len_local, wid_local, depth = out_ref.shape[1:]

    def one_row(row, carry):
        pops = [pop_ref[entry, row] for entry in range(19)]
        push = [push_ref[component, row] for component in range(3)]
        posts, velocity = collide(pops, fluid_ref[row], push)
        here = pl.program_id(0) * rows + row
        for entry in range(19):
            cx, cy, cz = LATTICE_VELOCITY[entry]
            moved = posts[entry]
            if cy != 0:
                moved = pltpu.roll(moved, cy % wid_local, 0)
            if cz != 0:
                moved = pltpu.roll(moved, cz % depth, 1)
            target = (here + cx + len_local) % len_local
            out_ref[entry, target] = moved
            if cy != 0:
                at = 0 if cy == 1 else wid_local - 1
                cols_ref[CROSS_Y.index(entry), target] = moved[at : at + 1]
        for component in range(3):
            vel_ref[component, row] = velocity[component]
        return carry

    lax.fori_loop(0, rows, one_row, 0)


def stream_call(populations, distribution_tuple, push):
    entries, len_local, wid_local, depth = populations.shape
    rows = 2
    big = lambda n: pl.BlockSpec((n, rows, wid_local, depth), lambda i: (0, i, 0, 0))
    return pl.pallas_call(
        stream_kernel,
        grid=(len_local // rows,),
        in_specs=[big(entries), pl.BlockSpec((rows, wid_local, depth), lambda i: (i, 0, 0)), big(3)],
        out_specs=[
            pl.BlockSpec(populations.shape, lambda i: (0, 0, 0, 0)),
            big(3),
            pl.BlockSpec((len(CROSS_Y), len_local, 1, depth), lambda i: (0, 0, 0, 0)),
        ],
        out_shape=[
            jax.ShapeDtypeStruct(populations.shape, jnp.float32),
            jax.ShapeDtypeStruct((3, len_local, wid_local, depth), jnp.float32),
            jax.ShapeDtypeStruct((len(CROSS_Y), len_local, 1, depth), jnp.float32),
        ],
        compiler_params=pltpu.CompilerParams(vmem_limit_bytes=48 * 1024 * 1024),
    )(populations, distribution_tuple, push)


def patch_kernel(rows_ref, cols_ref, wrapped_hbm, out_hbm, sems):
    del wrapped_hbm
    len_local, wid_local = out_hbm.shape[1:3]
    first = []
    for k, entry in enumerate(CROSS_X):
        at = 0 if LATTICE_VELOCITY[entry][0] == 1 else len_local - 1
        first.append(pltpu.make_async_copy(rows_ref.at[k], out_hbm.at[entry, pl.ds(at, 1)], sems.at[k]))
    for copy in first:
        copy.start()
    for copy in first:
        copy.wait()
    second = []
    for k, entry in enumerate(CROSS_Y):
        at = 0 if LATTICE_VELOCITY[entry][1] == 1 else wid_local - 1
        second.append(
            pltpu.make_async_copy(
                cols_ref.at[k], out_hbm.at[entry, :, pl.ds(at, 1)], sems.at[len(first) + k]
            )
        )
    for copy in second:
        copy.start()
    for copy in second:
        copy.wait()


def patch_call(rows, cols, wrapped):
    vmem = pl.BlockSpec(memory_space=pltpu.VMEM)
    return pl.pallas_call(
        patch_kernel,
        in_specs=[vmem, vmem, pl.BlockSpec(memory_space=pl.ANY)],
        out_specs=pl.BlockSpec(memory_space=pl.ANY),
        out_shape=jax.ShapeDtypeStruct(wrapped.shape, wrapped.dtype),
        scratch_shapes=[pltpu.SemaphoreType.DMA((len(CROSS_X) + len(CROSS_Y),))],
        input_output_aliases={2: 0},
    )(rows, cols, wrapped)


def drift_diffuse(
    conc,
    neighbour_cells,
    distribution_tuple,
    velocity,
    gradient_of_voltage,
    potential,
    free_electrostatic_share,
):
    laplace = -6.0 * conc
    drift = conc * (SCREENING * potential - free_electrostatic_share)[None]
    advect = jnp.zeros_like(conc)
    for component in range(3):
        upper, lower = neighbour_cells[component]
        up_val = upper[2:3] * upper[:2] + (1.0 - upper[2:3]) * conc
        low_val = lower[2:3] * lower[:2] + (1.0 - lower[2:3]) * conc
        laplace = laplace + up_val + low_val
        slope = 0.5 * (up_val - low_val)
        drift = drift - slope * gradient_of_voltage[component][None]
        advect = advect + slope * velocity[component][None]
    valence = jnp.asarray([1.0, -1.0], jnp.float32)[:, None, None, None]
    change = DIFFUSIVITY * (laplace + valence * drift) - advect
    return conc + distribution_tuple[None] * change


def shift_x(block, low, high, step, dim):
    if step == 1:
        return jnp.concatenate([low, lax.slice_in_dim(block, 0, block.shape[dim] - 1, axis=dim)], dim)
    if step == -1:
        return jnp.concatenate([lax.slice_in_dim(block, 1, None, axis=dim), high], dim)
    return block


def body(populations, ions, mask):
    len_local, wid_local, depth = mask.shape
    wid_parts = lax.axis_size("gy")
    wid_index = lax.axis_index("gy")
    distribution_tuple = (mask == 0).astype(jnp.float32)
    ionic = jnp.concatenate([ions, distribution_tuple[None]], axis=0)
    ionic_x = halos(ionic, "gx", 1)
    ionic_y = halos(ionic, "gy", 2)
    free_electrostatic_share = (
        distribution_tuple * (ions[0] - ions[1]) + (1.0 - distribution_tuple) * WALL_CHARGE
    )
    extended = solve_potential(free_electrostatic_share)
    potential = extended[1:-1, 1:-1]
    field_len = FIELD_EXT - 0.5 * (extended[2:, 1:-1] - extended[:-2, 1:-1])
    field_wid = -0.5 * (extended[1:-1, 2:] - extended[1:-1, :-2])
    depth_pad = jnp.pad(potential, ((0, 0), (0, 0), (1, 1)))
    field_depth = -0.5 * (depth_pad[:, :, 2:] - depth_pad[:, :, :-2])
    gradient_of_voltage = [field_len, field_wid, field_depth]
    ion_concentration_sum = distribution_tuple * free_electrostatic_share
    volumetric_push = [ion_concentration_sum * voltage_grid for voltage_grid in gradient_of_voltage]
    push = jnp.stack(volumetric_push)
    wrapped, velocity, edge_cols = stream_call(populations, distribution_tuple, push)
    velocity = [velocity[component] for component in range(3)]
    last_x = len_local - 1
    last_y = wid_local - 1
    edge_x = {1: 0, -1: last_x}
    edge_y = {1: 0, -1: last_y}
    rows = {}
    cols = {}
    for step in (1, -1):
        group = [e for e in range(19) if LATTICE_VELOCITY[e][0] == step]
        sent = jnp.stack([wrapped[e, edge_x[step]] for e in group])
        got = lax.ppermute(sent, "gx", ring("gx", step))
        rows.update({e: got[k] for k, e in enumerate(group)})
    for step in (1, -1):
        group = [e for e in range(19) if LATTICE_VELOCITY[e][1] == step]
        pieces = []
        for e in group:
            column = edge_cols[CROSS_Y.index(e)]
            cx = LATTICE_VELOCITY[e][0]
            if cx != 0:
                cell = rows[e][edge_y[step]][None, None]
                if edge_x[cx] == 0:
                    column = jnp.concatenate([cell, column[1:]])
                else:
                    column = jnp.concatenate([column[:-1], cell])
            pieces.append(column)
        got = lax.ppermute(jnp.stack(pieces), "gy", ring("gy", step))
        cols.update({e: got[k] for k, e in enumerate(group)})
    populations_out = patch_call(
        jnp.stack([rows[e][None] for e in CROSS_X]),
        jnp.stack([cols[e] for e in CROSS_Y]),
        wrapped,
    )

    low_ix, high_ix = ionic_x
    low_iy, high_iy = ionic_y
    neighbour_cells = [
        (shift_x(ionic, None, high_ix, -1, 1), shift_x(ionic, low_ix, None, 1, 1)),
        (shift_x(ionic, None, high_iy, -1, 2), shift_x(ionic, low_iy, None, 1, 2)),
        (jnp.roll(ionic, -1, 3), jnp.roll(ionic, 1, 3)),
    ]
    ions_out = drift_diffuse(
        ions,
        neighbour_cells,
        distribution_tuple,
        velocity,
        gradient_of_voltage,
        potential,
        free_electrostatic_share,
    )
    return (populations_out, ions_out, potential)


def solution(mesh):
    placed = (P(None, "gx", "gy", None), P(None, "gx", "gy", None), P("gx", "gy", None))
    return jax.shard_map(
        body,
        mesh=mesh,
        in_specs=placed,
        out_specs=(P(None, "gx", "gy", None), P(None, "gx", "gy", None), P("gx", "gy", None)),
        check_vma=False,
    )
```

```python
import math

import jax
import jax.numpy as jnp
from jax import lax
from jax.experimental import pallas as pl
from jax.experimental.pallas import tpu as pltpu
from jax.sharding import PartitionSpec as P

PRECISE = lax.Precision.HIGHEST
SOLVE = lax.Precision.HIGH
LATTICE_VELOCITY = [
    (0, 0, 0),
    (1, 0, 0),
    (-1, 0, 0),
    (0, 1, 0),
    (0, -1, 0),
    (0, 0, 1),
    (0, 0, -1),
    (1, 1, 0),
    (-1, -1, 0),
    (1, -1, 0),
    (-1, 1, 0),
    (1, 0, 1),
    (-1, 0, -1),
    (1, 0, -1),
    (-1, 0, 1),
    (0, 1, 1),
    (0, -1, -1),
    (0, 1, -1),
    (0, -1, 1),
]
WEIGHTS = [1.0 / 3.0] + [1.0 / 18.0] * 6 + [1.0 / 36.0] * 12
OPPOSITE = [0, 2, 1, 4, 3, 6, 5, 8, 7, 10, 9, 12, 11, 14, 13, 16, 15, 18, 17]
RELAXATION = 0.8
SCREENING = 0.001
WALL_CHARGE = -0.1
FIELD_EXT = 0.3
DIFFUSIVITY = 0.1

PLUS_X = [i for i in range(19) if LATTICE_VELOCITY[i][0] == 1]
MINUS_X = [i for i in range(19) if LATTICE_VELOCITY[i][0] == -1]
PLUS_Y = [i for i in range(19) if LATTICE_VELOCITY[i][1] == 1]
MINUS_Y = [i for i in range(19) if LATTICE_VELOCITY[i][1] == -1]
CROSS_X = PLUS_X + MINUS_X
CROSS_Y = PLUS_Y + MINUS_Y
DIAGONAL = [7, 8, 9, 10]


def ring(axis, step):
    count = lax.axis_size(axis)
    return [(i, (i + step) % count) for i in range(count)]


def halos(block, axis, dim):
    n = block.shape[dim]
    low = lax.ppermute(lax.slice_in_dim(block, n - 1, n, axis=dim), axis, ring(axis, 1))
    high = lax.ppermute(lax.slice_in_dim(block, 0, 1, axis=dim), axis, ring(axis, -1))
    return low, high


def diagonal_pairs(step_x, step_y):
    nx = lax.axis_size("gx")
    ny = lax.axis_size("gy")
    pairs = []
    for a in range(nx):
        for b in range(ny):
            pairs.append((a * ny + b, ((a + step_x) % nx) * ny + (b + step_y) % ny))
    return pairs


def sine_table(length):
    series = jnp.arange(length, dtype=jnp.int32) + 1
    product = series[:, None] * series[None, :] % (2 * (length + 1))
    return jnp.sin(product.astype(jnp.float32) * (math.pi / (length + 1)))


def fourier_pair(length):
    series = jnp.arange(length, dtype=jnp.int32)
    product = series[:, None] * series[None, :] % length
    angles = product.astype(jnp.float32) * (2.0 * math.pi / length)
    return jnp.stack([jnp.cos(angles), -jnp.sin(angles)])


def wall_eigen(first, number, total):
    modes = (jnp.arange(number, dtype=jnp.int32) + first + 1).astype(jnp.float32)
    return 2.0 - 2.0 * jnp.cos(modes * (math.pi / (total + 1)))


def cycle_angles(first, number, total):
    modes = jnp.arange(number, dtype=jnp.int32) + first
    return modes.astype(jnp.float32) * (2.0 * math.pi / total)


def solve_potential(charge):
    len_local, wid_local, depth = charge.shape
    len_parts = lax.axis_size("gx")
    wid_parts = lax.axis_size("gy")
    devices = len_parts * wid_parts
    modes_local = depth // devices
    full_len = len_local * len_parts
    full_wid = wid_local * wid_parts
    me = lax.axis_index("gx") * wid_parts + lax.axis_index("gy")
    depth_sine, wid_sine, pair_full = lax.optimization_barrier(
        (sine_table(depth), sine_table(full_wid), fourier_pair(full_len))
    )
    flat = charge.reshape(len_local * wid_local, depth)
    sectioned = jnp.einsum("pz,nz->np", flat, depth_sine, precision=SOLVE)
    chunk = modes_local * len_local * wid_local
    sectioned = sectioned.reshape(devices, chunk // 128, 128)
    plane = lax.all_to_all(sectioned, ("gx", "gy"), 0, 0, tiled=True)
    plane = plane.reshape(len_parts, wid_parts, modes_local, len_local, wid_local)
    pair = pair_full.reshape(2, full_len, len_parts, len_local)
    spectra = jnp.einsum("rkax,abnxy->rknby", pair, plane, precision=SOLVE)
    spectra = spectra.reshape(2, full_len, modes_local, full_wid)
    spectra = jnp.einsum("my,rkny->rknm", wid_sine, spectra, precision=SOLVE)
    angles = cycle_angles(0, full_len, full_len)
    denom = (
        SCREENING
        + (2.0 - 2.0 * jnp.cos(angles))[:, None, None]
        + wall_eigen(me * modes_local, modes_local, depth)[None, :, None]
        + wall_eigen(0, full_wid, full_wid)[None, None, :]
    )
    spectra = spectra / denom[None]
    level = jnp.einsum("ym,rknm->rkny", wid_sine, spectra, precision=SOLVE) * (
        2.0 / (full_wid + 1)
    )
    plane = jnp.einsum("rkX,rknY->nXY", pair_full, level, precision=SOLVE) * (
        1.0 / full_len
    )
    plane = jnp.concatenate([plane[:, -1:], plane, plane[:, :1]], axis=1)
    plane = jnp.pad(plane, ((0, 0), (0, 0), (1, 1)))
    blocks = jnp.stack(
        [
            plane[:, a * len_local : a * len_local + len_local + 2, b * wid_local : b * wid_local + wid_local + 2]
            for a in range(len_parts)
            for b in range(wid_parts)
        ]
    )
    back = lax.all_to_all(blocks, ("gx", "gy"), 0, 0, tiled=True)
    back = back.reshape(depth, len_local + 2, wid_local + 2)
    return jnp.einsum("nz,nxy->xyz", depth_sine, back, precision=SOLVE) * (2.0 / (depth + 1))


def signed_sum(terms):
    total = None
    for sign, value in terms:
        if total is None:
            total = value if sign > 0 else -value
        else:
            total = total + value if sign > 0 else total - value
    return total


def collide(populations, distribution_tuple, volumetric_push):
    density = populations[0]
    for entry in range(1, 19):
        density = density + populations[entry]
    inverse = 1.0 / density
    velocity = []
    for component in range(3):
        moment = signed_sum(
            [(LATTICE_VELOCITY[e][component], populations[e]) for e in range(19) if LATTICE_VELOCITY[e][component] != 0]
        )
        velocity.append((moment + 0.5 * volumetric_push[component]) * inverse)
    speed_sq = velocity[0] * velocity[0] + velocity[1] * velocity[1] + velocity[2] * velocity[2]
    power = (
        velocity[0] * volumetric_push[0]
        + velocity[1] * volumetric_push[1]
        + velocity[2] * volumetric_push[2]
    )
    base = density * (1.0 - 1.5 * speed_sq)
    power3 = 3.0 * power
    keep = 1.0 - 1.0 / RELAXATION
    fluid = distribution_tuple > 0.5
    posts = []
    for entry in range(19):
        along = LATTICE_VELOCITY[entry]
        weight = WEIGHTS[entry]
        if entry == 0:
            equil = base
            source = -power3
        else:
            proj_vel = signed_sum([(along[c], velocity[c]) for c in range(3) if along[c] != 0])
            proj_force = signed_sum([(along[c], volumetric_push[c]) for c in range(3) if along[c] != 0])
            equil = base + density * proj_vel * (3.0 + 4.5 * proj_vel)
            source = proj_force * (3.0 + 9.0 * proj_vel) - power3
        moved = (
            keep * populations[entry]
            + (weight / RELAXATION) * equil
            + ((1.0 - 0.5 / RELAXATION) * weight) * source
        )
        posts.append(jnp.where(fluid, moved, populations[OPPOSITE[entry]]))
    return (posts, velocity)


def stream_kernel(pop_ref, fluid_ref, push_ref, out_ref, vel_ref, cols_ref):
    rows = pop_ref.shape[1]
    len_local, wid_local, depth = out_ref.shape[1:]

    def one_row(row, carry):
        pops = [pop_ref[entry, row] for entry in range(19)]
        push = [push_ref[component, row] for component in range(3)]
        posts, velocity = collide(pops, fluid_ref[row], push)
        here = pl.program_id(0) * rows + row
        for entry in range(19):
            cx, cy, cz = LATTICE_VELOCITY[entry]
            moved = posts[entry]
            if cy != 0:
                moved = pltpu.roll(moved, cy % wid_local, 0)
            if cz != 0:
                moved = pltpu.roll(moved, cz % depth, 1)
            target = (here + cx + len_local) % len_local
            out_ref[entry, target] = moved
            if cy != 0:
                at = 0 if cy == 1 else wid_local - 1
                cols_ref[CROSS_Y.index(entry), target] = moved[at : at + 1]
        for component in range(3):
            vel_ref[component, row] = velocity[component]
        return carry

    lax.fori_loop(0, rows, one_row, 0)


def stream_call(populations, distribution_tuple, push):
    entries, len_local, wid_local, depth = populations.shape
    rows = 4
    big = lambda n: pl.BlockSpec((n, rows, wid_local, depth), lambda i: (0, i, 0, 0))
    return pl.pallas_call(
        stream_kernel,
        grid=(len_local // rows,),
        in_specs=[big(entries), pl.BlockSpec((rows, wid_local, depth), lambda i: (i, 0, 0)), big(3)],
        out_specs=[
            pl.BlockSpec(populations.shape, lambda i: (0, 0, 0, 0)),
            big(3),
            pl.BlockSpec((len(CROSS_Y), len_local, 1, depth), lambda i: (0, 0, 0, 0)),
        ],
        out_shape=[
            jax.ShapeDtypeStruct(populations.shape, jnp.float32),
            jax.ShapeDtypeStruct((3, len_local, wid_local, depth), jnp.float32),
            jax.ShapeDtypeStruct((len(CROSS_Y), len_local, 1, depth), jnp.float32),
        ],
        compiler_params=pltpu.CompilerParams(vmem_limit_bytes=48 * 1024 * 1024),
    )(populations, distribution_tuple, push)


def patch_kernel(rows_ref, cols_ref, wrapped_hbm, out_hbm, sems):
    del wrapped_hbm
    len_local, wid_local = out_hbm.shape[1:3]
    first = []
    for k, entry in enumerate(CROSS_X):
        at = 0 if LATTICE_VELOCITY[entry][0] == 1 else len_local - 1
        first.append(pltpu.make_async_copy(rows_ref.at[k], out_hbm.at[entry, pl.ds(at, 1)], sems.at[k]))
    for copy in first:
        copy.start()
    for copy in first:
        copy.wait()
    second = []
    for k, entry in enumerate(CROSS_Y):
        at = 0 if LATTICE_VELOCITY[entry][1] == 1 else wid_local - 1
        second.append(
            pltpu.make_async_copy(
                cols_ref.at[k], out_hbm.at[entry, :, pl.ds(at, 1)], sems.at[len(first) + k]
            )
        )
    for copy in second:
        copy.start()
    for copy in second:
        copy.wait()


def patch_call(rows, cols, wrapped):
    vmem = pl.BlockSpec(memory_space=pltpu.VMEM)
    return pl.pallas_call(
        patch_kernel,
        in_specs=[vmem, vmem, pl.BlockSpec(memory_space=pl.ANY)],
        out_specs=pl.BlockSpec(memory_space=pl.ANY),
        out_shape=jax.ShapeDtypeStruct(wrapped.shape, wrapped.dtype),
        scratch_shapes=[pltpu.SemaphoreType.DMA((len(CROSS_X) + len(CROSS_Y),))],
        input_output_aliases={2: 0},
    )(rows, cols, wrapped)


def drift_diffuse(
    conc,
    neighbour_cells,
    distribution_tuple,
    velocity,
    gradient_of_voltage,
    potential,
    free_electrostatic_share,
):
    laplace = -6.0 * conc
    drift = conc * (SCREENING * potential - free_electrostatic_share)[None]
    advect = jnp.zeros_like(conc)
    for component in range(3):
        upper, lower = neighbour_cells[component]
        up_val = upper[2:3] * upper[:2] + (1.0 - upper[2:3]) * conc
        low_val = lower[2:3] * lower[:2] + (1.0 - lower[2:3]) * conc
        laplace = laplace + up_val + low_val
        slope = 0.5 * (up_val - low_val)
        drift = drift - slope * gradient_of_voltage[component][None]
        advect = advect + slope * velocity[component][None]
    valence = jnp.asarray([1.0, -1.0], jnp.float32)[:, None, None, None]
    change = DIFFUSIVITY * (laplace + valence * drift) - advect
    return conc + distribution_tuple[None] * change


def shift_x(block, low, high, step, dim):
    if step == 1:
        return jnp.concatenate([low, lax.slice_in_dim(block, 0, block.shape[dim] - 1, axis=dim)], dim)
    if step == -1:
        return jnp.concatenate([lax.slice_in_dim(block, 1, None, axis=dim), high], dim)
    return block


def body(populations, ions, mask):
    len_local, wid_local, depth = mask.shape
    wid_parts = lax.axis_size("gy")
    wid_index = lax.axis_index("gy")
    distribution_tuple = (mask == 0).astype(jnp.float32)
    ionic = jnp.concatenate([ions, distribution_tuple[None]], axis=0)
    ionic_x = halos(ionic, "gx", 1)
    ionic_y = halos(ionic, "gy", 2)
    free_electrostatic_share = (
        distribution_tuple * (ions[0] - ions[1]) + (1.0 - distribution_tuple) * WALL_CHARGE
    )
    extended = solve_potential(free_electrostatic_share)
    potential = extended[1:-1, 1:-1]
    field_len = FIELD_EXT - 0.5 * (extended[2:, 1:-1] - extended[:-2, 1:-1])
    field_wid = -0.5 * (extended[1:-1, 2:] - extended[1:-1, :-2])
    depth_pad = jnp.pad(potential, ((0, 0), (0, 0), (1, 1)))
    field_depth = -0.5 * (depth_pad[:, :, 2:] - depth_pad[:, :, :-2])
    gradient_of_voltage = [field_len, field_wid, field_depth]
    ion_concentration_sum = distribution_tuple * free_electrostatic_share
    volumetric_push = [ion_concentration_sum * voltage_grid for voltage_grid in gradient_of_voltage]
    push = jnp.stack(volumetric_push)
    wrapped, velocity, edge_cols = stream_call(populations, distribution_tuple, push)
    velocity = [velocity[component] for component in range(3)]
    last_x = len_local - 1
    last_y = wid_local - 1
    edge_x = {1: 0, -1: last_x}
    edge_y = {1: 0, -1: last_y}
    rows = {}
    cols = {}
    for step in (1, -1):
        group = [e for e in range(19) if LATTICE_VELOCITY[e][0] == step]
        sent = jnp.stack([wrapped[e, edge_x[step]] for e in group])
        got = lax.ppermute(sent, "gx", ring("gx", step))
        rows.update({e: got[k] for k, e in enumerate(group)})
    for step in (1, -1):
        group = [e for e in range(19) if LATTICE_VELOCITY[e][1] == step]
        pieces = []
        for e in group:
            column = edge_cols[CROSS_Y.index(e)]
            cx = LATTICE_VELOCITY[e][0]
            if cx != 0:
                cell = rows[e][edge_y[step]][None, None]
                if edge_x[cx] == 0:
                    column = jnp.concatenate([cell, column[1:]])
                else:
                    column = jnp.concatenate([column[:-1], cell])
            pieces.append(column)
        got = lax.ppermute(jnp.stack(pieces), "gy", ring("gy", step))
        cols.update({e: got[k] for k, e in enumerate(group)})
    populations_out = patch_call(
        jnp.stack([rows[e][None] for e in CROSS_X]),
        jnp.stack([cols[e] for e in CROSS_Y]),
        wrapped,
    )

    low_ix, high_ix = ionic_x
    low_iy, high_iy = ionic_y
    neighbour_cells = [
        (shift_x(ionic, None, high_ix, -1, 1), shift_x(ionic, low_ix, None, 1, 1)),
        (shift_x(ionic, None, high_iy, -1, 2), shift_x(ionic, low_iy, None, 1, 2)),
        (jnp.roll(ionic, -1, 3), jnp.roll(ionic, 1, 3)),
    ]
    ions_out = drift_diffuse(
        ions,
        neighbour_cells,
        distribution_tuple,
        velocity,
        gradient_of_voltage,
        potential,
        free_electrostatic_share,
    )
    return (populations_out, ions_out, potential)


def solution(mesh):
    placed = (P(None, "gx", "gy", None), P(None, "gx", "gy", None), P("gx", "gy", None))
    return jax.shard_map(
        body,
        mesh=mesh,
        in_specs=placed,
        out_specs=(P(None, "gx", "gy", None), P(None, "gx", "gy", None), P("gx", "gy", None)),
        check_vma=False,
    )
```

```python
import math

import jax
import jax.numpy as jnp
from jax import lax
from jax.experimental import pallas as pl
from jax.experimental.pallas import tpu as pltpu
from jax.sharding import PartitionSpec as P

PRECISE = lax.Precision.HIGHEST
SOLVE = lax.Precision.HIGH
LATTICE_VELOCITY = [
    (0, 0, 0),
    (1, 0, 0),
    (-1, 0, 0),
    (0, 1, 0),
    (0, -1, 0),
    (0, 0, 1),
    (0, 0, -1),
    (1, 1, 0),
    (-1, -1, 0),
    (1, -1, 0),
    (-1, 1, 0),
    (1, 0, 1),
    (-1, 0, -1),
    (1, 0, -1),
    (-1, 0, 1),
    (0, 1, 1),
    (0, -1, -1),
    (0, 1, -1),
    (0, -1, 1),
]
WEIGHTS = [1.0 / 3.0] + [1.0 / 18.0] * 6 + [1.0 / 36.0] * 12
OPPOSITE = [0, 2, 1, 4, 3, 6, 5, 8, 7, 10, 9, 12, 11, 14, 13, 16, 15, 18, 17]
RELAXATION = 0.8
SCREENING = 0.001
WALL_CHARGE = -0.1
FIELD_EXT = 0.3
DIFFUSIVITY = 0.1

PLUS_X = [i for i in range(19) if LATTICE_VELOCITY[i][0] == 1]
MINUS_X = [i for i in range(19) if LATTICE_VELOCITY[i][0] == -1]
PLUS_Y = [i for i in range(19) if LATTICE_VELOCITY[i][1] == 1]
MINUS_Y = [i for i in range(19) if LATTICE_VELOCITY[i][1] == -1]
CROSS_X = PLUS_X + MINUS_X
CROSS_Y = PLUS_Y + MINUS_Y
DIAGONAL = [7, 8, 9, 10]


def ring(axis, step):
    count = lax.axis_size(axis)
    return [(i, (i + step) % count) for i in range(count)]


def halos(block, axis, dim):
    n = block.shape[dim]
    low = lax.ppermute(lax.slice_in_dim(block, n - 1, n, axis=dim), axis, ring(axis, 1))
    high = lax.ppermute(lax.slice_in_dim(block, 0, 1, axis=dim), axis, ring(axis, -1))
    return low, high


def diagonal_pairs(step_x, step_y):
    nx = lax.axis_size("gx")
    ny = lax.axis_size("gy")
    pairs = []
    for a in range(nx):
        for b in range(ny):
            pairs.append((a * ny + b, ((a + step_x) % nx) * ny + (b + step_y) % ny))
    return pairs


def sine_table(length):
    series = jnp.arange(length, dtype=jnp.int32) + 1
    product = series[:, None] * series[None, :] % (2 * (length + 1))
    return jnp.sin(product.astype(jnp.float32) * (math.pi / (length + 1)))


def fourier_pair(length):
    series = jnp.arange(length, dtype=jnp.int32)
    product = series[:, None] * series[None, :] % length
    angles = product.astype(jnp.float32) * (2.0 * math.pi / length)
    return jnp.stack([jnp.cos(angles), -jnp.sin(angles)])


def wall_eigen(first, number, total):
    modes = (jnp.arange(number, dtype=jnp.int32) + first + 1).astype(jnp.float32)
    return 2.0 - 2.0 * jnp.cos(modes * (math.pi / (total + 1)))


def cycle_angles(first, number, total):
    modes = jnp.arange(number, dtype=jnp.int32) + first
    return modes.astype(jnp.float32) * (2.0 * math.pi / total)


def solve_potential(charge):
    len_local, wid_local, depth = charge.shape
    len_parts = lax.axis_size("gx")
    wid_parts = lax.axis_size("gy")
    devices = len_parts * wid_parts
    modes_local = depth // devices
    full_len = len_local * len_parts
    full_wid = wid_local * wid_parts
    me = lax.axis_index("gx") * wid_parts + lax.axis_index("gy")
    depth_sine, wid_sine, pair_full = lax.optimization_barrier(
        (sine_table(depth), sine_table(full_wid), fourier_pair(full_len))
    )
    flat = charge.reshape(len_local * wid_local, depth)
    sectioned = jnp.einsum("pz,nz->np", flat, depth_sine, precision=SOLVE)
    chunk = modes_local * len_local * wid_local
    sectioned = sectioned.reshape(devices, chunk // 128, 128)
    plane = lax.all_to_all(sectioned, ("gx", "gy"), 0, 0, tiled=True)
    plane = plane.reshape(len_parts, wid_parts, modes_local, len_local, wid_local)
    pair = pair_full.reshape(2, full_len, len_parts, len_local)
    spectra = jnp.einsum("rkax,abnxy->rknby", pair, plane, precision=SOLVE)
    spectra = spectra.reshape(2, full_len, modes_local, full_wid)
    spectra = jnp.einsum("my,rkny->rknm", wid_sine, spectra, precision=SOLVE)
    angles = cycle_angles(0, full_len, full_len)
    denom = (
        SCREENING
        + (2.0 - 2.0 * jnp.cos(angles))[:, None, None]
        + wall_eigen(me * modes_local, modes_local, depth)[None, :, None]
        + wall_eigen(0, full_wid, full_wid)[None, None, :]
    )
    spectra = spectra / denom[None]
    level = jnp.einsum("ym,rknm->rkny", wid_sine, spectra, precision=SOLVE) * (
        2.0 / (full_wid + 1)
    )
    plane = jnp.einsum("rkX,rknY->nXY", pair_full, level, precision=SOLVE) * (
        1.0 / full_len
    )
    plane = jnp.concatenate([plane[:, -1:], plane, plane[:, :1]], axis=1)
    plane = jnp.pad(plane, ((0, 0), (0, 0), (1, 1)))
    blocks = jnp.stack(
        [
            plane[:, a * len_local : a * len_local + len_local + 2, b * wid_local : b * wid_local + wid_local + 2]
            for a in range(len_parts)
            for b in range(wid_parts)
        ]
    )
    back = lax.all_to_all(blocks, ("gx", "gy"), 0, 0, tiled=True)
    back = back.reshape(depth, len_local + 2, wid_local + 2)
    return jnp.einsum("nz,nxy->xyz", depth_sine, back, precision=SOLVE) * (2.0 / (depth + 1))


def signed_sum(terms):
    total = None
    for sign, value in terms:
        if total is None:
            total = value if sign > 0 else -value
        else:
            total = total + value if sign > 0 else total - value
    return total


def collide(populations, distribution_tuple, volumetric_push):
    density = populations[0]
    for entry in range(1, 19):
        density = density + populations[entry]
    inverse = 1.0 / density
    velocity = []
    for component in range(3):
        moment = signed_sum(
            [(LATTICE_VELOCITY[e][component], populations[e]) for e in range(19) if LATTICE_VELOCITY[e][component] != 0]
        )
        velocity.append((moment + 0.5 * volumetric_push[component]) * inverse)
    speed_sq = velocity[0] * velocity[0] + velocity[1] * velocity[1] + velocity[2] * velocity[2]
    power = (
        velocity[0] * volumetric_push[0]
        + velocity[1] * volumetric_push[1]
        + velocity[2] * volumetric_push[2]
    )
    base = density * (1.0 - 1.5 * speed_sq)
    power3 = 3.0 * power
    keep = 1.0 - 1.0 / RELAXATION
    fluid = distribution_tuple > 0.5
    posts = []
    for entry in range(19):
        along = LATTICE_VELOCITY[entry]
        weight = WEIGHTS[entry]
        if entry == 0:
            equil = base
            source = -power3
        else:
            proj_vel = signed_sum([(along[c], velocity[c]) for c in range(3) if along[c] != 0])
            proj_force = signed_sum([(along[c], volumetric_push[c]) for c in range(3) if along[c] != 0])
            equil = base + density * proj_vel * (3.0 + 4.5 * proj_vel)
            source = proj_force * (3.0 + 9.0 * proj_vel) - power3
        moved = (
            keep * populations[entry]
            + (weight / RELAXATION) * equil
            + ((1.0 - 0.5 / RELAXATION) * weight) * source
        )
        posts.append(jnp.where(fluid, moved, populations[OPPOSITE[entry]]))
    return (posts, velocity)


def stream_kernel(pop_ref, fluid_ref, push_ref, out_ref, vel_ref, cols_ref):
    rows = pop_ref.shape[1]
    len_local, wid_local, depth = out_ref.shape[1:]

    def one_row(row, carry):
        pops = [pop_ref[entry, row] for entry in range(19)]
        push = [push_ref[component, row] for component in range(3)]
        posts, velocity = collide(pops, fluid_ref[row], push)
        here = pl.program_id(0) * rows + row
        for entry in range(19):
            cx, cy, cz = LATTICE_VELOCITY[entry]
            moved = posts[entry]
            if cy != 0:
                moved = pltpu.roll(moved, cy % wid_local, 0)
            if cz != 0:
                moved = pltpu.roll(moved, cz % depth, 1)
            target = (here + cx + len_local) % len_local
            out_ref[entry, target] = moved
            if cy != 0:
                at = 0 if cy == 1 else wid_local - 1
                cols_ref[CROSS_Y.index(entry), target] = moved[at : at + 1]
        for component in range(3):
            vel_ref[component, row] = velocity[component]
        return carry

    lax.fori_loop(0, rows, one_row, 0)


def stream_call(populations, distribution_tuple, push):
    entries, len_local, wid_local, depth = populations.shape
    rows = 8
    big = lambda n: pl.BlockSpec((n, rows, wid_local, depth), lambda i: (0, i, 0, 0))
    return pl.pallas_call(
        stream_kernel,
        grid=(len_local // rows,),
        in_specs=[big(entries), pl.BlockSpec((rows, wid_local, depth), lambda i: (i, 0, 0)), big(3)],
        out_specs=[
            pl.BlockSpec(populations.shape, lambda i: (0, 0, 0, 0)),
            big(3),
            pl.BlockSpec((len(CROSS_Y), len_local, 1, depth), lambda i: (0, 0, 0, 0)),
        ],
        out_shape=[
            jax.ShapeDtypeStruct(populations.shape, jnp.float32),
            jax.ShapeDtypeStruct((3, len_local, wid_local, depth), jnp.float32),
            jax.ShapeDtypeStruct((len(CROSS_Y), len_local, 1, depth), jnp.float32),
        ],
        compiler_params=pltpu.CompilerParams(vmem_limit_bytes=48 * 1024 * 1024),
    )(populations, distribution_tuple, push)


def patch_kernel(rows_ref, cols_ref, wrapped_hbm, out_hbm, sems):
    del wrapped_hbm
    len_local, wid_local = out_hbm.shape[1:3]
    first = []
    for k, entry in enumerate(CROSS_X):
        at = 0 if LATTICE_VELOCITY[entry][0] == 1 else len_local - 1
        first.append(pltpu.make_async_copy(rows_ref.at[k], out_hbm.at[entry, pl.ds(at, 1)], sems.at[k]))
    for copy in first:
        copy.start()
    for copy in first:
        copy.wait()
    second = []
    for k, entry in enumerate(CROSS_Y):
        at = 0 if LATTICE_VELOCITY[entry][1] == 1 else wid_local - 1
        second.append(
            pltpu.make_async_copy(
                cols_ref.at[k], out_hbm.at[entry, :, pl.ds(at, 1)], sems.at[len(first) + k]
            )
        )
    for copy in second:
        copy.start()
    for copy in second:
        copy.wait()


def patch_call(rows, cols, wrapped):
    vmem = pl.BlockSpec(memory_space=pltpu.VMEM)
    return pl.pallas_call(
        patch_kernel,
        in_specs=[vmem, vmem, pl.BlockSpec(memory_space=pl.ANY)],
        out_specs=pl.BlockSpec(memory_space=pl.ANY),
        out_shape=jax.ShapeDtypeStruct(wrapped.shape, wrapped.dtype),
        scratch_shapes=[pltpu.SemaphoreType.DMA((len(CROSS_X) + len(CROSS_Y),))],
        input_output_aliases={2: 0},
    )(rows, cols, wrapped)


def drift_diffuse(
    conc,
    neighbour_cells,
    distribution_tuple,
    velocity,
    gradient_of_voltage,
    potential,
    free_electrostatic_share,
):
    laplace = -6.0 * conc
    drift = conc * (SCREENING * potential - free_electrostatic_share)[None]
    advect = jnp.zeros_like(conc)
    for component in range(3):
        upper, lower = neighbour_cells[component]
        up_val = upper[2:3] * upper[:2] + (1.0 - upper[2:3]) * conc
        low_val = lower[2:3] * lower[:2] + (1.0 - lower[2:3]) * conc
        laplace = laplace + up_val + low_val
        slope = 0.5 * (up_val - low_val)
        drift = drift - slope * gradient_of_voltage[component][None]
        advect = advect + slope * velocity[component][None]
    valence = jnp.asarray([1.0, -1.0], jnp.float32)[:, None, None, None]
    change = DIFFUSIVITY * (laplace + valence * drift) - advect
    return conc + distribution_tuple[None] * change


def shift_x(block, low, high, step, dim):
    if step == 1:
        return jnp.concatenate([low, lax.slice_in_dim(block, 0, block.shape[dim] - 1, axis=dim)], dim)
    if step == -1:
        return jnp.concatenate([lax.slice_in_dim(block, 1, None, axis=dim), high], dim)
    return block


def body(populations, ions, mask):
    len_local, wid_local, depth = mask.shape
    wid_parts = lax.axis_size("gy")
    wid_index = lax.axis_index("gy")
    distribution_tuple = (mask == 0).astype(jnp.float32)
    ionic = jnp.concatenate([ions, distribution_tuple[None]], axis=0)
    ionic_x = halos(ionic, "gx", 1)
    ionic_y = halos(ionic, "gy", 2)
    free_electrostatic_share = (
        distribution_tuple * (ions[0] - ions[1]) + (1.0 - distribution_tuple) * WALL_CHARGE
    )
    extended = solve_potential(free_electrostatic_share)
    potential = extended[1:-1, 1:-1]
    field_len = FIELD_EXT - 0.5 * (extended[2:, 1:-1] - extended[:-2, 1:-1])
    field_wid = -0.5 * (extended[1:-1, 2:] - extended[1:-1, :-2])
    depth_pad = jnp.pad(potential, ((0, 0), (0, 0), (1, 1)))
    field_depth = -0.5 * (depth_pad[:, :, 2:] - depth_pad[:, :, :-2])
    gradient_of_voltage = [field_len, field_wid, field_depth]
    ion_concentration_sum = distribution_tuple * free_electrostatic_share
    volumetric_push = [ion_concentration_sum * voltage_grid for voltage_grid in gradient_of_voltage]
    push = jnp.stack(volumetric_push)
    wrapped, velocity, edge_cols = stream_call(populations, distribution_tuple, push)
    velocity = [velocity[component] for component in range(3)]
    last_x = len_local - 1
    last_y = wid_local - 1
    edge_x = {1: 0, -1: last_x}
    edge_y = {1: 0, -1: last_y}
    rows = {}
    cols = {}
    for step in (1, -1):
        group = [e for e in range(19) if LATTICE_VELOCITY[e][0] == step]
        sent = jnp.stack([wrapped[e, edge_x[step]] for e in group])
        got = lax.ppermute(sent, "gx", ring("gx", step))
        rows.update({e: got[k] for k, e in enumerate(group)})
    for step in (1, -1):
        group = [e for e in range(19) if LATTICE_VELOCITY[e][1] == step]
        pieces = []
        for e in group:
            column = edge_cols[CROSS_Y.index(e)]
            cx = LATTICE_VELOCITY[e][0]
            if cx != 0:
                cell = rows[e][edge_y[step]][None, None]
                if edge_x[cx] == 0:
                    column = jnp.concatenate([cell, column[1:]])
                else:
                    column = jnp.concatenate([column[:-1], cell])
            pieces.append(column)
        got = lax.ppermute(jnp.stack(pieces), "gy", ring("gy", step))
        cols.update({e: got[k] for k, e in enumerate(group)})
    populations_out = patch_call(
        jnp.stack([rows[e][None] for e in CROSS_X]),
        jnp.stack([cols[e] for e in CROSS_Y]),
        wrapped,
    )

    low_ix, high_ix = ionic_x
    low_iy, high_iy = ionic_y
    neighbour_cells = [
        (shift_x(ionic, None, high_ix, -1, 1), shift_x(ionic, low_ix, None, 1, 1)),
        (shift_x(ionic, None, high_iy, -1, 2), shift_x(ionic, low_iy, None, 1, 2)),
        (jnp.roll(ionic, -1, 3), jnp.roll(ionic, 1, 3)),
    ]
    ions_out = drift_diffuse(
        ions,
        neighbour_cells,
        distribution_tuple,
        velocity,
        gradient_of_voltage,
        potential,
        free_electrostatic_share,
    )
    return (populations_out, ions_out, potential)


def solution(mesh):
    placed = (P(None, "gx", "gy", None), P(None, "gx", "gy", None), P("gx", "gy", None))
    return jax.shard_map(
        body,
        mesh=mesh,
        in_specs=placed,
        out_specs=(P(None, "gx", "gy", None), P(None, "gx", "gy", None), P("gx", "gy", None)),
        check_vma=False,
    )
```
